32 devices in a mesh: groups: 2 (over y), seq: 8 (over z, x), wg: 2 (over core).
Axes of the slice: x: 2, y: 2, z: 4, core: 2. Of those that a mesh axis runs over, the one named last changes fastest.
Arguments:
- generator_rows: bfloat16 [2048, 2304], P(('groups', 'seq'), 'wg'), parts along dimension 0, may hold values from -120 to 120, as said below
- pre_gain: float32 [2304], replicated, may hold values from 0.1 to 1.9
- query_weight: bfloat16 [2304, 2048], P('seq', 'wg'), may hold values from -2 to 2, as said below
- key_weight: bfloat16 [2304, 1024], P('seq', 'wg'), may hold values from -2 to 2, as said below
- value_weight: bfloat16 [2304, 1024], P('seq', 'wg'), may hold values from -0.125 to 0.125
- out_weight: bfloat16 [2048, 2304], P('wg', 'seq'), may hold values from -0.125 to 0.125
- post_gain: float32 [2304], replicated, may hold values from 0.1 to 1.9
- final_gain: float32 [2304], replicated, may hold values from 0.1 to 1.9
- label_table: bfloat16 [64, 2304], replicated, may hold values from -0.375 to 0.375
- lengths: int32 [16], P('groups'), parts along dimension 0, may hold values from 65 to 127
- label_index: int32 [16], P('groups'), parts along dimension 0, may hold values from 0 to 63
Outputs:
- input_grad: bfloat16 [2048, 2304], P(('groups', 'seq'), 'wg'), parts along dimension 0
The draws below stay inside these ranges and needn't reach their ends.
There are 2 independent parts, one for each index of `groups`. The reference program is written for one: setup_inputs(seed, part) draws one part's arguments, and reference() takes and returns one part's arrays. A program takes and returns all parts, laid end to end along the dimension named above; an argument that names none is the same for every part. Nothing has to cross between parts.
Inputs may be any that keep to these rules, and one draw needn't show every extreme that they name: `generator_rows`: finite real entries. `query_weight`: finite real entries. `key_weight`: finite real entries.
All inputs are finite; a program needn't handle non-finite values.
Results may differ from the reference program's by a relative error of at most 0.017.
The reference program's roundings to bfloat16 on the way count: a program that leaves them out, or rounds other values in their place, can miss the bound.
Values may be sent and summed in bfloat16 or wider, within the bound.
No kernel may reach another device: no remote copies, remote signals or barrier semaphores. Data moves between devices by JAX's collectives and lax.ppermute only.
A program may use at most 128 MiB of HBM per device.

```python
import math
import jax
import jax.numpy as jnp
from jax import lax

D = 2304
HQ = 16
HK = 8
HD = 128
LABELS = 64
TOK_DEV = 128
BLOCKS = 8
PIECE = 16
TOKENS = 1024
LEN = 128
TRANS = 8
N_WG = 2


def draw_generator_rows(key, part):
    row_key, column_key, value_key = jax.random.split(key, 3)
    row_scale = jnp.exp(jax.random.uniform(row_key, (TOKENS, 1), jnp.float32, 0.0, math.log(10.0)))
    column_scale = jnp.exp(jax.random.uniform(column_key, (1, D), jnp.float32, math.log(0.3), math.log(3.0)))
    values = jax.random.truncated_normal(value_key, -4.0, 4.0, (TOKENS, D), jnp.float32)
    return (values * row_scale * column_scale).astype(jnp.bfloat16)


def head_levels(key):
    order = jax.random.permutation(jax.random.fold_in(key, 7), HK)
    return order.astype(jnp.float32) / max(HK - 1, 1)


def draw_query_weight(key, part):
    levels = jnp.repeat(head_levels(key), HQ // HK)
    column_scale = jnp.repeat(jnp.exp(levels * math.log(8.0)), HD)
    noise_key = jax.random.fold_in(key, 11)
    base_values = jax.random.truncated_normal(noise_key, -4.0, 4.0, (D, HQ * HD), jnp.float32)
    return (base_values * (1.0 / math.sqrt(D)) * column_scale[None, :]).astype(jnp.bfloat16)


def draw_key_weight(key, part):
    levels = head_levels(key)
    column_scale = jnp.repeat(jnp.exp(levels * math.log(6.0)), HD)
    noise_key = jax.random.fold_in(key, 13)
    base_values = jax.random.truncated_normal(noise_key, -4.0, 4.0, (D, HK * HD), jnp.float32)
    return (base_values * (1.0 / math.sqrt(D)) * column_scale[None, :]).astype(jnp.bfloat16)


def with_ends(result, stream_key, smallest, high):
    dims = result.shape
    place = [jax.random.randint(jax.random.fold_in(stream_key, axis), (), 0, dims[axis]) for axis in range(len(dims))]
    result = result.at[tuple(place)].set(smallest)
    longest = dims.index(max(dims))
    place[longest] = (place[longest] + 1) % dims[longest]
    return result.at[tuple(place)].set(high)


def block_scale(stream_key, dims, shards, least, high):
    gain = 1.0
    for axis_at, shards_of in shards:
        draws = jax.random.uniform(jax.random.fold_in(jax.random.fold_in(stream_key, 6), axis_at), (shards_of,), jnp.float32, least / len(shards), high / len(shards))
        gain = gain * jnp.repeat(jnp.exp(draws), dims[axis_at] // shards_of).reshape((-1,) + (1,) * (len(dims) - 1 - axis_at))
    return gain


def gaussian(own_key, extent, spread, limit, pieces=(), kind=jnp.bfloat16):
    level = block_scale(own_key, extent, pieces, -0.22, 0.18) if pieces else 1.0
    result = jax.random.normal(own_key, extent, jnp.float32) * spread * level
    return jnp.minimum(jnp.maximum(result, -limit), limit).astype(kind)


def setup_inputs(seed: int = 0, part: int = 0) -> dict:
    key_of = jax.random.split(jax.random.key(seed), 12)
    part_splits = jax.random.split(jax.random.fold_in(key_of[11], part), 12)
    generator_rows = draw_generator_rows(jax.random.fold_in(jax.random.fold_in(key_of[11], part), 71), part)
    pre_gain = jnp.clip(1.0 + 0.18 * jax.random.normal(key_of[1], (D,), jnp.float32), 0.1, 1.9)
    query_weight = draw_query_weight(jax.random.fold_in(key_of[11], 71), part)
    key_weight = draw_key_weight(jax.random.fold_in(key_of[11], 71), part)
    value_weight = gaussian(key_of[4], (D, HK * HD), D ** -0.5, 0.125, ((0, 8), (1, 2)))
    out_weight = gaussian(key_of[5], (HQ * HD, D), (HQ * HD) ** -0.5, 0.125, ((0, 2), (1, 8)))
    post_gain = jnp.clip(1.0 + 0.18 * jax.random.normal(key_of[6], (D,), jnp.float32), 0.1, 1.9)
    final_gain = jnp.clip(1.0 + 0.18 * jax.random.normal(key_of[7], (D,), jnp.float32), 0.1, 1.9)
    label_table = gaussian(key_of[8], (LABELS, D), (D // 9) ** -0.5, 0.375)
    lengths = with_ends(jax.random.randint(part_splits[9], (TRANS,), TOK_DEV // 2 + 1, TOK_DEV), jax.random.fold_in(part_splits[9], 1), TOK_DEV // 2 + 1, TOK_DEV - 1).astype(jnp.int32)
    label_index = with_ends(jax.random.randint(part_splits[10], (TRANS,), 0, LABELS), jax.random.fold_in(part_splits[10], 1), 0, LABELS - 1).astype(jnp.int32)
    return dict(generator_rows=generator_rows, pre_gain=pre_gain, query_weight=query_weight, key_weight=key_weight, value_weight=value_weight, out_weight=out_weight, post_gain=post_gain, final_gain=final_gain, label_table=label_table, lengths=lengths, label_index=label_index)


EPSILON = 1e-06
ATTEND_CAP = 50.0
LABEL_CAP = 30.0
QUERY_SCALE = 1.0 / 12.0

def rounded(values):
    return lax.optimization_barrier(values.astype(jnp.bfloat16)).astype(jnp.float32)

def rope_tables(positions, head_width):
    frequency = 10000.0 ** (-2.0 * jnp.arange(head_width // 2, dtype=jnp.float32) / head_width)
    angles = positions.astype(jnp.float32)[:, None] * frequency[None, :]
    return (jnp.cos(angles), jnp.sin(angles))

def rotate(values, cos_table, sin_table):
    half_width = values.shape[-1] // 2
    lower_part = values[..., :half_width]
    upper_part = values[..., half_width:]
    return jnp.concatenate([lower_part * cos_table - upper_part * sin_table, upper_part * cos_table + lower_part * sin_table], axis=-1)

def rotate_back(values, cos_table, sin_table):
    half_width = values.shape[-1] // 2
    lower_part = values[..., :half_width]
    upper_part = values[..., half_width:]
    return jnp.concatenate([lower_part * cos_table + upper_part * sin_table, upper_part * cos_table - lower_part * sin_table], axis=-1)

def relay_rows(source):
    return source.reshape(BLOCKS, BLOCKS, PIECE, D).transpose(1, 0, 2, 3).reshape(TOKENS, D)

def split_heads_sum(factor_pairs):
    summed = None
    for group_index in range(N_WG):
        partial_value = None
        for left_side, right_side in factor_pairs:
            width_group = left_side.shape[1] // N_WG
            begin = group_index * width_group
            product = jnp.dot(left_side[:, begin:begin + width_group], right_side[begin:begin + width_group], preferred_element_type=jnp.float32)
            partial_value = product if partial_value is None else partial_value + product
        part_round = rounded(partial_value)
        summed = part_round if summed is None else summed + part_round
    return summed

def transcript(block_rows, length, target, pre_gain, query_weight, key_weight, value_weight, out_weight, post_gain, final_gain, label_table):
    inputs = block_rows.astype(jnp.float32)
    scale_in = lax.rsqrt(lax.optimization_barrier(jnp.mean(inputs * inputs, axis=-1, keepdims=True)) + EPSILON)
    normed = (inputs * scale_in * pre_gain.astype(jnp.float32)).astype(jnp.bfloat16)
    offsets = jnp.arange(LEN, dtype=jnp.int32)
    cos_table, sin_table = rope_tables(offsets, HD)
    query_proj = jnp.dot(normed, query_weight, preferred_element_type=jnp.float32).reshape(LEN, HQ, HD).transpose(1, 0, 2)
    queries = (rotate(query_proj, cos_table, sin_table) * QUERY_SCALE).astype(jnp.bfloat16)
    key_proj = jnp.dot(normed, key_weight, preferred_element_type=jnp.float32).reshape(LEN, HK, HD).transpose(1, 0, 2)
    keys = rotate(key_proj, cos_table, sin_table).astype(jnp.bfloat16)
    values = jnp.dot(normed, value_weight, preferred_element_type=jnp.float32).astype(jnp.bfloat16).reshape(LEN, HK, HD).transpose(1, 0, 2)
    group_size = HQ // HK
    query_four = queries.reshape(HK, group_size, LEN, HD).astype(jnp.float32)
    keys_float = keys.astype(jnp.float32)
    values_float = values.astype(jnp.float32)
    raw_scores = jnp.einsum('kgid,kjd->kgij', query_four, keys_float)
    capped = jnp.tanh(raw_scores / ATTEND_CAP)
    allowed = (offsets[None, :] <= offsets[:, None]) & (offsets[None, :] < length)
    weight_exp = jnp.where(allowed[None, None], jnp.exp(ATTEND_CAP * capped), 0.0)
    soft_weights = weight_exp / lax.optimization_barrier(jnp.sum(weight_exp, axis=-1, keepdims=True))
    attend = rounded(soft_weights)
    context = jnp.einsum('kgij,kjd->kgid', attend, values_float).astype(jnp.bfloat16)
    context_rows = context.reshape(HQ, LEN, HD).transpose(1, 0, 2).reshape(LEN, HQ * HD)
    attention = split_heads_sum([(context_rows, out_weight)])
    scale_attn = lax.rsqrt(lax.optimization_barrier(jnp.mean(attention * attention, axis=-1, keepdims=True)) + EPSILON)
    post_float = post_gain.astype(jnp.float32)
    mixed_rows = inputs + attention * scale_attn * post_float
    scale_out = lax.rsqrt(lax.optimization_barrier(jnp.mean(mixed_rows * mixed_rows, axis=-1, keepdims=True)) + EPSILON)
    final_float = final_gain.astype(jnp.float32)
    final_rows = (mixed_rows * scale_out * final_float).astype(jnp.bfloat16)
    logits = jnp.dot(final_rows, label_table.T, preferred_element_type=jnp.float32)
    label_cap = jnp.tanh(logits / LABEL_CAP)
    label_exp = jnp.exp(LABEL_CAP * label_cap)
    chance = label_exp / lax.optimization_barrier(jnp.sum(label_exp, axis=-1, keepdims=True))
    live_rows = (offsets < length)[:, None]
    onehot = (jnp.arange(LABELS, dtype=jnp.int32) == target).astype(jnp.float32)[None, :]
    grad_logit = (jnp.where(live_rows, chance - onehot, 0.0) * (1.0 - label_cap * label_cap)).astype(jnp.bfloat16)
    grad_final = jnp.dot(grad_logit, label_table, preferred_element_type=jnp.float32)
    scaled_final = grad_final * final_float
    cube_out = scale_out * scale_out * scale_out
    grad_mixed = scale_out * scaled_final - mixed_rows * cube_out * lax.optimization_barrier(jnp.mean(scaled_final * mixed_rows, axis=-1, keepdims=True))
    scaled_post = grad_mixed * post_float
    cube_attn = scale_attn * scale_attn * scale_attn
    grad_attention = scale_attn * scaled_post - attention * cube_attn * lax.optimization_barrier(jnp.mean(scaled_post * attention, axis=-1, keepdims=True))
    grad_context = jnp.dot(grad_attention.astype(jnp.bfloat16), out_weight.T, preferred_element_type=jnp.float32).astype(jnp.bfloat16)
    grad_four = grad_context.reshape(LEN, HK, group_size, HD).transpose(1, 2, 0, 3).astype(jnp.float32)
    grad_prob = jnp.einsum('kgid,kjd->kgij', grad_four, values_float)
    grad_score = soft_weights * (grad_prob - lax.optimization_barrier(jnp.sum(soft_weights * grad_prob, axis=-1, keepdims=True))) * (1.0 - capped * capped)
    score_round = rounded(grad_score)
    grad_query = jnp.einsum('kgij,kjd->kgid', score_round, keys_float).reshape(HQ, LEN, HD)
    grad_queries = rotate_back(grad_query * QUERY_SCALE, cos_table, sin_table).astype(jnp.bfloat16)
    grad_key = jnp.einsum('kgij,kgid->kjd', score_round, query_four)
    grad_value = jnp.einsum('kgij,kgid->kjd', attend, grad_four)
    grad_keys = rotate_back(grad_key, cos_table, sin_table).astype(jnp.bfloat16)
    grad_values = grad_value.astype(jnp.bfloat16)
    query_rows = grad_queries.transpose(1, 0, 2).reshape(LEN, HQ * HD)
    key_rows = grad_keys.transpose(1, 0, 2).reshape(LEN, HK * HD)
    value_rows = grad_values.transpose(1, 0, 2).reshape(LEN, HK * HD)
    grad_normed = split_heads_sum([(query_rows, query_weight.T), (key_rows, key_weight.T), (value_rows, value_weight.T)])
    scaled_in = grad_normed * pre_gain.astype(jnp.float32)
    cube_in = scale_in * scale_in * scale_in
    grad_hidden = scale_in * scaled_in - inputs * cube_in * lax.optimization_barrier(jnp.mean(scaled_in * inputs, axis=-1, keepdims=True)) + grad_mixed
    return grad_hidden.astype(jnp.bfloat16)

def reference(generator_rows, pre_gain, query_weight, key_weight, value_weight, out_weight, post_gain, final_gain, label_table, lengths, label_index):
    guard_rows = relay_rows(generator_rows).reshape(TRANS, LEN, D)

    def per_transcript(carry_in):
        block_rows, length, target = carry_in
        return transcript(block_rows, length, target, pre_gain, query_weight, key_weight, value_weight, out_weight, post_gain, final_gain, label_table)
    grad_blocks = lax.map(per_transcript, (guard_rows, lengths, label_index))
    return relay_rows(grad_blocks.reshape(TOKENS, D))
```

```python
import jax
import jax.numpy as jnp
from jax import lax
from jax.sharding import PartitionSpec as P

HD = 128
LABELS = 64


EPSILON = 1e-06
ATTEND_CAP = 50.0
LABEL_CAP = 30.0
QUERY_SCALE = 1.0 / 12.0


def rope_tables(positions, head_width):
    frequency = 10000.0 ** (-2.0 * jnp.arange(head_width // 2, dtype=jnp.float32) / head_width)
    angles = positions.astype(jnp.float32)[:, None] * frequency[None, :]
    return (jnp.cos(angles), jnp.sin(angles))


def rotate(values, cos_table, sin_table):
    half_width = values.shape[-1] // 2
    lower_part = values[..., :half_width]
    upper_part = values[..., half_width:]
    return jnp.concatenate(
        [
            lower_part * cos_table - upper_part * sin_table,
            upper_part * cos_table + lower_part * sin_table,
        ],
        axis=-1,
    )


def rotate_back(values, cos_table, sin_table):
    half_width = values.shape[-1] // 2
    lower_part = values[..., :half_width]
    upper_part = values[..., half_width:]
    return jnp.concatenate(
        [
            lower_part * cos_table + upper_part * sin_table,
            upper_part * cos_table - lower_part * sin_table,
        ],
        axis=-1,
    )


def times_transposed(left_side, right_side):
    return lax.dot_general(
        left_side, right_side, (((1,), (1,)), ((), ())), preferred_element_type=jnp.float32
    )


def pair_sum(rounded_part):
    other = lax.ppermute(rounded_part, "wg", perm=[(0, 1), (1, 0)])
    return rounded_part.astype(jnp.float32) + other.astype(jnp.float32)


def shards(
    generator_rows,
    pre_gain,
    query_weight,
    key_weight,
    value_weight,
    out_weight,
    post_gain,
    final_gain,
    label_table,
    lengths,
    label_index,
):
    seq_rank = lax.axis_index("seq")
    core_rank = lax.axis_index("wg")
    whole_rows = lax.all_gather(generator_rows, "wg", axis=1, tiled=True)
    guard_rows = lax.all_to_all(whole_rows, "seq", split_axis=0, concat_axis=0, tiled=True)
    q_cols = query_weight.shape[1]
    k_cols = key_weight.shape[1]
    packed = jnp.concatenate([query_weight, key_weight, value_weight, out_weight.T], axis=1)
    gathered = lax.all_gather(packed, "seq", axis=0, tiled=True)
    w_query = gathered[:, :q_cols]
    w_key = gathered[:, q_cols:q_cols + k_cols]
    w_value = gathered[:, q_cols + k_cols:q_cols + 2 * k_cols]
    w_out_t = gathered[:, q_cols + 2 * k_cols:]
    tok_rows = guard_rows.shape[0]
    half_width = generator_rows.shape[1]
    local_heads = w_query.shape[1] // HD
    local_kv = w_key.shape[1] // HD
    group_size = local_heads // local_kv
    length = lax.dynamic_index_in_dim(lengths, seq_rank, 0, keepdims=False)
    target = lax.dynamic_index_in_dim(label_index, seq_rank, 0, keepdims=False)
    offsets = jnp.arange(tok_rows, dtype=jnp.int32)
    cos_table, sin_table = rope_tables(offsets, HD)
    inputs = guard_rows.astype(jnp.float32)
    scale_in = lax.rsqrt(jnp.mean(inputs * inputs, axis=-1, keepdims=True) + EPSILON)
    normed = (inputs * scale_in * pre_gain).astype(jnp.bfloat16)
    query_proj = (
        jnp.dot(normed, w_query, preferred_element_type=jnp.float32)
        .reshape(tok_rows, local_heads, HD)
        .transpose(1, 0, 2)
    )
    queries = (rotate(query_proj, cos_table, sin_table) * QUERY_SCALE).astype(jnp.bfloat16)
    key_proj = (
        jnp.dot(normed, w_key, preferred_element_type=jnp.float32)
        .reshape(tok_rows, local_kv, HD)
        .transpose(1, 0, 2)
    )
    keys_own = rotate(key_proj, cos_table, sin_table).astype(jnp.bfloat16)
    values_own = (
        jnp.dot(normed, w_value, preferred_element_type=jnp.float32)
        .astype(jnp.bfloat16)
        .reshape(tok_rows, local_kv, HD)
        .transpose(1, 0, 2)
    )
    allowed = (offsets[None, :] <= offsets[:, None]) & (offsets[None, :] < length)
    query_four = queries.reshape(local_kv, group_size, tok_rows, HD)
    raw_scores = jnp.einsum(
        "kgid,kjd->kgij", query_four, keys_own, preferred_element_type=jnp.float32
    )
    capped = jnp.tanh(raw_scores / ATTEND_CAP)
    weight_exp = jnp.where(allowed[None, None], jnp.exp(ATTEND_CAP * capped), 0.0)
    soft_weights = weight_exp / jnp.sum(weight_exp, axis=-1, keepdims=True)
    attend = soft_weights.astype(jnp.bfloat16)
    context = jnp.einsum(
        "kgij,kjd->kgid", attend, values_own, preferred_element_type=jnp.float32
    ).astype(jnp.bfloat16)
    context_rows = (
        context.reshape(local_heads, tok_rows, HD)
        .transpose(1, 0, 2)
        .reshape(tok_rows, local_heads * HD)
    )
    out_part = times_transposed(context_rows, w_out_t)
    attention = pair_sum(out_part.astype(jnp.bfloat16))
    scale_attn = lax.rsqrt(jnp.mean(attention * attention, axis=-1, keepdims=True) + EPSILON)
    mixed_rows = inputs + attention * scale_attn * post_gain
    scale_out = lax.rsqrt(jnp.mean(mixed_rows * mixed_rows, axis=-1, keepdims=True) + EPSILON)
    final_rows = (mixed_rows * scale_out * final_gain).astype(jnp.bfloat16)
    logits = times_transposed(final_rows, label_table)
    label_cap = jnp.tanh(logits / LABEL_CAP)
    label_exp = jnp.exp(LABEL_CAP * label_cap)
    chance = label_exp / jnp.sum(label_exp, axis=-1, keepdims=True)
    live_rows = (offsets < length)[:, None]
    onehot = (jnp.arange(LABELS, dtype=jnp.int32) == target).astype(jnp.float32)[None, :]
    grad_logit = (
        jnp.where(live_rows, chance - onehot, 0.0) * (1.0 - label_cap * label_cap)
    ).astype(jnp.bfloat16)
    grad_final = jnp.dot(grad_logit, label_table, preferred_element_type=jnp.float32)
    scaled_final = grad_final * final_gain
    cube_out = scale_out * scale_out * scale_out
    grad_mixed = scale_out * scaled_final - mixed_rows * cube_out * jnp.mean(
        scaled_final * mixed_rows, axis=-1, keepdims=True
    )
    scaled_post = grad_mixed * post_gain
    cube_attn = scale_attn * scale_attn * scale_attn
    grad_attention = scale_attn * scaled_post - attention * cube_attn * jnp.mean(
        scaled_post * attention, axis=-1, keepdims=True
    )
    grad_context = jnp.dot(
        grad_attention.astype(jnp.bfloat16), w_out_t, preferred_element_type=jnp.float32
    ).astype(jnp.bfloat16)
    grad_four = grad_context.reshape(tok_rows, local_kv, group_size, HD).transpose(1, 2, 0, 3)
    grad_prob = jnp.einsum(
        "kgid,kjd->kgij", grad_four, values_own, preferred_element_type=jnp.float32
    )
    grad_score = (
        soft_weights
        * (grad_prob - jnp.sum(soft_weights * grad_prob, axis=-1, keepdims=True))
        * (1.0 - capped * capped)
    )
    score_round = grad_score.astype(jnp.bfloat16)
    grad_query = jnp.einsum(
        "kgij,kjd->kgid", score_round, keys_own, preferred_element_type=jnp.float32
    ).reshape(local_heads, tok_rows, HD)
    grad_queries = rotate_back(grad_query * QUERY_SCALE, cos_table, sin_table).astype(jnp.bfloat16)
    grad_key = jnp.einsum(
        "kgij,kgid->kjd", score_round, query_four, preferred_element_type=jnp.float32
    )
    grad_value = jnp.einsum("kgij,kgid->kjd", attend, grad_four, preferred_element_type=jnp.float32)
    grad_keys = rotate_back(grad_key, cos_table, sin_table).astype(jnp.bfloat16)
    grad_values = grad_value.astype(jnp.bfloat16)
    query_rows = grad_queries.transpose(1, 0, 2).reshape(tok_rows, local_heads * HD)
    key_rows = grad_keys.transpose(1, 0, 2).reshape(tok_rows, local_kv * HD)
    value_rows = grad_values.transpose(1, 0, 2).reshape(tok_rows, local_kv * HD)
    grad_part = (
        times_transposed(query_rows, w_query)
        + times_transposed(key_rows, w_key)
        + times_transposed(value_rows, w_value)
    )
    cube_in = scale_in * scale_in * scale_in
    grad_normed = pair_sum(grad_part.astype(jnp.bfloat16))
    scaled_in = grad_normed * pre_gain
    row_stat = jnp.mean(scaled_in * inputs, axis=-1, keepdims=True)
    grad_full = scale_in * scaled_in - inputs * cube_in * row_stat + grad_mixed
    grad_rows = lax.dynamic_slice_in_dim(grad_full, core_rank * half_width, half_width, 1)
    return lax.all_to_all(
        grad_rows.astype(jnp.bfloat16), "seq", split_axis=0, concat_axis=0, tiled=True
    )


def solution(mesh):
    return jax.shard_map(
        shards,
        mesh=mesh,
        in_specs=(
            P(("groups", "seq"), "wg"),
            P(),
            P("seq", "wg"),
            P("seq", "wg"),
            P("seq", "wg"),
            P("wg", "seq"),
            P(),
            P(),
            P(),
            P("groups"),
            P("groups"),
        ),
        out_specs=P(("groups", "seq"), "wg"),
        check_vma=False,
    )
```

```python
import functools

import jax
import jax.numpy as jnp
from jax import lax
from jax.sharding import PartitionSpec as P

HD = 128
LABELS = 64


EPSILON = 1e-06
ATTEND_CAP = 50.0
LABEL_CAP = 30.0
QUERY_SCALE = 1.0 / 12.0


def rope_tables(positions, head_width):
    frequency = 10000.0 ** (-2.0 * jnp.arange(head_width // 2, dtype=jnp.float32) / head_width)
    angles = positions.astype(jnp.float32)[:, None] * frequency[None, :]
    return (jnp.cos(angles), jnp.sin(angles))


def rotate(values, cos_table, sin_table):
    half_width = values.shape[-1] // 2
    lower_part = values[..., :half_width]
    upper_part = values[..., half_width:]
    return jnp.concatenate(
        [
            lower_part * cos_table - upper_part * sin_table,
            upper_part * cos_table + lower_part * sin_table,
        ],
        axis=-1,
    )


def rotate_back(values, cos_table, sin_table):
    half_width = values.shape[-1] // 2
    lower_part = values[..., :half_width]
    upper_part = values[..., half_width:]
    return jnp.concatenate(
        [
            lower_part * cos_table + upper_part * sin_table,
            upper_part * cos_table - lower_part * sin_table,
        ],
        axis=-1,
    )


def times_transposed(left_side, right_side):
    return lax.dot_general(
        left_side, right_side, (((1,), (1,)), ((), ())), preferred_element_type=jnp.float32
    )


def pair_sum(rounded_part):
    other = lax.ppermute(rounded_part, "wg", perm=[(0, 1), (1, 0)])
    return rounded_part.astype(jnp.float32) + other.astype(jnp.float32)


def ring_order(n):
    if n % 2:
        return list(range(n))
    return list(range(0, n, 2)) + list(range(n - 1, 0, -2))


def ring_gather(front, back, seq_rank, n):
    order = ring_order(n)
    position = [0] * n
    for place, member in enumerate(order):
        position[member] = place
    forward_pairs = [(order[p], order[(p + 1) % n]) for p in range(n)]
    backward_pairs = [(order[p], order[(p - 1) % n]) for p in range(n)]
    order_table = jnp.array(order, dtype=jnp.int32)
    place = jnp.array(position, dtype=jnp.int32)[seq_rank]
    rows = front.shape[0]
    front_all = jnp.zeros((n * rows, front.shape[1]), front.dtype)
    back_all = jnp.zeros((n * rows, back.shape[1]), back.dtype)
    front_all = lax.dynamic_update_slice(front_all, front, (seq_rank * rows, 0))
    back_all = lax.dynamic_update_slice(back_all, back, (seq_rank * rows, 0))
    for step in range(1, n):
        front = lax.ppermute(front, "seq", forward_pairs)
        back = lax.ppermute(back, "seq", backward_pairs)
        front_src = order_table[(place - step) % n]
        back_src = order_table[(place + step) % n]
        front_all = lax.dynamic_update_slice(front_all, front, (front_src * rows, 0))
        back_all = lax.dynamic_update_slice(back_all, back, (back_src * rows, 0))
    return front_all, back_all


def shards(
    n_seq,
    generator_rows,
    pre_gain,
    query_weight,
    key_weight,
    value_weight,
    out_weight,
    post_gain,
    final_gain,
    label_table,
    lengths,
    label_index,
):
    seq_rank = lax.axis_index("seq")
    core_rank = lax.axis_index("wg")
    whole_rows = lax.all_gather(generator_rows, "wg", axis=1, tiled=True)
    guard_rows = lax.all_to_all(whole_rows, "seq", split_axis=0, concat_axis=0, tiled=True)
    q_cols = query_weight.shape[1]
    k_cols = key_weight.shape[1]
    front = jnp.concatenate([query_weight, key_weight], axis=1)
    back = jnp.concatenate([value_weight, out_weight.T], axis=1)
    front_all, back_all = ring_gather(front, back, seq_rank, n_seq)
    w_query = front_all[:, :q_cols]
    w_key = front_all[:, q_cols:]
    w_value = back_all[:, :k_cols]
    w_out_t = back_all[:, k_cols:]
    tok_rows = guard_rows.shape[0]
    half_width = generator_rows.shape[1]
    local_heads = w_query.shape[1] // HD
    local_kv = w_key.shape[1] // HD
    group_size = local_heads // local_kv
    length = lax.dynamic_index_in_dim(lengths, seq_rank, 0, keepdims=False)
    target = lax.dynamic_index_in_dim(label_index, seq_rank, 0, keepdims=False)
    offsets = jnp.arange(tok_rows, dtype=jnp.int32)
    cos_table, sin_table = rope_tables(offsets, HD)
    inputs = guard_rows.astype(jnp.float32)
    scale_in = lax.rsqrt(jnp.mean(inputs * inputs, axis=-1, keepdims=True) + EPSILON)
    normed = (inputs * scale_in * pre_gain).astype(jnp.bfloat16)
    query_proj = (
        jnp.dot(normed, w_query, preferred_element_type=jnp.float32)
        .reshape(tok_rows, local_heads, HD)
        .transpose(1, 0, 2)
    )
    queries = (rotate(query_proj, cos_table, sin_table) * QUERY_SCALE).astype(jnp.bfloat16)
    key_proj = (
        jnp.dot(normed, w_key, preferred_element_type=jnp.float32)
        .reshape(tok_rows, local_kv, HD)
        .transpose(1, 0, 2)
    )
    keys_own = rotate(key_proj, cos_table, sin_table).astype(jnp.bfloat16)
    values_own = (
        jnp.dot(normed, w_value, preferred_element_type=jnp.float32)
        .astype(jnp.bfloat16)
        .reshape(tok_rows, local_kv, HD)
        .transpose(1, 0, 2)
    )
    allowed = (offsets[None, :] <= offsets[:, None]) & (offsets[None, :] < length)
    query_four = queries.reshape(local_kv, group_size, tok_rows, HD)
    raw_scores = jnp.einsum(
        "kgid,kjd->kgij", query_four, keys_own, preferred_element_type=jnp.float32
    )
    capped = jnp.tanh(raw_scores / ATTEND_CAP)
    weight_exp = jnp.where(allowed[None, None], jnp.exp(ATTEND_CAP * capped), 0.0)
    soft_weights = weight_exp / jnp.sum(weight_exp, axis=-1, keepdims=True)
    attend = soft_weights.astype(jnp.bfloat16)
    context = jnp.einsum(
        "kgij,kjd->kgid", attend, values_own, preferred_element_type=jnp.float32
    ).astype(jnp.bfloat16)
    context_rows = (
        context.reshape(local_heads, tok_rows, HD)
        .transpose(1, 0, 2)
        .reshape(tok_rows, local_heads * HD)
    )
    out_part = times_transposed(context_rows, w_out_t)
    attention = pair_sum(out_part.astype(jnp.bfloat16))
    scale_attn = lax.rsqrt(jnp.mean(attention * attention, axis=-1, keepdims=True) + EPSILON)
    mixed_rows = inputs + attention * scale_attn * post_gain
    scale_out = lax.rsqrt(jnp.mean(mixed_rows * mixed_rows, axis=-1, keepdims=True) + EPSILON)
    final_rows = (mixed_rows * scale_out * final_gain).astype(jnp.bfloat16)
    logits = times_transposed(final_rows, label_table)
    label_cap = jnp.tanh(logits / LABEL_CAP)
    label_exp = jnp.exp(LABEL_CAP * label_cap)
    chance = label_exp / jnp.sum(label_exp, axis=-1, keepdims=True)
    live_rows = (offsets < length)[:, None]
    onehot = (jnp.arange(LABELS, dtype=jnp.int32) == target).astype(jnp.float32)[None, :]
    grad_logit = (
        jnp.where(live_rows, chance - onehot, 0.0) * (1.0 - label_cap * label_cap)
    ).astype(jnp.bfloat16)
    grad_final = jnp.dot(grad_logit, label_table, preferred_element_type=jnp.float32)
    scaled_final = grad_final * final_gain
    cube_out = scale_out * scale_out * scale_out
    grad_mixed = scale_out * scaled_final - mixed_rows * cube_out * jnp.mean(
        scaled_final * mixed_rows, axis=-1, keepdims=True
    )
    scaled_post = grad_mixed * post_gain
    cube_attn = scale_attn * scale_attn * scale_attn
    grad_attention = scale_attn * scaled_post - attention * cube_attn * jnp.mean(
        scaled_post * attention, axis=-1, keepdims=True
    )
    grad_context = jnp.dot(
        grad_attention.astype(jnp.bfloat16), w_out_t, preferred_element_type=jnp.float32
    ).astype(jnp.bfloat16)
    grad_four = grad_context.reshape(tok_rows, local_kv, group_size, HD).transpose(1, 2, 0, 3)
    grad_prob = jnp.einsum(
        "kgid,kjd->kgij", grad_four, values_own, preferred_element_type=jnp.float32
    )
    grad_score = (
        soft_weights
        * (grad_prob - jnp.sum(soft_weights * grad_prob, axis=-1, keepdims=True))
        * (1.0 - capped * capped)
    )
    score_round = grad_score.astype(jnp.bfloat16)
    grad_query = jnp.einsum(
        "kgij,kjd->kgid", score_round, keys_own, preferred_element_type=jnp.float32
    ).reshape(local_heads, tok_rows, HD)
    grad_queries = rotate_back(grad_query * QUERY_SCALE, cos_table, sin_table).astype(jnp.bfloat16)
    grad_key = jnp.einsum(
        "kgij,kgid->kjd", score_round, query_four, preferred_element_type=jnp.float32
    )
    grad_value = jnp.einsum("kgij,kgid->kjd", attend, grad_four, preferred_element_type=jnp.float32)
    grad_keys = rotate_back(grad_key, cos_table, sin_table).astype(jnp.bfloat16)
    grad_values = grad_value.astype(jnp.bfloat16)
    query_rows = grad_queries.transpose(1, 0, 2).reshape(tok_rows, local_heads * HD)
    key_rows = grad_keys.transpose(1, 0, 2).reshape(tok_rows, local_kv * HD)
    value_rows = grad_values.transpose(1, 0, 2).reshape(tok_rows, local_kv * HD)
    grad_part = (
        times_transposed(query_rows, w_query)
        + times_transposed(key_rows, w_key)
        + times_transposed(value_rows, w_value)
    )
    cube_in = scale_in * scale_in * scale_in
    grad_normed = pair_sum(grad_part.astype(jnp.bfloat16))
    scaled_in = grad_normed * pre_gain
    row_stat = jnp.mean(scaled_in * inputs, axis=-1, keepdims=True)
    grad_full = scale_in * scaled_in - inputs * cube_in * row_stat + grad_mixed
    grad_rows = lax.dynamic_slice_in_dim(grad_full, core_rank * half_width, half_width, 1)
    return lax.all_to_all(
        grad_rows.astype(jnp.bfloat16), "seq", split_axis=0, concat_axis=0, tiled=True
    )


def solution(mesh):
    return jax.shard_map(
        functools.partial(shards, mesh.shape["seq"]),
        mesh=mesh,
        in_specs=(
            P(("groups", "seq"), "wg"),
            P(),
            P("seq", "wg"),
            P("seq", "wg"),
            P("seq", "wg"),
            P("wg", "seq"),
            P(),
            P(),
            P(),
            P("groups"),
            P("groups"),
        ),
        out_specs=P(("groups", "seq"), "wg"),
        check_vma=False,
    )
```

```python
import functools

import jax
import jax.numpy as jnp
from jax import lax
from jax.sharding import PartitionSpec as P

HD = 128
LABELS = 64


EPSILON = 1e-06
ATTEND_CAP = 50.0
LABEL_CAP = 30.0
QUERY_SCALE = 1.0 / 12.0


def rope_tables(positions, head_width):
    frequency = 10000.0 ** (-2.0 * jnp.arange(head_width // 2, dtype=jnp.float32) / head_width)
    angles = positions.astype(jnp.float32)[:, None] * frequency[None, :]
    return (jnp.cos(angles), jnp.sin(angles))


def rotate(values, cos_table, sin_table):
    half_width = values.shape[-1] // 2
    lower_part = values[..., :half_width]
    upper_part = values[..., half_width:]
    return jnp.concatenate(
        [
            lower_part * cos_table - upper_part * sin_table,
            upper_part * cos_table + lower_part * sin_table,
        ],
        axis=-1,
    )


def rotate_back(values, cos_table, sin_table):
    half_width = values.shape[-1] // 2
    lower_part = values[..., :half_width]
    upper_part = values[..., half_width:]
    return jnp.concatenate(
        [
            lower_part * cos_table + upper_part * sin_table,
            upper_part * cos_table - lower_part * sin_table,
        ],
        axis=-1,
    )


def times_transposed(left_side, right_side):
    return lax.dot_general(
        left_side, right_side, (((1,), (1,)), ((), ())), preferred_element_type=jnp.float32
    )


def pair_sum(rounded_part):
    other = lax.ppermute(rounded_part, "wg", perm=[(0, 1), (1, 0)])
    return rounded_part.astype(jnp.float32) + other.astype(jnp.float32)


def ring_order(n):
    if n % 2:
        return list(range(n))
    return list(range(0, n, 2)) + list(range(n - 1, 0, -2))


def ring_gather(front, back, seq_rank, n):
    order = ring_order(n)
    position = [0] * n
    for place, member in enumerate(order):
        position[member] = place
    forward_pairs = [(order[p], order[(p + 1) % n]) for p in range(n)]
    backward_pairs = [(order[p], order[(p - 1) % n]) for p in range(n)]
    place = jnp.array(position, dtype=jnp.int32)[seq_rank]
    steps = jnp.arange(n, dtype=jnp.int32)
    block_of = jnp.array(order, dtype=jnp.int32)[(place - steps) % n]
    slot_of = (place - jnp.array(position, dtype=jnp.int32)) % n
    front_pieces = [front]
    back_pieces = [back]
    for step in range(1, n):
        front_pieces.append(lax.ppermute(front_pieces[-1], "seq", forward_pairs))
        back_pieces.append(lax.ppermute(back_pieces[-1], "seq", backward_pairs))
    back_pieces = [back_pieces[(n - k) % n] for k in range(n)]
    front_all = jnp.concatenate(front_pieces, axis=0)
    back_all = jnp.concatenate(back_pieces, axis=0)
    return front_all, back_all, block_of, slot_of


def permute_blocks(values, block_order, n):
    lead = values.shape[:-1]
    width = values.shape[-1] // n
    blocks = values.reshape(lead + (n, width))
    return jnp.take(blocks, block_order, axis=-2).reshape(values.shape)


def shards(
    n_seq,
    generator_rows,
    pre_gain,
    query_weight,
    key_weight,
    value_weight,
    out_weight,
    post_gain,
    final_gain,
    label_table,
    lengths,
    label_index,
):
    seq_rank = lax.axis_index("seq")
    core_rank = lax.axis_index("wg")
    whole_rows = lax.all_gather(generator_rows, "wg", axis=1, tiled=True)
    guard_rows = lax.all_to_all(whole_rows, "seq", split_axis=0, concat_axis=0, tiled=True)
    q_cols = query_weight.shape[1]
    k_cols = key_weight.shape[1]
    front = jnp.concatenate([query_weight, key_weight], axis=1)
    back = jnp.concatenate([value_weight, out_weight.T], axis=1)
    front_all, back_all, block_of, slot_of = ring_gather(front, back, seq_rank, n_seq)
    guard_rows = permute_blocks(guard_rows, block_of, n_seq)
    pre_gain = permute_blocks(pre_gain, block_of, n_seq)
    post_gain = permute_blocks(post_gain, block_of, n_seq)
    final_gain = permute_blocks(final_gain, block_of, n_seq)
    label_table = permute_blocks(label_table, block_of, n_seq)
    w_query = front_all[:, :q_cols]
    w_key = front_all[:, q_cols:]
    w_value = back_all[:, :k_cols]
    w_out_t = back_all[:, k_cols:]
    tok_rows = guard_rows.shape[0]
    half_width = generator_rows.shape[1]
    local_heads = w_query.shape[1] // HD
    local_kv = w_key.shape[1] // HD
    group_size = local_heads // local_kv
    length = lax.dynamic_index_in_dim(lengths, seq_rank, 0, keepdims=False)
    target = lax.dynamic_index_in_dim(label_index, seq_rank, 0, keepdims=False)
    offsets = jnp.arange(tok_rows, dtype=jnp.int32)
    cos_table, sin_table = rope_tables(offsets, HD)
    inputs = guard_rows.astype(jnp.float32)
    scale_in = lax.rsqrt(jnp.mean(inputs * inputs, axis=-1, keepdims=True) + EPSILON)
    normed = (inputs * scale_in * pre_gain).astype(jnp.bfloat16)
    query_proj = (
        jnp.dot(normed, w_query, preferred_element_type=jnp.float32)
        .reshape(tok_rows, local_heads, HD)
        .transpose(1, 0, 2)
    )
    queries = (rotate(query_proj, cos_table, sin_table) * QUERY_SCALE).astype(jnp.bfloat16)
    key_proj = (
        jnp.dot(normed, w_key, preferred_element_type=jnp.float32)
        .reshape(tok_rows, local_kv, HD)
        .transpose(1, 0, 2)
    )
    keys_own = rotate(key_proj, cos_table, sin_table).astype(jnp.bfloat16)
    values_own = (
        jnp.dot(normed, w_value, preferred_element_type=jnp.float32)
        .astype(jnp.bfloat16)
        .reshape(tok_rows, local_kv, HD)
        .transpose(1, 0, 2)
    )
    allowed = (offsets[None, :] <= offsets[:, None]) & (offsets[None, :] < length)
    query_four = queries.reshape(local_kv, group_size, tok_rows, HD)
    raw_scores = jnp.einsum(
        "kgid,kjd->kgij", query_four, keys_own, preferred_element_type=jnp.float32
    )
    capped = jnp.tanh(raw_scores / ATTEND_CAP)
    weight_exp = jnp.where(allowed[None, None], jnp.exp(ATTEND_CAP * capped), 0.0)
    soft_weights = weight_exp / jnp.sum(weight_exp, axis=-1, keepdims=True)
    attend = soft_weights.astype(jnp.bfloat16)
    context = jnp.einsum(
        "kgij,kjd->kgid", attend, values_own, preferred_element_type=jnp.float32
    ).astype(jnp.bfloat16)
    context_rows = (
        context.reshape(local_heads, tok_rows, HD)
        .transpose(1, 0, 2)
        .reshape(tok_rows, local_heads * HD)
    )
    out_part = times_transposed(context_rows, w_out_t)
    attention = pair_sum(out_part.astype(jnp.bfloat16))
    scale_attn = lax.rsqrt(jnp.mean(attention * attention, axis=-1, keepdims=True) + EPSILON)
    mixed_rows = inputs + attention * scale_attn * post_gain
    scale_out = lax.rsqrt(jnp.mean(mixed_rows * mixed_rows, axis=-1, keepdims=True) + EPSILON)
    final_rows = (mixed_rows * scale_out * final_gain).astype(jnp.bfloat16)
    logits = times_transposed(final_rows, label_table)
    label_cap = jnp.tanh(logits / LABEL_CAP)
    label_exp = jnp.exp(LABEL_CAP * label_cap)
    chance = label_exp / jnp.sum(label_exp, axis=-1, keepdims=True)
    live_rows = (offsets < length)[:, None]
    onehot = (jnp.arange(LABELS, dtype=jnp.int32) == target).astype(jnp.float32)[None, :]
    grad_logit = (
        jnp.where(live_rows, chance - onehot, 0.0) * (1.0 - label_cap * label_cap)
    ).astype(jnp.bfloat16)
    grad_final = jnp.dot(grad_logit, label_table, preferred_element_type=jnp.float32)
    scaled_final = grad_final * final_gain
    cube_out = scale_out * scale_out * scale_out
    grad_mixed = scale_out * scaled_final - mixed_rows * cube_out * jnp.mean(
        scaled_final * mixed_rows, axis=-1, keepdims=True
    )
    scaled_post = grad_mixed * post_gain
    cube_attn = scale_attn * scale_attn * scale_attn
    grad_attention = scale_attn * scaled_post - attention * cube_attn * jnp.mean(
        scaled_post * attention, axis=-1, keepdims=True
    )
    grad_context = jnp.dot(
        grad_attention.astype(jnp.bfloat16), w_out_t, preferred_element_type=jnp.float32
    ).astype(jnp.bfloat16)
    grad_four = grad_context.reshape(tok_rows, local_kv, group_size, HD).transpose(1, 2, 0, 3)
    grad_prob = jnp.einsum(
        "kgid,kjd->kgij", grad_four, values_own, preferred_element_type=jnp.float32
    )
    grad_score = (
        soft_weights
        * (grad_prob - jnp.sum(soft_weights * grad_prob, axis=-1, keepdims=True))
        * (1.0 - capped * capped)
    )
    score_round = grad_score.astype(jnp.bfloat16)
    grad_query = jnp.einsum(
        "kgij,kjd->kgid", score_round, keys_own, preferred_element_type=jnp.float32
    ).reshape(local_heads, tok_rows, HD)
    grad_queries = rotate_back(grad_query * QUERY_SCALE, cos_table, sin_table).astype(jnp.bfloat16)
    grad_key = jnp.einsum(
        "kgij,kgid->kjd", score_round, query_four, preferred_element_type=jnp.float32
    )
    grad_value = jnp.einsum("kgij,kgid->kjd", attend, grad_four, preferred_element_type=jnp.float32)
    grad_keys = rotate_back(grad_key, cos_table, sin_table).astype(jnp.bfloat16)
    grad_values = grad_value.astype(jnp.bfloat16)
    query_rows = grad_queries.transpose(1, 0, 2).reshape(tok_rows, local_heads * HD)
    key_rows = grad_keys.transpose(1, 0, 2).reshape(tok_rows, local_kv * HD)
    value_rows = grad_values.transpose(1, 0, 2).reshape(tok_rows, local_kv * HD)
    grad_part = (
        times_transposed(query_rows, w_query)
        + times_transposed(key_rows, w_key)
        + times_transposed(value_rows, w_value)
    )
    cube_in = scale_in * scale_in * scale_in
    grad_normed = pair_sum(grad_part.astype(jnp.bfloat16))
    scaled_in = grad_normed * pre_gain
    row_stat = jnp.mean(scaled_in * inputs, axis=-1, keepdims=True)
    grad_full = scale_in * scaled_in - inputs * cube_in * row_stat + grad_mixed
    grad_full = permute_blocks(grad_full, slot_of, n_seq)
    grad_rows = lax.dynamic_slice_in_dim(grad_full, core_rank * half_width, half_width, 1)
    return lax.all_to_all(
        grad_rows.astype(jnp.bfloat16), "seq", split_axis=0, concat_axis=0, tiled=True
    )


def solution(mesh):
    return jax.shard_map(
        functools.partial(shards, mesh.shape["seq"]),
        mesh=mesh,
        in_specs=(
            P(("groups", "seq"), "wg"),
            P(),
            P("seq", "wg"),
            P("seq", "wg"),
            P("seq", "wg"),
            P("wg", "seq"),
            P(),
            P(),
            P(),
            P("groups"),
            P("groups"),
        ),
        out_specs=P(("groups", "seq"), "wg"),
        check_vma=False,
    )
```

```python
import functools

import jax
import jax.numpy as jnp
from jax import lax
from jax.sharding import PartitionSpec as P

HD = 128
LABELS = 64


EPSILON = 1e-06
ATTEND_CAP = 50.0
LABEL_CAP = 30.0
QUERY_SCALE = 1.0 / 12.0


def rope_tables(positions, head_width):
    frequency = 10000.0 ** (-2.0 * jnp.arange(head_width // 2, dtype=jnp.float32) / head_width)
    angles = positions.astype(jnp.float32)[:, None] * frequency[None, :]
    return (jnp.cos(angles), jnp.sin(angles))


def rotate(values, cos_table, sin_table):
    half_width = values.shape[-1] // 2
    lower_part = values[..., :half_width]
    upper_part = values[..., half_width:]
    return jnp.concatenate(
        [
            lower_part * cos_table - upper_part * sin_table,
            upper_part * cos_table + lower_part * sin_table,
        ],
        axis=-1,
    )


def rotate_back(values, cos_table, sin_table):
    half_width = values.shape[-1] // 2
    lower_part = values[..., :half_width]
    upper_part = values[..., half_width:]
    return jnp.concatenate(
        [
            lower_part * cos_table + upper_part * sin_table,
            upper_part * cos_table - lower_part * sin_table,
        ],
        axis=-1,
    )


def times_transposed(left_side, right_side):
    return lax.dot_general(
        left_side, right_side, (((1,), (1,)), ((), ())), preferred_element_type=jnp.float32
    )


def pair_sum(rounded_part):
    other = lax.ppermute(rounded_part, "wg", perm=[(0, 1), (1, 0)])
    return rounded_part.astype(jnp.float32) + other.astype(jnp.float32)


def ring_order(n):
    if n % 2:
        return list(range(n))
    return list(range(0, n, 2)) + list(range(n - 1, 0, -2))


def ring_gather(front, back, seq_rank, group_rank, n):
    order = ring_order(n)
    position = [0] * n
    for place, member in enumerate(order):
        position[member] = place
    forward_pairs = [(order[p], order[(p + 1) % n]) for p in range(n)]
    backward_pairs = [(order[p], order[(p - 1) % n]) for p in range(n)]
    group_pairs = [(0, 1), (1, 0)]
    place = jnp.array(position, dtype=jnp.int32)[seq_rank]
    steps = jnp.arange(n, dtype=jnp.int32)
    block_of = jnp.array(order, dtype=jnp.int32)[(place - steps) % n]
    slot_of = (place - jnp.array(position, dtype=jnp.int32)) % n
    first_group = group_rank == 0

    def thirds(values):
        width = values.shape[1] // 3
        return [values[:, i * width:(i + 1) * width] for i in range(3)]

    def carried(values):
        left, middle, right = thirds(values)
        return jnp.stack([jnp.where(first_group, left, right), middle])

    front_ring = [carried(front)]
    back_ring = [carried(back)]
    for step in range(1, n):
        front_ring.append(lax.ppermute(front_ring[-1], "seq", forward_pairs))
        back_ring.append(lax.ppermute(back_ring[-1], "seq", backward_pairs))
    front_pieces = [front]
    back_pieces = [back]
    for step in range(1, n):
        handed = lax.ppermute(
            jnp.stack([front_ring[step][0], back_ring[step][0]]), "groups", group_pairs
        )
        for ring, pieces, other in ((front_ring, front_pieces, handed[0]), (back_ring, back_pieces, handed[1])):
            own, middle = ring[step][0], ring[step][1]
            pieces.append(
                jnp.concatenate(
                    [jnp.where(first_group, own, other), middle, jnp.where(first_group, other, own)],
                    axis=1,
                )
            )
    back_pieces = [back_pieces[(n - k) % n] for k in range(n)]
    front_all = jnp.concatenate(front_pieces, axis=0)
    back_all = jnp.concatenate(back_pieces, axis=0)
    return front_all, back_all, block_of, slot_of


def permute_blocks(values, block_order, n):
    lead = values.shape[:-1]
    width = values.shape[-1] // n
    blocks = values.reshape(lead + (n, width))
    return jnp.take(blocks, block_order, axis=-2).reshape(values.shape)


def shards(
    n_seq,
    generator_rows,
    pre_gain,
    query_weight,
    key_weight,
    value_weight,
    out_weight,
    post_gain,
    final_gain,
    label_table,
    lengths,
    label_index,
):
    seq_rank = lax.axis_index("seq")
    core_rank = lax.axis_index("wg")
    whole_rows = lax.all_gather(generator_rows, "wg", axis=1, tiled=True)
    guard_rows = lax.all_to_all(whole_rows, "seq", split_axis=0, concat_axis=0, tiled=True)
    q_cols = query_weight.shape[1]
    k_cols = key_weight.shape[1]
    front = jnp.concatenate([query_weight, key_weight], axis=1)
    back = jnp.concatenate([value_weight, out_weight.T], axis=1)
    front_all, back_all, block_of, slot_of = ring_gather(front, back, seq_rank, lax.axis_index("groups"), n_seq)
    guard_rows = permute_blocks(guard_rows, block_of, n_seq)
    pre_gain = permute_blocks(pre_gain, block_of, n_seq)
    post_gain = permute_blocks(post_gain, block_of, n_seq)
    final_gain = permute_blocks(final_gain, block_of, n_seq)
    label_table = permute_blocks(label_table, block_of, n_seq)
    w_query = front_all[:, :q_cols]
    w_key = front_all[:, q_cols:]
    w_value = back_all[:, :k_cols]
    w_out_t = back_all[:, k_cols:]
    tok_rows = guard_rows.shape[0]
    half_width = generator_rows.shape[1]
    local_heads = w_query.shape[1] // HD
    local_kv = w_key.shape[1] // HD
    group_size = local_heads // local_kv
    length = lax.dynamic_index_in_dim(lengths, seq_rank, 0, keepdims=False)
    target = lax.dynamic_index_in_dim(label_index, seq_rank, 0, keepdims=False)
    offsets = jnp.arange(tok_rows, dtype=jnp.int32)
    cos_table, sin_table = rope_tables(offsets, HD)
    inputs = guard_rows.astype(jnp.float32)
    scale_in = lax.rsqrt(jnp.mean(inputs * inputs, axis=-1, keepdims=True) + EPSILON)
    normed = (inputs * scale_in * pre_gain).astype(jnp.bfloat16)
    query_proj = (
        jnp.dot(normed, w_query, preferred_element_type=jnp.float32)
        .reshape(tok_rows, local_heads, HD)
        .transpose(1, 0, 2)
    )
    queries = (rotate(query_proj, cos_table, sin_table) * QUERY_SCALE).astype(jnp.bfloat16)
    key_proj = (
        jnp.dot(normed, w_key, preferred_element_type=jnp.float32)
        .reshape(tok_rows, local_kv, HD)
        .transpose(1, 0, 2)
    )
    keys_own = rotate(key_proj, cos_table, sin_table).astype(jnp.bfloat16)
    values_own = (
        jnp.dot(normed, w_value, preferred_element_type=jnp.float32)
        .astype(jnp.bfloat16)
        .reshape(tok_rows, local_kv, HD)
        .transpose(1, 0, 2)
    )
    allowed = (offsets[None, :] <= offsets[:, None]) & (offsets[None, :] < length)
    query_four = queries.reshape(local_kv, group_size, tok_rows, HD)
    raw_scores = jnp.einsum(
        "kgid,kjd->kgij", query_four, keys_own, preferred_element_type=jnp.float32
    )
    capped = jnp.tanh(raw_scores / ATTEND_CAP)
    weight_exp = jnp.where(allowed[None, None], jnp.exp(ATTEND_CAP * capped), 0.0)
    soft_weights = weight_exp / jnp.sum(weight_exp, axis=-1, keepdims=True)
    attend = soft_weights.astype(jnp.bfloat16)
    context = jnp.einsum(
        "kgij,kjd->kgid", attend, values_own, preferred_element_type=jnp.float32
    ).astype(jnp.bfloat16)
    context_rows = (
        context.reshape(local_heads, tok_rows, HD)
        .transpose(1, 0, 2)
        .reshape(tok_rows, local_heads * HD)
    )
    out_part = times_transposed(context_rows, w_out_t)
    attention = pair_sum(out_part.astype(jnp.bfloat16))
    scale_attn = lax.rsqrt(jnp.mean(attention * attention, axis=-1, keepdims=True) + EPSILON)
    mixed_rows = inputs + attention * scale_attn * post_gain
    scale_out = lax.rsqrt(jnp.mean(mixed_rows * mixed_rows, axis=-1, keepdims=True) + EPSILON)
    final_rows = (mixed_rows * scale_out * final_gain).astype(jnp.bfloat16)
    logits = times_transposed(final_rows, label_table)
    label_cap = jnp.tanh(logits / LABEL_CAP)
    label_exp = jnp.exp(LABEL_CAP * label_cap)
    chance = label_exp / jnp.sum(label_exp, axis=-1, keepdims=True)
    live_rows = (offsets < length)[:, None]
    onehot = (jnp.arange(LABELS, dtype=jnp.int32) == target).astype(jnp.float32)[None, :]
    grad_logit = (
        jnp.where(live_rows, chance - onehot, 0.0) * (1.0 - label_cap * label_cap)
    ).astype(jnp.bfloat16)
    grad_final = jnp.dot(grad_logit, label_table, preferred_element_type=jnp.float32)
    scaled_final = grad_final * final_gain
    cube_out = scale_out * scale_out * scale_out
    grad_mixed = scale_out * scaled_final - mixed_rows * cube_out * jnp.mean(
        scaled_final * mixed_rows, axis=-1, keepdims=True
    )
    scaled_post = grad_mixed * post_gain
    cube_attn = scale_attn * scale_attn * scale_attn
    grad_attention = scale_attn * scaled_post - attention * cube_attn * jnp.mean(
        scaled_post * attention, axis=-1, keepdims=True
    )
    grad_context = jnp.dot(
        grad_attention.astype(jnp.bfloat16), w_out_t, preferred_element_type=jnp.float32
    ).astype(jnp.bfloat16)
    grad_four = grad_context.reshape(tok_rows, local_kv, group_size, HD).transpose(1, 2, 0, 3)
    grad_prob = jnp.einsum(
        "kgid,kjd->kgij", grad_four, values_own, preferred_element_type=jnp.float32
    )
    grad_score = (
        soft_weights
        * (grad_prob - jnp.sum(soft_weights * grad_prob, axis=-1, keepdims=True))
        * (1.0 - capped * capped)
    )
    score_round = grad_score.astype(jnp.bfloat16)
    grad_query = jnp.einsum(
        "kgij,kjd->kgid", score_round, keys_own, preferred_element_type=jnp.float32
    ).reshape(local_heads, tok_rows, HD)
    grad_queries = rotate_back(grad_query * QUERY_SCALE, cos_table, sin_table).astype(jnp.bfloat16)
    grad_key = jnp.einsum(
        "kgij,kgid->kjd", score_round, query_four, preferred_element_type=jnp.float32
    )
    grad_value = jnp.einsum("kgij,kgid->kjd", attend, grad_four, preferred_element_type=jnp.float32)
    grad_keys = rotate_back(grad_key, cos_table, sin_table).astype(jnp.bfloat16)
    grad_values = grad_value.astype(jnp.bfloat16)
    query_rows = grad_queries.transpose(1, 0, 2).reshape(tok_rows, local_heads * HD)
    key_rows = grad_keys.transpose(1, 0, 2).reshape(tok_rows, local_kv * HD)
    value_rows = grad_values.transpose(1, 0, 2).reshape(tok_rows, local_kv * HD)
    grad_part = (
        times_transposed(query_rows, w_query)
        + times_transposed(key_rows, w_key)
        + times_transposed(value_rows, w_value)
    )
    cube_in = scale_in * scale_in * scale_in
    grad_normed = pair_sum(grad_part.astype(jnp.bfloat16))
    scaled_in = grad_normed * pre_gain
    row_stat = jnp.mean(scaled_in * inputs, axis=-1, keepdims=True)
    grad_full = scale_in * scaled_in - inputs * cube_in * row_stat + grad_mixed
    grad_full = permute_blocks(grad_full, slot_of, n_seq)
    grad_rows = lax.dynamic_slice_in_dim(grad_full, core_rank * half_width, half_width, 1)
    return lax.all_to_all(
        grad_rows.astype(jnp.bfloat16), "seq", split_axis=0, concat_axis=0, tiled=True
    )


def solution(mesh):
    return jax.shard_map(
        functools.partial(shards, mesh.shape["seq"]),
        mesh=mesh,
        in_specs=(
            P(("groups", "seq"), "wg"),
            P(),
            P("seq", "wg"),
            P("seq", "wg"),
            P("seq", "wg"),
            P("wg", "seq"),
            P(),
            P(),
            P(),
            P("groups"),
            P("groups"),
        ),
        out_specs=P(("groups", "seq"), "wg"),
        check_vma=False,
    )
```

```python
import functools

import jax
import jax.numpy as jnp
from jax import lax
from jax.sharding import PartitionSpec as P

HD = 128
LABELS = 64


PIECEWISE_RING = 16
EPSILON = 1e-06
ATTEND_CAP = 50.0
LABEL_CAP = 30.0
QUERY_SCALE = 1.0 / 12.0


def rope_tables(positions, head_width):
    frequency = 10000.0 ** (-2.0 * jnp.arange(head_width // 2, dtype=jnp.float32) / head_width)
    angles = positions.astype(jnp.float32)[:, None] * frequency[None, :]
    return (jnp.cos(angles), jnp.sin(angles))


def rotate(values, cos_table, sin_table):
    half_width = values.shape[-1] // 2
    lower_part = values[..., :half_width]
    upper_part = values[..., half_width:]
    return jnp.concatenate(
        [
            lower_part * cos_table - upper_part * sin_table,
            upper_part * cos_table + lower_part * sin_table,
        ],
        axis=-1,
    )


def rotate_back(values, cos_table, sin_table):
    half_width = values.shape[-1] // 2
    lower_part = values[..., :half_width]
    upper_part = values[..., half_width:]
    return jnp.concatenate(
        [
            lower_part * cos_table + upper_part * sin_table,
            upper_part * cos_table - lower_part * sin_table,
        ],
        axis=-1,
    )


def times_transposed(left_side, right_side):
    return lax.dot_general(
        left_side, right_side, (((1,), (1,)), ((), ())), preferred_element_type=jnp.float32
    )


def pair_sum(rounded_part):
    other = lax.ppermute(rounded_part, "wg", perm=[(0, 1), (1, 0)])
    return rounded_part.astype(jnp.float32) + other.astype(jnp.float32)


def ring_order(n):
    if n % 2:
        return list(range(n))
    return list(range(0, n, 2)) + list(range(n - 1, 0, -2))


def ring_gather(front, back, seq_rank, group_rank, n):
    order = ring_order(n)
    position = [0] * n
    for place, member in enumerate(order):
        position[member] = place
    forward_pairs = [(order[p], order[(p + 1) % n]) for p in range(n)]
    backward_pairs = [(order[p], order[(p - 1) % n]) for p in range(n)]
    group_pairs = [(0, 1), (1, 0)]
    place = jnp.array(position, dtype=jnp.int32)[seq_rank]
    steps = jnp.arange(n, dtype=jnp.int32)
    block_of = jnp.array(order, dtype=jnp.int32)[(place - steps) % n]
    slot_of = (place - jnp.array(position, dtype=jnp.int32)) % n
    first_group = group_rank == 0

    def thirds(values):
        width = values.shape[1] // 3
        return [values[:, i * width:(i + 1) * width] for i in range(3)]

    def carried(values):
        left, middle, right = thirds(values)
        return jnp.stack([jnp.where(first_group, left, right), middle])

    front_ring = [carried(front)]
    back_ring = [carried(back)]
    for step in range(1, n):
        front_ring.append(lax.ppermute(front_ring[-1], "seq", forward_pairs))
        back_ring.append(lax.ppermute(back_ring[-1], "seq", backward_pairs))
    front_pieces = [front]
    back_pieces = [back]
    for step in range(1, n):
        handed = lax.ppermute(
            jnp.stack([front_ring[step][0], back_ring[step][0]]), "groups", group_pairs
        )
        for ring, pieces, other in ((front_ring, front_pieces, handed[0]), (back_ring, back_pieces, handed[1])):
            own, middle = ring[step][0], ring[step][1]
            pieces.append(
                jnp.concatenate(
                    [jnp.where(first_group, own, other), middle, jnp.where(first_group, other, own)],
                    axis=1,
                )
            )
    back_pieces = [back_pieces[(n - k) % n] for k in range(n)]
    return front_pieces, back_pieces, block_of, slot_of


def permute_blocks(values, block_order, n):
    lead = values.shape[:-1]
    width = values.shape[-1] // n
    blocks = values.reshape(lead + (n, width))
    return jnp.take(blocks, block_order, axis=-2).reshape(values.shape)


def shards(
    n_seq,
    generator_rows,
    pre_gain,
    query_weight,
    key_weight,
    value_weight,
    out_weight,
    post_gain,
    final_gain,
    label_table,
    lengths,
    label_index,
):
    seq_rank = lax.axis_index("seq")
    core_rank = lax.axis_index("wg")
    whole_rows = lax.all_gather(generator_rows, "wg", axis=1, tiled=True)
    guard_rows = lax.all_to_all(whole_rows, "seq", split_axis=0, concat_axis=0, tiled=True)
    q_cols = query_weight.shape[1]
    k_cols = key_weight.shape[1]
    front = jnp.concatenate([query_weight, key_weight], axis=1)
    back = jnp.concatenate([value_weight, out_weight.T], axis=1)
    front_pieces, back_pieces, block_of, slot_of = ring_gather(
        front, back, seq_rank, lax.axis_index("groups"), n_seq
    )
    guard_rows = permute_blocks(guard_rows, block_of, n_seq)
    pre_gain = permute_blocks(pre_gain, block_of, n_seq)
    post_gain = permute_blocks(post_gain, block_of, n_seq)
    final_gain = permute_blocks(final_gain, block_of, n_seq)
    label_table = permute_blocks(label_table, block_of, n_seq)
    piecewise = n_seq <= PIECEWISE_RING
    if piecewise:
        w_query_t = jnp.concatenate([piece[:, :q_cols].T for piece in front_pieces], axis=1)
        w_key_t = jnp.concatenate([piece[:, q_cols:].T for piece in front_pieces], axis=1)
        w_value_t = jnp.concatenate([piece[:, :k_cols].T for piece in back_pieces], axis=1)
        w_out = jnp.concatenate([piece[:, k_cols:].T for piece in back_pieces], axis=1)
    else:
        front_all = jnp.concatenate(front_pieces, axis=0)
        back_all = jnp.concatenate(back_pieces, axis=0)
        w_query_t = front_all[:, :q_cols].T
        w_key_t = front_all[:, q_cols:].T
        w_value_t = back_all[:, :k_cols].T
        w_out = back_all[:, k_cols:].T
    tok_rows = guard_rows.shape[0]
    half_width = generator_rows.shape[1]
    local_heads = q_cols // HD
    local_kv = k_cols // HD
    group_size = local_heads // local_kv
    length = lax.dynamic_index_in_dim(lengths, seq_rank, 0, keepdims=False)
    target = lax.dynamic_index_in_dim(label_index, seq_rank, 0, keepdims=False)
    offsets = jnp.arange(tok_rows, dtype=jnp.int32)
    cos_table, sin_table = rope_tables(offsets, HD)
    inputs = guard_rows.astype(jnp.float32)
    scale_in = lax.rsqrt(jnp.mean(inputs * inputs, axis=-1, keepdims=True) + EPSILON)
    normed = (inputs * scale_in * pre_gain).astype(jnp.bfloat16)
    if piecewise:
        block_rows = front_pieces[0].shape[0]
        front_proj = None
        back_proj = None
        for index, (front_piece, back_piece) in enumerate(zip(front_pieces, back_pieces)):
            normed_block = normed[:, index * block_rows:(index + 1) * block_rows]
            front_term = jnp.dot(normed_block, front_piece, preferred_element_type=jnp.float32)
            back_term = jnp.dot(normed_block, back_piece[:, :k_cols], preferred_element_type=jnp.float32)
            front_proj = front_term if front_proj is None else front_proj + front_term
            back_proj = back_term if back_proj is None else back_proj + back_term
    else:
        front_proj = jnp.dot(normed, front_all, preferred_element_type=jnp.float32)
        back_proj = jnp.dot(normed, back_all[:, :k_cols], preferred_element_type=jnp.float32)
    query_proj = front_proj[:, :q_cols].reshape(tok_rows, local_heads, HD).transpose(1, 0, 2)
    queries = (rotate(query_proj, cos_table, sin_table) * QUERY_SCALE).astype(jnp.bfloat16)
    key_proj = front_proj[:, q_cols:].reshape(tok_rows, local_kv, HD).transpose(1, 0, 2)
    keys_own = rotate(key_proj, cos_table, sin_table).astype(jnp.bfloat16)
    values_own = (
        back_proj
        .astype(jnp.bfloat16)
        .reshape(tok_rows, local_kv, HD)
        .transpose(1, 0, 2)
    )
    allowed = (offsets[None, :] <= offsets[:, None]) & (offsets[None, :] < length)
    query_four = queries.reshape(local_kv, group_size, tok_rows, HD)
    raw_scores = jnp.einsum(
        "kgid,kjd->kgij", query_four, keys_own, preferred_element_type=jnp.float32
    )
    capped = jnp.tanh(raw_scores / ATTEND_CAP)
    weight_exp = jnp.where(allowed[None, None], jnp.exp(ATTEND_CAP * capped), 0.0)
    soft_weights = weight_exp / jnp.sum(weight_exp, axis=-1, keepdims=True)
    attend = soft_weights.astype(jnp.bfloat16)
    context = jnp.einsum(
        "kgij,kjd->kgid", attend, values_own, preferred_element_type=jnp.float32
    ).astype(jnp.bfloat16)
    context_rows = (
        context.reshape(local_heads, tok_rows, HD)
        .transpose(1, 0, 2)
        .reshape(tok_rows, local_heads * HD)
    )
    out_part = jnp.dot(context_rows, w_out, preferred_element_type=jnp.float32)
    attention = pair_sum(out_part.astype(jnp.bfloat16))
    scale_attn = lax.rsqrt(jnp.mean(attention * attention, axis=-1, keepdims=True) + EPSILON)
    mixed_rows = inputs + attention * scale_attn * post_gain
    scale_out = lax.rsqrt(jnp.mean(mixed_rows * mixed_rows, axis=-1, keepdims=True) + EPSILON)
    final_rows = (mixed_rows * scale_out * final_gain).astype(jnp.bfloat16)
    logits = times_transposed(final_rows, label_table)
    label_cap = jnp.tanh(logits / LABEL_CAP)
    label_exp = jnp.exp(LABEL_CAP * label_cap)
    chance = label_exp / jnp.sum(label_exp, axis=-1, keepdims=True)
    live_rows = (offsets < length)[:, None]
    onehot = (jnp.arange(LABELS, dtype=jnp.int32) == target).astype(jnp.float32)[None, :]
    grad_logit = (
        jnp.where(live_rows, chance - onehot, 0.0) * (1.0 - label_cap * label_cap)
    ).astype(jnp.bfloat16)
    grad_final = jnp.dot(grad_logit, label_table, preferred_element_type=jnp.float32)
    scaled_final = grad_final * final_gain
    cube_out = scale_out * scale_out * scale_out
    grad_mixed = scale_out * scaled_final - mixed_rows * cube_out * jnp.mean(
        scaled_final * mixed_rows, axis=-1, keepdims=True
    )
    scaled_post = grad_mixed * post_gain
    cube_attn = scale_attn * scale_attn * scale_attn
    grad_attention = scale_attn * scaled_post - attention * cube_attn * jnp.mean(
        scaled_post * attention, axis=-1, keepdims=True
    )
    grad_context = times_transposed(grad_attention.astype(jnp.bfloat16), w_out).astype(jnp.bfloat16)
    grad_four = grad_context.reshape(tok_rows, local_kv, group_size, HD).transpose(1, 2, 0, 3)
    grad_prob = jnp.einsum(
        "kgid,kjd->kgij", grad_four, values_own, preferred_element_type=jnp.float32
    )
    grad_score = (
        soft_weights
        * (grad_prob - jnp.sum(soft_weights * grad_prob, axis=-1, keepdims=True))
        * (1.0 - capped * capped)
    )
    score_round = grad_score.astype(jnp.bfloat16)
    grad_query = jnp.einsum(
        "kgij,kjd->kgid", score_round, keys_own, preferred_element_type=jnp.float32
    ).reshape(local_heads, tok_rows, HD)
    grad_queries = rotate_back(grad_query * QUERY_SCALE, cos_table, sin_table).astype(jnp.bfloat16)
    grad_key = jnp.einsum(
        "kgij,kgid->kjd", score_round, query_four, preferred_element_type=jnp.float32
    )
    grad_value = jnp.einsum("kgij,kgid->kjd", attend, grad_four, preferred_element_type=jnp.float32)
    grad_keys = rotate_back(grad_key, cos_table, sin_table).astype(jnp.bfloat16)
    grad_values = grad_value.astype(jnp.bfloat16)
    query_rows = grad_queries.transpose(1, 0, 2).reshape(tok_rows, local_heads * HD)
    key_rows = grad_keys.transpose(1, 0, 2).reshape(tok_rows, local_kv * HD)
    value_rows = grad_values.transpose(1, 0, 2).reshape(tok_rows, local_kv * HD)
    grad_part = (
        jnp.dot(query_rows, w_query_t, preferred_element_type=jnp.float32)
        + jnp.dot(key_rows, w_key_t, preferred_element_type=jnp.float32)
        + jnp.dot(value_rows, w_value_t, preferred_element_type=jnp.float32)
    )
    cube_in = scale_in * scale_in * scale_in
    grad_normed = pair_sum(grad_part.astype(jnp.bfloat16))
    scaled_in = grad_normed * pre_gain
    row_stat = jnp.mean(scaled_in * inputs, axis=-1, keepdims=True)
    grad_full = scale_in * scaled_in - inputs * cube_in * row_stat + grad_mixed
    grad_full = permute_blocks(grad_full, slot_of, n_seq)
    grad_rows = lax.dynamic_slice_in_dim(grad_full, core_rank * half_width, half_width, 1)
    return lax.all_to_all(
        grad_rows.astype(jnp.bfloat16), "seq", split_axis=0, concat_axis=0, tiled=True
    )


def solution(mesh):
    return jax.shard_map(
        functools.partial(shards, mesh.shape["seq"]),
        mesh=mesh,
        in_specs=(
            P(("groups", "seq"), "wg"),
            P(),
            P("seq", "wg"),
            P("seq", "wg"),
            P("seq", "wg"),
            P("wg", "seq"),
            P(),
            P(),
            P(),
            P("groups"),
            P("groups"),
        ),
        out_specs=P(("groups", "seq"), "wg"),
        check_vma=False,
    )
```

```python
import functools

import jax
import jax.numpy as jnp
from jax import lax
from jax.sharding import PartitionSpec as P

HD = 128
LABELS = 64


PIECEWISE_RING = 16
EPSILON = 1e-06
ATTEND_CAP = 50.0
LABEL_CAP = 30.0
QUERY_SCALE = 1.0 / 12.0


def rope_tables(positions, head_width):
    frequency = 10000.0 ** (-2.0 * jnp.arange(head_width // 2, dtype=jnp.float32) / head_width)
    angles = positions.astype(jnp.float32)[:, None] * frequency[None, :]
    return (jnp.cos(angles), jnp.sin(angles))


def rotate(values, cos_table, sin_table):
    half_width = values.shape[-1] // 2
    lower_part = values[..., :half_width]
    upper_part = values[..., half_width:]
    return jnp.concatenate(
        [
            lower_part * cos_table - upper_part * sin_table,
            upper_part * cos_table + lower_part * sin_table,
        ],
        axis=-1,
    )


def rotate_back(values, cos_table, sin_table):
    half_width = values.shape[-1] // 2
    lower_part = values[..., :half_width]
    upper_part = values[..., half_width:]
    return jnp.concatenate(
        [
            lower_part * cos_table + upper_part * sin_table,
            upper_part * cos_table - lower_part * sin_table,
        ],
        axis=-1,
    )


def times_transposed(left_side, right_side):
    return lax.dot_general(
        left_side, right_side, (((1,), (1,)), ((), ())), preferred_element_type=jnp.float32
    )


def pair_sum(rounded_part):
    other = lax.ppermute(rounded_part, "wg", perm=[(0, 1), (1, 0)])
    return rounded_part.astype(jnp.float32) + other.astype(jnp.float32)


def ring_order(n):
    if n % 2:
        return list(range(n))
    return list(range(0, n, 2)) + list(range(n - 1, 0, -2))


def ring_gather(front, back, seq_rank, group_rank, n):
    order = ring_order(n)
    position = [0] * n
    for place, member in enumerate(order):
        position[member] = place
    forward_pairs = [(order[p], order[(p + 1) % n]) for p in range(n)]
    backward_pairs = [(order[p], order[(p - 1) % n]) for p in range(n)]
    group_pairs = [(0, 1), (1, 0)]
    place = jnp.array(position, dtype=jnp.int32)[seq_rank]
    steps = jnp.arange(n, dtype=jnp.int32)
    block_of = jnp.array(order, dtype=jnp.int32)[(place - steps) % n]
    slot_of = (place - jnp.array(position, dtype=jnp.int32)) % n
    first_group = group_rank == 0

    def thirds(values):
        width = values.shape[1] // 3
        return [values[:, i * width:(i + 1) * width] for i in range(3)]

    def carried(values):
        left, middle, right = thirds(values)
        return jnp.stack([jnp.where(first_group, left, right), middle])

    front_ring = [carried(front)]
    back_ring = [carried(back)]
    for step in range(1, n):
        front_ring.append(lax.ppermute(front_ring[-1], "seq", forward_pairs))
        back_ring.append(lax.ppermute(back_ring[-1], "seq", backward_pairs))
    front_pieces = [front]
    back_pieces = [back]
    for step in range(1, n):
        handed = lax.ppermute(
            jnp.stack([front_ring[step][0], back_ring[step][0]]), "groups", group_pairs
        )
        for ring, pieces, other in ((front_ring, front_pieces, handed[0]), (back_ring, back_pieces, handed[1])):
            own, middle = ring[step][0], ring[step][1]
            pieces.append(
                jnp.concatenate(
                    [jnp.where(first_group, own, other), middle, jnp.where(first_group, other, own)],
                    axis=1,
                )
            )
    if n <= PIECEWISE_RING:
        for step in range(n - 1):
            front_pieces[step], back_pieces[step], _, _ = lax.optimization_barrier(
                (front_pieces[step], back_pieces[step], front_ring[step + 1], back_ring[step + 1])
            )
    back_pieces = [back_pieces[(n - k) % n] for k in range(n)]
    return front_pieces, back_pieces, block_of, slot_of


def permute_blocks(values, block_order, n):
    lead = values.shape[:-1]
    width = values.shape[-1] // n
    blocks = values.reshape(lead + (n, width))
    return jnp.take(blocks, block_order, axis=-2).reshape(values.shape)


def shards(
    n_seq,
    generator_rows,
    pre_gain,
    query_weight,
    key_weight,
    value_weight,
    out_weight,
    post_gain,
    final_gain,
    label_table,
    lengths,
    label_index,
):
    seq_rank = lax.axis_index("seq")
    core_rank = lax.axis_index("wg")
    whole_rows = lax.all_gather(generator_rows, "wg", axis=1, tiled=True)
    guard_rows = lax.all_to_all(whole_rows, "seq", split_axis=0, concat_axis=0, tiled=True)
    q_cols = query_weight.shape[1]
    k_cols = key_weight.shape[1]
    front = jnp.concatenate([query_weight, key_weight], axis=1)
    back = jnp.concatenate([value_weight, out_weight.T], axis=1)
    front_pieces, back_pieces, block_of, slot_of = ring_gather(
        front, back, seq_rank, lax.axis_index("groups"), n_seq
    )
    guard_rows = permute_blocks(guard_rows, block_of, n_seq)
    pre_gain = permute_blocks(pre_gain, block_of, n_seq)
    post_gain = permute_blocks(post_gain, block_of, n_seq)
    final_gain = permute_blocks(final_gain, block_of, n_seq)
    label_table = permute_blocks(label_table, block_of, n_seq)
    piecewise = n_seq <= PIECEWISE_RING
    if piecewise:
        w_query_t = jnp.concatenate([piece[:, :q_cols].T for piece in front_pieces], axis=1)
        w_key_t = jnp.concatenate([piece[:, q_cols:].T for piece in front_pieces], axis=1)
        w_value_t = jnp.concatenate([piece[:, :k_cols].T for piece in back_pieces], axis=1)
        w_out = jnp.concatenate([piece[:, k_cols:].T for piece in back_pieces], axis=1)
    else:
        front_all = jnp.concatenate(front_pieces, axis=0)
        back_all = jnp.concatenate(back_pieces, axis=0)
        w_query_t = front_all[:, :q_cols].T
        w_key_t = front_all[:, q_cols:].T
        w_value_t = back_all[:, :k_cols].T
        w_out = back_all[:, k_cols:].T
    tok_rows = guard_rows.shape[0]
    half_width = generator_rows.shape[1]
    local_heads = q_cols // HD
    local_kv = k_cols // HD
    group_size = local_heads // local_kv
    length = lax.dynamic_index_in_dim(lengths, seq_rank, 0, keepdims=False)
    target = lax.dynamic_index_in_dim(label_index, seq_rank, 0, keepdims=False)
    offsets = jnp.arange(tok_rows, dtype=jnp.int32)
    cos_table, sin_table = rope_tables(offsets, HD)
    inputs = guard_rows.astype(jnp.float32)
    scale_in = lax.rsqrt(jnp.mean(inputs * inputs, axis=-1, keepdims=True) + EPSILON)
    normed = (inputs * scale_in * pre_gain).astype(jnp.bfloat16)
    if piecewise:
        block_rows = front_pieces[0].shape[0]
        front_proj = None
        back_proj = None
        for index, (front_piece, back_piece) in enumerate(zip(front_pieces, back_pieces)):
            normed_block = normed[:, index * block_rows:(index + 1) * block_rows]
            front_term = jnp.dot(normed_block, front_piece, preferred_element_type=jnp.float32)
            back_term = jnp.dot(normed_block, back_piece[:, :k_cols], preferred_element_type=jnp.float32)
            front_proj = front_term if front_proj is None else front_proj + front_term
            back_proj = back_term if back_proj is None else back_proj + back_term
    else:
        front_proj = jnp.dot(normed, front_all, preferred_element_type=jnp.float32)
        back_proj = jnp.dot(normed, back_all[:, :k_cols], preferred_element_type=jnp.float32)
    query_proj = front_proj[:, :q_cols].reshape(tok_rows, local_heads, HD).transpose(1, 0, 2)
    queries = (rotate(query_proj, cos_table, sin_table) * QUERY_SCALE).astype(jnp.bfloat16)
    key_proj = front_proj[:, q_cols:].reshape(tok_rows, local_kv, HD).transpose(1, 0, 2)
    keys_own = rotate(key_proj, cos_table, sin_table).astype(jnp.bfloat16)
    values_own = (
        back_proj
        .astype(jnp.bfloat16)
        .reshape(tok_rows, local_kv, HD)
        .transpose(1, 0, 2)
    )
    allowed = (offsets[None, :] <= offsets[:, None]) & (offsets[None, :] < length)
    query_four = queries.reshape(local_kv, group_size, tok_rows, HD)
    raw_scores = jnp.einsum(
        "kgid,kjd->kgij", query_four, keys_own, preferred_element_type=jnp.float32
    )
    capped = jnp.tanh(raw_scores / ATTEND_CAP)
    weight_exp = jnp.where(allowed[None, None], jnp.exp(ATTEND_CAP * capped), 0.0)
    soft_weights = weight_exp / jnp.sum(weight_exp, axis=-1, keepdims=True)
    attend = soft_weights.astype(jnp.bfloat16)
    context = jnp.einsum(
        "kgij,kjd->kgid", attend, values_own, preferred_element_type=jnp.float32
    ).astype(jnp.bfloat16)
    context_rows = (
        context.reshape(local_heads, tok_rows, HD)
        .transpose(1, 0, 2)
        .reshape(tok_rows, local_heads * HD)
    )
    out_part = jnp.dot(context_rows, w_out, preferred_element_type=jnp.float32)
    attention = pair_sum(out_part.astype(jnp.bfloat16))
    scale_attn = lax.rsqrt(jnp.mean(attention * attention, axis=-1, keepdims=True) + EPSILON)
    mixed_rows = inputs + attention * scale_attn * post_gain
    scale_out = lax.rsqrt(jnp.mean(mixed_rows * mixed_rows, axis=-1, keepdims=True) + EPSILON)
    final_rows = (mixed_rows * scale_out * final_gain).astype(jnp.bfloat16)
    logits = times_transposed(final_rows, label_table)
    label_cap = jnp.tanh(logits / LABEL_CAP)
    label_exp = jnp.exp(LABEL_CAP * label_cap)
    chance = label_exp / jnp.sum(label_exp, axis=-1, keepdims=True)
    live_rows = (offsets < length)[:, None]
    onehot = (jnp.arange(LABELS, dtype=jnp.int32) == target).astype(jnp.float32)[None, :]
    grad_logit = (
        jnp.where(live_rows, chance - onehot, 0.0) * (1.0 - label_cap * label_cap)
    ).astype(jnp.bfloat16)
    grad_final = jnp.dot(grad_logit, label_table, preferred_element_type=jnp.float32)
    scaled_final = grad_final * final_gain
    cube_out = scale_out * scale_out * scale_out
    grad_mixed = scale_out * scaled_final - mixed_rows * cube_out * jnp.mean(
        scaled_final * mixed_rows, axis=-1, keepdims=True
    )
    scaled_post = grad_mixed * post_gain
    cube_attn = scale_attn * scale_attn * scale_attn
    grad_attention = scale_attn * scaled_post - attention * cube_attn * jnp.mean(
        scaled_post * attention, axis=-1, keepdims=True
    )
    grad_context = times_transposed(grad_attention.astype(jnp.bfloat16), w_out).astype(jnp.bfloat16)
    grad_four = grad_context.reshape(tok_rows, local_kv, group_size, HD).transpose(1, 2, 0, 3)
    grad_prob = jnp.einsum(
        "kgid,kjd->kgij", grad_four, values_own, preferred_element_type=jnp.float32
    )
    grad_score = (
        soft_weights
        * (grad_prob - jnp.sum(soft_weights * grad_prob, axis=-1, keepdims=True))
        * (1.0 - capped * capped)
    )
    score_round = grad_score.astype(jnp.bfloat16)
    grad_query = jnp.einsum(
        "kgij,kjd->kgid", score_round, keys_own, preferred_element_type=jnp.float32
    ).reshape(local_heads, tok_rows, HD)
    grad_queries = rotate_back(grad_query * QUERY_SCALE, cos_table, sin_table).astype(jnp.bfloat16)
    grad_key = jnp.einsum(
        "kgij,kgid->kjd", score_round, query_four, preferred_element_type=jnp.float32
    )
    grad_value = jnp.einsum("kgij,kgid->kjd", attend, grad_four, preferred_element_type=jnp.float32)
    grad_keys = rotate_back(grad_key, cos_table, sin_table).astype(jnp.bfloat16)
    grad_values = grad_value.astype(jnp.bfloat16)
    query_rows = grad_queries.transpose(1, 0, 2).reshape(tok_rows, local_heads * HD)
    key_rows = grad_keys.transpose(1, 0, 2).reshape(tok_rows, local_kv * HD)
    value_rows = grad_values.transpose(1, 0, 2).reshape(tok_rows, local_kv * HD)
    grad_part = (
        jnp.dot(query_rows, w_query_t, preferred_element_type=jnp.float32)
        + jnp.dot(key_rows, w_key_t, preferred_element_type=jnp.float32)
        + jnp.dot(value_rows, w_value_t, preferred_element_type=jnp.float32)
    )
    cube_in = scale_in * scale_in * scale_in
    grad_normed = pair_sum(grad_part.astype(jnp.bfloat16))
    scaled_in = grad_normed * pre_gain
    row_stat = jnp.mean(scaled_in * inputs, axis=-1, keepdims=True)
    grad_full = scale_in * scaled_in - inputs * cube_in * row_stat + grad_mixed
    grad_full = permute_blocks(grad_full, slot_of, n_seq)
    grad_rows = lax.dynamic_slice_in_dim(grad_full, core_rank * half_width, half_width, 1)
    return lax.all_to_all(
        grad_rows.astype(jnp.bfloat16), "seq", split_axis=0, concat_axis=0, tiled=True
    )


def solution(mesh):
    return jax.shard_map(
        functools.partial(shards, mesh.shape["seq"]),
        mesh=mesh,
        in_specs=(
            P(("groups", "seq"), "wg"),
            P(),
            P("seq", "wg"),
            P("seq", "wg"),
            P("seq", "wg"),
            P("wg", "seq"),
            P(),
            P(),
            P(),
            P("groups"),
            P("groups"),
        ),
        out_specs=P(("groups", "seq"), "wg"),
        check_vma=False,
    )
```

```python
import functools

import jax
import jax.numpy as jnp
from jax import lax
from jax.sharding import PartitionSpec as P

HD = 128
LABELS = 64


PIECEWISE_RING = 16
EPSILON = 1e-06
ATTEND_CAP = 50.0
LABEL_CAP = 30.0
QUERY_SCALE = 1.0 / 12.0


def rope_tables(positions, head_width):
    frequency = 10000.0 ** (-2.0 * jnp.arange(head_width // 2, dtype=jnp.float32) / head_width)
    angles = positions.astype(jnp.float32)[:, None] * frequency[None, :]
    return (jnp.cos(angles), jnp.sin(angles))


def rotate(values, cos_table, sin_table):
    half_width = values.shape[-1] // 2
    lower_part = values[..., :half_width]
    upper_part = values[..., half_width:]
    return jnp.concatenate(
        [
            lower_part * cos_table - upper_part * sin_table,
            upper_part * cos_table + lower_part * sin_table,
        ],
        axis=-1,
    )


def rotate_back(values, cos_table, sin_table):
    half_width = values.shape[-1] // 2
    lower_part = values[..., :half_width]
    upper_part = values[..., half_width:]
    return jnp.concatenate(
        [
            lower_part * cos_table + upper_part * sin_table,
            upper_part * cos_table - lower_part * sin_table,
        ],
        axis=-1,
    )


def times_transposed(left_side, right_side):
    return lax.dot_general(
        left_side, right_side, (((1,), (1,)), ((), ())), preferred_element_type=jnp.float32
    )


def pair_sum(rounded_part):
    other = lax.ppermute(rounded_part, "wg", perm=[(0, 1), (1, 0)])
    return rounded_part.astype(jnp.float32) + other.astype(jnp.float32)


def ring_order(n):
    if n % 2:
        return list(range(n))
    return list(range(0, n, 2)) + list(range(n - 1, 0, -2))


def ring_gather(front, back, seq_rank, group_rank, n):
    order = ring_order(n)
    position = [0] * n
    for place, member in enumerate(order):
        position[member] = place
    forward_pairs = [(order[p], order[(p + 1) % n]) for p in range(n)]
    backward_pairs = [(order[p], order[(p - 1) % n]) for p in range(n)]
    group_pairs = [(0, 1), (1, 0)]
    place = jnp.array(position, dtype=jnp.int32)[seq_rank]
    steps = jnp.arange(n, dtype=jnp.int32)
    block_of = jnp.array(order, dtype=jnp.int32)[(place - steps) % n]
    slot_of = (place - jnp.array(position, dtype=jnp.int32)) % n
    first_group = group_rank == 0

    def thirds(values):
        width = values.shape[1] // 3
        return [values[:, i * width:(i + 1) * width] for i in range(3)]

    def carried(values):
        left, middle, right = thirds(values)
        return jnp.stack([jnp.where(first_group, left, right), middle])

    front_ring = [carried(front)]
    back_ring = [carried(back)]
    for step in range(1, n):
        front_ring.append(lax.ppermute(front_ring[-1], "seq", forward_pairs))
        back_ring.append(lax.ppermute(back_ring[-1], "seq", backward_pairs))
    front_pieces = [front]
    back_pieces = [back]
    for step in range(1, n):
        handed = lax.ppermute(
            jnp.stack([front_ring[step][0], back_ring[step][0]]), "groups", group_pairs
        )
        for ring, pieces, other in ((front_ring, front_pieces, handed[0]), (back_ring, back_pieces, handed[1])):
            own, middle = ring[step][0], ring[step][1]
            pieces.append(
                jnp.concatenate(
                    [jnp.where(first_group, own, other), middle, jnp.where(first_group, other, own)],
                    axis=1,
                )
            )
    if n <= PIECEWISE_RING:
        for step in range(n - 1):
            front_pieces[step], back_pieces[step], _, _ = lax.optimization_barrier(
                (front_pieces[step], back_pieces[step], front_ring[step + 1], back_ring[step + 1])
            )
    back_pieces = [back_pieces[(n - k) % n] for k in range(n)]
    return front_pieces, back_pieces, block_of, slot_of


def permute_blocks(values, block_order, n):
    lead = values.shape[:-1]
    width = values.shape[-1] // n
    blocks = values.reshape(lead + (n, width))
    return jnp.take(blocks, block_order, axis=-2).reshape(values.shape)


def shards(
    n_seq,
    generator_rows,
    pre_gain,
    query_weight,
    key_weight,
    value_weight,
    out_weight,
    post_gain,
    final_gain,
    label_table,
    lengths,
    label_index,
):
    seq_rank = lax.axis_index("seq")
    core_rank = lax.axis_index("wg")
    guard_half = lax.all_to_all(generator_rows, "seq", split_axis=0, concat_axis=0, tiled=True)
    guard_rows = lax.all_gather(guard_half, "wg", axis=1, tiled=True)
    q_cols = query_weight.shape[1]
    k_cols = key_weight.shape[1]
    front = jnp.concatenate([query_weight, key_weight], axis=1)
    back = jnp.concatenate([value_weight, out_weight.T], axis=1)
    front_pieces, back_pieces, block_of, slot_of = ring_gather(
        front, back, seq_rank, lax.axis_index("groups"), n_seq
    )
    guard_rows = permute_blocks(guard_rows, block_of, n_seq)
    pre_gain = permute_blocks(pre_gain, block_of, n_seq)
    post_gain = permute_blocks(post_gain, block_of, n_seq)
    final_gain = permute_blocks(final_gain, block_of, n_seq)
    label_table = permute_blocks(label_table, block_of, n_seq)
    piecewise = n_seq <= PIECEWISE_RING
    if piecewise:
        w_query_t = jnp.concatenate([piece[:, :q_cols].T for piece in front_pieces], axis=1)
        w_key_t = jnp.concatenate([piece[:, q_cols:].T for piece in front_pieces], axis=1)
        w_value_t = jnp.concatenate([piece[:, :k_cols].T for piece in back_pieces], axis=1)
        w_out = jnp.concatenate([piece[:, k_cols:].T for piece in back_pieces], axis=1)
    else:
        front_all = jnp.concatenate(front_pieces, axis=0)
        back_all = jnp.concatenate(back_pieces, axis=0)
        w_query_t = front_all[:, :q_cols].T
        w_key_t = front_all[:, q_cols:].T
        w_value_t = back_all[:, :k_cols].T
        w_out = back_all[:, k_cols:].T
    tok_rows = guard_rows.shape[0]
    half_width = generator_rows.shape[1]
    local_heads = q_cols // HD
    local_kv = k_cols // HD
    group_size = local_heads // local_kv
    length = lax.dynamic_index_in_dim(lengths, seq_rank, 0, keepdims=False)
    target = lax.dynamic_index_in_dim(label_index, seq_rank, 0, keepdims=False)
    offsets = jnp.arange(tok_rows, dtype=jnp.int32)
    cos_table, sin_table = rope_tables(offsets, HD)
    inputs = guard_rows.astype(jnp.float32)
    scale_in = lax.rsqrt(jnp.mean(inputs * inputs, axis=-1, keepdims=True) + EPSILON)
    normed = (inputs * scale_in * pre_gain).astype(jnp.bfloat16)
    if piecewise:
        block_rows = front_pieces[0].shape[0]
        front_proj = None
        back_proj = None
        for index, (front_piece, back_piece) in enumerate(zip(front_pieces, back_pieces)):
            normed_block = normed[:, index * block_rows:(index + 1) * block_rows]
            front_term = jnp.dot(normed_block, front_piece, preferred_element_type=jnp.float32)
            back_term = jnp.dot(normed_block, back_piece[:, :k_cols], preferred_element_type=jnp.float32)
            front_proj = front_term if front_proj is None else front_proj + front_term
            back_proj = back_term if back_proj is None else back_proj + back_term
    else:
        front_proj = jnp.dot(normed, front_all, preferred_element_type=jnp.float32)
        back_proj = jnp.dot(normed, back_all[:, :k_cols], preferred_element_type=jnp.float32)
    query_proj = front_proj[:, :q_cols].reshape(tok_rows, local_heads, HD).transpose(1, 0, 2)
    queries = (rotate(query_proj, cos_table, sin_table) * QUERY_SCALE).astype(jnp.bfloat16)
    key_proj = front_proj[:, q_cols:].reshape(tok_rows, local_kv, HD).transpose(1, 0, 2)
    keys_own = rotate(key_proj, cos_table, sin_table).astype(jnp.bfloat16)
    values_own = (
        back_proj
        .astype(jnp.bfloat16)
        .reshape(tok_rows, local_kv, HD)
        .transpose(1, 0, 2)
    )
    allowed = (offsets[None, :] <= offsets[:, None]) & (offsets[None, :] < length)
    query_four = queries.reshape(local_kv, group_size, tok_rows, HD)
    raw_scores = jnp.einsum(
        "kgid,kjd->kgij", query_four, keys_own, preferred_element_type=jnp.float32
    )
    capped = jnp.tanh(raw_scores / ATTEND_CAP)
    weight_exp = jnp.where(allowed[None, None], jnp.exp(ATTEND_CAP * capped), 0.0)
    soft_weights = weight_exp / jnp.sum(weight_exp, axis=-1, keepdims=True)
    attend = soft_weights.astype(jnp.bfloat16)
    context = jnp.einsum(
        "kgij,kjd->kgid", attend, values_own, preferred_element_type=jnp.float32
    ).astype(jnp.bfloat16)
    context_rows = (
        context.reshape(local_heads, tok_rows, HD)
        .transpose(1, 0, 2)
        .reshape(tok_rows, local_heads * HD)
    )
    out_part = jnp.dot(context_rows, w_out, preferred_element_type=jnp.float32)
    attention = pair_sum(out_part.astype(jnp.bfloat16))
    scale_attn = lax.rsqrt(jnp.mean(attention * attention, axis=-1, keepdims=True) + EPSILON)
    mixed_rows = inputs + attention * scale_attn * post_gain
    scale_out = lax.rsqrt(jnp.mean(mixed_rows * mixed_rows, axis=-1, keepdims=True) + EPSILON)
    final_rows = (mixed_rows * scale_out * final_gain).astype(jnp.bfloat16)
    logits = times_transposed(final_rows, label_table)
    label_cap = jnp.tanh(logits / LABEL_CAP)
    label_exp = jnp.exp(LABEL_CAP * label_cap)
    chance = label_exp / jnp.sum(label_exp, axis=-1, keepdims=True)
    live_rows = (offsets < length)[:, None]
    onehot = (jnp.arange(LABELS, dtype=jnp.int32) == target).astype(jnp.float32)[None, :]
    grad_logit = (
        jnp.where(live_rows, chance - onehot, 0.0) * (1.0 - label_cap * label_cap)
    ).astype(jnp.bfloat16)
    grad_final = jnp.dot(grad_logit, label_table, preferred_element_type=jnp.float32)
    scaled_final = grad_final * final_gain
    cube_out = scale_out * scale_out * scale_out
    grad_mixed = scale_out * scaled_final - mixed_rows * cube_out * jnp.mean(
        scaled_final * mixed_rows, axis=-1, keepdims=True
    )
    scaled_post = grad_mixed * post_gain
    cube_attn = scale_attn * scale_attn * scale_attn
    grad_attention = scale_attn * scaled_post - attention * cube_attn * jnp.mean(
        scaled_post * attention, axis=-1, keepdims=True
    )
    grad_context = times_transposed(grad_attention.astype(jnp.bfloat16), w_out).astype(jnp.bfloat16)
    grad_four = grad_context.reshape(tok_rows, local_kv, group_size, HD).transpose(1, 2, 0, 3)
    grad_prob = jnp.einsum(
        "kgid,kjd->kgij", grad_four, values_own, preferred_element_type=jnp.float32
    )
    grad_score = (
        soft_weights
        * (grad_prob - jnp.sum(soft_weights * grad_prob, axis=-1, keepdims=True))
        * (1.0 - capped * capped)
    )
    score_round = grad_score.astype(jnp.bfloat16)
    grad_query = jnp.einsum(
        "kgij,kjd->kgid", score_round, keys_own, preferred_element_type=jnp.float32
    ).reshape(local_heads, tok_rows, HD)
    grad_queries = rotate_back(grad_query * QUERY_SCALE, cos_table, sin_table).astype(jnp.bfloat16)
    grad_key = jnp.einsum(
        "kgij,kgid->kjd", score_round, query_four, preferred_element_type=jnp.float32
    )
    grad_value = jnp.einsum("kgij,kgid->kjd", attend, grad_four, preferred_element_type=jnp.float32)
    grad_keys = rotate_back(grad_key, cos_table, sin_table).astype(jnp.bfloat16)
    grad_values = grad_value.astype(jnp.bfloat16)
    query_rows = grad_queries.transpose(1, 0, 2).reshape(tok_rows, local_heads * HD)
    key_rows = grad_keys.transpose(1, 0, 2).reshape(tok_rows, local_kv * HD)
    value_rows = grad_values.transpose(1, 0, 2).reshape(tok_rows, local_kv * HD)
    grad_part = (
        jnp.dot(query_rows, w_query_t, preferred_element_type=jnp.float32)
        + jnp.dot(key_rows, w_key_t, preferred_element_type=jnp.float32)
        + jnp.dot(value_rows, w_value_t, preferred_element_type=jnp.float32)
    )
    cube_in = scale_in * scale_in * scale_in
    grad_normed = pair_sum(grad_part.astype(jnp.bfloat16))
    scaled_in = grad_normed * pre_gain
    row_stat = jnp.mean(scaled_in * inputs, axis=-1, keepdims=True)
    grad_full = scale_in * scaled_in - inputs * cube_in * row_stat + grad_mixed
    grad_full = permute_blocks(grad_full, slot_of, n_seq)
    grad_rows = lax.dynamic_slice_in_dim(grad_full, core_rank * half_width, half_width, 1)
    return lax.all_to_all(
        grad_rows.astype(jnp.bfloat16), "seq", split_axis=0, concat_axis=0, tiled=True
    )


def solution(mesh):
    return jax.shard_map(
        functools.partial(shards, mesh.shape["seq"]),
        mesh=mesh,
        in_specs=(
            P(("groups", "seq"), "wg"),
            P(),
            P("seq", "wg"),
            P("seq", "wg"),
            P("seq", "wg"),
            P("wg", "seq"),
            P(),
            P(),
            P(),
            P("groups"),
            P("groups"),
        ),
        out_specs=P(("groups", "seq"), "wg"),
        check_vma=False,
    )
```

```python
import functools

import jax
import jax.numpy as jnp
from jax import lax
from jax.sharding import PartitionSpec as P

HD = 128
LABELS = 64


PIECEWISE_RING = 16
EPSILON = 1e-06
ATTEND_CAP = 50.0
LABEL_CAP = 30.0
QUERY_SCALE = 1.0 / 12.0


def rope_tables(positions, head_width):
    frequency = 10000.0 ** (-2.0 * jnp.arange(head_width // 2, dtype=jnp.float32) / head_width)
    angles = positions.astype(jnp.float32)[:, None] * frequency[None, :]
    return (jnp.cos(angles), jnp.sin(angles))


def rotate(values, cos_table, sin_table):
    half_width = values.shape[-1] // 2
    lower_part = values[..., :half_width]
    upper_part = values[..., half_width:]
    return jnp.concatenate(
        [
            lower_part * cos_table - upper_part * sin_table,
            upper_part * cos_table + lower_part * sin_table,
        ],
        axis=-1,
    )


def rotate_back(values, cos_table, sin_table):
    half_width = values.shape[-1] // 2
    lower_part = values[..., :half_width]
    upper_part = values[..., half_width:]
    return jnp.concatenate(
        [
            lower_part * cos_table + upper_part * sin_table,
            upper_part * cos_table - lower_part * sin_table,
        ],
        axis=-1,
    )


def times_transposed(left_side, right_side):
    return lax.dot_general(
        left_side, right_side, (((1,), (1,)), ((), ())), preferred_element_type=jnp.float32
    )


def pair_sum(rounded_part):
    other = lax.ppermute(rounded_part, "wg", perm=[(0, 1), (1, 0)])
    return rounded_part.astype(jnp.float32) + other.astype(jnp.float32)


def ring_order(n):
    if n % 2:
        return list(range(n))
    return list(range(0, n, 2)) + list(range(n - 1, 0, -2))


def ring_gather(front, back, seq_rank, group_rank, n):
    order = ring_order(n)
    position = [0] * n
    for place, member in enumerate(order):
        position[member] = place
    forward_pairs = [(order[p], order[(p + 1) % n]) for p in range(n)]
    backward_pairs = [(order[p], order[(p - 1) % n]) for p in range(n)]
    group_pairs = [(0, 1), (1, 0)]
    place = jnp.array(position, dtype=jnp.int32)[seq_rank]
    steps = jnp.arange(n, dtype=jnp.int32)
    block_of = jnp.array(order, dtype=jnp.int32)[(place - steps) % n]
    slot_of = (place - jnp.array(position, dtype=jnp.int32)) % n
    first_group = group_rank == 0

    def thirds(values):
        width = values.shape[1] // 3
        return [values[:, i * width:(i + 1) * width] for i in range(3)]

    def carried(values):
        left, middle, right = thirds(values)
        return jnp.stack([jnp.where(first_group, left, right), middle])

    front_ring = [carried(front)]
    back_ring = [carried(back)]
    for step in range(1, n):
        front_ring.append(lax.ppermute(front_ring[-1], "seq", forward_pairs))
        back_ring.append(lax.ppermute(back_ring[-1], "seq", backward_pairs))
    front_pieces = [front]
    back_pieces = [back]
    for step in range(1, n):
        handed = lax.ppermute(
            jnp.stack([front_ring[step][0], back_ring[step][0]]), "groups", group_pairs
        )
        for ring, pieces, other in ((front_ring, front_pieces, handed[0]), (back_ring, back_pieces, handed[1])):
            own, middle = ring[step][0], ring[step][1]
            pieces.append(
                jnp.concatenate(
                    [jnp.where(first_group, own, other), middle, jnp.where(first_group, other, own)],
                    axis=1,
                )
            )
    if n <= PIECEWISE_RING:
        for step in range(n - 1):
            front_pieces[step], back_pieces[step], _, _ = lax.optimization_barrier(
                (front_pieces[step], back_pieces[step], front_ring[step + 1], back_ring[step + 1])
            )
    back_pieces = [back_pieces[(n - k) % n] for k in range(n)]
    return front_pieces, back_pieces, block_of, slot_of, front_ring[1]


def permute_blocks(values, block_order, n):
    lead = values.shape[:-1]
    width = values.shape[-1] // n
    blocks = values.reshape(lead + (n, width))
    return jnp.take(blocks, block_order, axis=-2).reshape(values.shape)


def shards(
    n_seq,
    generator_rows,
    pre_gain,
    query_weight,
    key_weight,
    value_weight,
    out_weight,
    post_gain,
    final_gain,
    label_table,
    lengths,
    label_index,
):
    seq_rank = lax.axis_index("seq")
    core_rank = lax.axis_index("wg")
    q_cols = query_weight.shape[1]
    k_cols = key_weight.shape[1]
    front = jnp.concatenate([query_weight, key_weight], axis=1)
    back = jnp.concatenate([value_weight, out_weight.T], axis=1)
    front_pieces, back_pieces, block_of, slot_of, first_arrival = ring_gather(
        front, back, seq_rank, lax.axis_index("groups"), n_seq
    )
    generator_rows, pre_gain, post_gain, final_gain, label_table, lengths, label_index, _ = lax.optimization_barrier(
        (generator_rows, pre_gain, post_gain, final_gain, label_table, lengths, label_index, first_arrival)
    )
    guard_half = lax.all_to_all(generator_rows, "seq", split_axis=0, concat_axis=0, tiled=True)
    guard_rows = lax.all_gather(guard_half, "wg", axis=1, tiled=True)
    guard_rows = permute_blocks(guard_rows, block_of, n_seq)
    pre_gain = permute_blocks(pre_gain, block_of, n_seq)
    post_gain = permute_blocks(post_gain, block_of, n_seq)
    final_gain = permute_blocks(final_gain, block_of, n_seq)
    label_table = permute_blocks(label_table, block_of, n_seq)
    piecewise = n_seq <= PIECEWISE_RING
    if piecewise:
        w_query_t = jnp.concatenate([piece[:, :q_cols].T for piece in front_pieces], axis=1)
        w_key_t = jnp.concatenate([piece[:, q_cols:].T for piece in front_pieces], axis=1)
        w_value_t = jnp.concatenate([piece[:, :k_cols].T for piece in back_pieces], axis=1)
        w_out = jnp.concatenate([piece[:, k_cols:].T for piece in back_pieces], axis=1)
    else:
        front_all = jnp.concatenate(front_pieces, axis=0)
        back_all = jnp.concatenate(back_pieces, axis=0)
        w_query_t = front_all[:, :q_cols].T
        w_key_t = front_all[:, q_cols:].T
        w_value_t = back_all[:, :k_cols].T
        w_out = back_all[:, k_cols:].T
    tok_rows = guard_rows.shape[0]
    half_width = generator_rows.shape[1]
    local_heads = q_cols // HD
    local_kv = k_cols // HD
    group_size = local_heads // local_kv
    length = lax.dynamic_index_in_dim(lengths, seq_rank, 0, keepdims=False)
    target = lax.dynamic_index_in_dim(label_index, seq_rank, 0, keepdims=False)
    offsets = jnp.arange(tok_rows, dtype=jnp.int32)
    cos_table, sin_table = rope_tables(offsets, HD)
    inputs = guard_rows.astype(jnp.float32)
    scale_in = lax.rsqrt(jnp.mean(inputs * inputs, axis=-1, keepdims=True) + EPSILON)
    normed = (inputs * scale_in * pre_gain).astype(jnp.bfloat16)
    if piecewise:
        block_rows = front_pieces[0].shape[0]
        front_proj = None
        back_proj = None
        for index, (front_piece, back_piece) in enumerate(zip(front_pieces, back_pieces)):
            normed_block = normed[:, index * block_rows:(index + 1) * block_rows]
            front_term = jnp.dot(normed_block, front_piece, preferred_element_type=jnp.float32)
            back_term = jnp.dot(normed_block, back_piece[:, :k_cols], preferred_element_type=jnp.float32)
            front_proj = front_term if front_proj is None else front_proj + front_term
            back_proj = back_term if back_proj is None else back_proj + back_term
    else:
        front_proj = jnp.dot(normed, front_all, preferred_element_type=jnp.float32)
        back_proj = jnp.dot(normed, back_all[:, :k_cols], preferred_element_type=jnp.float32)
    query_proj = front_proj[:, :q_cols].reshape(tok_rows, local_heads, HD).transpose(1, 0, 2)
    queries = (rotate(query_proj, cos_table, sin_table) * QUERY_SCALE).astype(jnp.bfloat16)
    key_proj = front_proj[:, q_cols:].reshape(tok_rows, local_kv, HD).transpose(1, 0, 2)
    keys_own = rotate(key_proj, cos_table, sin_table).astype(jnp.bfloat16)
    values_own = (
        back_proj
        .astype(jnp.bfloat16)
        .reshape(tok_rows, local_kv, HD)
        .transpose(1, 0, 2)
    )
    allowed = (offsets[None, :] <= offsets[:, None]) & (offsets[None, :] < length)
    query_four = queries.reshape(local_kv, group_size, tok_rows, HD)
    raw_scores = jnp.einsum(
        "kgid,kjd->kgij", query_four, keys_own, preferred_element_type=jnp.float32
    )
    capped = jnp.tanh(raw_scores / ATTEND_CAP)
    weight_exp = jnp.where(allowed[None, None], jnp.exp(ATTEND_CAP * capped), 0.0)
    soft_weights = weight_exp / jnp.sum(weight_exp, axis=-1, keepdims=True)
    attend = soft_weights.astype(jnp.bfloat16)
    context = jnp.einsum(
        "kgij,kjd->kgid", attend, values_own, preferred_element_type=jnp.float32
    ).astype(jnp.bfloat16)
    context_rows = (
        context.reshape(local_heads, tok_rows, HD)
        .transpose(1, 0, 2)
        .reshape(tok_rows, local_heads * HD)
    )
    out_part = jnp.dot(context_rows, w_out, preferred_element_type=jnp.float32)
    attention = pair_sum(out_part.astype(jnp.bfloat16))
    scale_attn = lax.rsqrt(jnp.mean(attention * attention, axis=-1, keepdims=True) + EPSILON)
    mixed_rows = inputs + attention * scale_attn * post_gain
    scale_out = lax.rsqrt(jnp.mean(mixed_rows * mixed_rows, axis=-1, keepdims=True) + EPSILON)
    final_rows = (mixed_rows * scale_out * final_gain).astype(jnp.bfloat16)
    logits = times_transposed(final_rows, label_table)
    label_cap = jnp.tanh(logits / LABEL_CAP)
    label_exp = jnp.exp(LABEL_CAP * label_cap)
    chance = label_exp / jnp.sum(label_exp, axis=-1, keepdims=True)
    live_rows = (offsets < length)[:, None]
    onehot = (jnp.arange(LABELS, dtype=jnp.int32) == target).astype(jnp.float32)[None, :]
    grad_logit = (
        jnp.where(live_rows, chance - onehot, 0.0) * (1.0 - label_cap * label_cap)
    ).astype(jnp.bfloat16)
    grad_final = jnp.dot(grad_logit, label_table, preferred_element_type=jnp.float32)
    scaled_final = grad_final * final_gain
    cube_out = scale_out * scale_out * scale_out
    grad_mixed = scale_out * scaled_final - mixed_rows * cube_out * jnp.mean(
        scaled_final * mixed_rows, axis=-1, keepdims=True
    )
    scaled_post = grad_mixed * post_gain
    cube_attn = scale_attn * scale_attn * scale_attn
    grad_attention = scale_attn * scaled_post - attention * cube_attn * jnp.mean(
        scaled_post * attention, axis=-1, keepdims=True
    )
    grad_context = times_transposed(grad_attention.astype(jnp.bfloat16), w_out).astype(jnp.bfloat16)
    grad_four = grad_context.reshape(tok_rows, local_kv, group_size, HD).transpose(1, 2, 0, 3)
    grad_prob = jnp.einsum(
        "kgid,kjd->kgij", grad_four, values_own, preferred_element_type=jnp.float32
    )
    grad_score = (
        soft_weights
        * (grad_prob - jnp.sum(soft_weights * grad_prob, axis=-1, keepdims=True))
        * (1.0 - capped * capped)
    )
    score_round = grad_score.astype(jnp.bfloat16)
    grad_query = jnp.einsum(
        "kgij,kjd->kgid", score_round, keys_own, preferred_element_type=jnp.float32
    ).reshape(local_heads, tok_rows, HD)
    grad_queries = rotate_back(grad_query * QUERY_SCALE, cos_table, sin_table).astype(jnp.bfloat16)
    grad_key = jnp.einsum(
        "kgij,kgid->kjd", score_round, query_four, preferred_element_type=jnp.float32
    )
    grad_value = jnp.einsum("kgij,kgid->kjd", attend, grad_four, preferred_element_type=jnp.float32)
    grad_keys = rotate_back(grad_key, cos_table, sin_table).astype(jnp.bfloat16)
    grad_values = grad_value.astype(jnp.bfloat16)
    query_rows = grad_queries.transpose(1, 0, 2).reshape(tok_rows, local_heads * HD)
    key_rows = grad_keys.transpose(1, 0, 2).reshape(tok_rows, local_kv * HD)
    value_rows = grad_values.transpose(1, 0, 2).reshape(tok_rows, local_kv * HD)
    grad_part = (
        jnp.dot(query_rows, w_query_t, preferred_element_type=jnp.float32)
        + jnp.dot(key_rows, w_key_t, preferred_element_type=jnp.float32)
        + jnp.dot(value_rows, w_value_t, preferred_element_type=jnp.float32)
    )
    cube_in = scale_in * scale_in * scale_in
    grad_normed = pair_sum(grad_part.astype(jnp.bfloat16))
    scaled_in = grad_normed * pre_gain
    row_stat = jnp.mean(scaled_in * inputs, axis=-1, keepdims=True)
    grad_full = scale_in * scaled_in - inputs * cube_in * row_stat + grad_mixed
    grad_full = permute_blocks(grad_full, slot_of, n_seq)
    grad_rows = lax.dynamic_slice_in_dim(grad_full, core_rank * half_width, half_width, 1)
    return lax.all_to_all(
        grad_rows.astype(jnp.bfloat16), "seq", split_axis=0, concat_axis=0, tiled=True
    )


def solution(mesh):
    return jax.shard_map(
        functools.partial(shards, mesh.shape["seq"]),
        mesh=mesh,
        in_specs=(
            P(("groups", "seq"), "wg"),
            P(),
            P("seq", "wg"),
            P("seq", "wg"),
            P("seq", "wg"),
            P("wg", "seq"),
            P(),
            P(),
            P(),
            P("groups"),
            P("groups"),
        ),
        out_specs=P(("groups", "seq"), "wg"),
        check_vma=False,
    )
```

```python
import functools

import jax
import jax.numpy as jnp
from jax import lax
from jax.sharding import PartitionSpec as P

HD = 128
LABELS = 64


PIECEWISE_RING = 16
EPSILON = 1e-06
ATTEND_CAP = 50.0
LABEL_CAP = 30.0
QUERY_SCALE = 1.0 / 12.0


def rope_tables(positions, head_width):
    frequency = 10000.0 ** (-2.0 * jnp.arange(head_width // 2, dtype=jnp.float32) / head_width)
    angles = positions.astype(jnp.float32)[:, None] * frequency[None, :]
    return (jnp.cos(angles), jnp.sin(angles))


def rotate(values, cos_table, sin_table):
    half_width = values.shape[-1] // 2
    lower_part = values[..., :half_width]
    upper_part = values[..., half_width:]
    return jnp.concatenate(
        [
            lower_part * cos_table - upper_part * sin_table,
            upper_part * cos_table + lower_part * sin_table,
        ],
        axis=-1,
    )


def rotate_back(values, cos_table, sin_table):
    half_width = values.shape[-1] // 2
    lower_part = values[..., :half_width]
    upper_part = values[..., half_width:]
    return jnp.concatenate(
        [
            lower_part * cos_table + upper_part * sin_table,
            upper_part * cos_table - lower_part * sin_table,
        ],
        axis=-1,
    )


def times_transposed(left_side, right_side):
    return lax.dot_general(
        left_side, right_side, (((1,), (1,)), ((), ())), preferred_element_type=jnp.float32
    )


def pair_sum(rounded_part):
    other = lax.ppermute(rounded_part, "wg", perm=[(0, 1), (1, 0)])
    return rounded_part.astype(jnp.float32) + other.astype(jnp.float32)


def ring_order(n):
    if n % 2:
        return list(range(n))
    return list(range(0, n, 2)) + list(range(n - 1, 0, -2))


def ring_member(place, n):
    if n % 2:
        return place
    return jnp.where(place < n // 2, 2 * place, 2 * (n - 1 - place) + 1)


def ring_position(member, n):
    if n % 2:
        return member
    return jnp.where(member % 2 == 0, member // 2, n - 1 - member // 2)


def ring_gather(front, back, seq_rank, group_rank, n):
    order = ring_order(n)
    position = [0] * n
    for place, member in enumerate(order):
        position[member] = place
    forward_pairs = [(order[p], order[(p + 1) % n]) for p in range(n)]
    backward_pairs = [(order[p], order[(p - 1) % n]) for p in range(n)]
    group_pairs = [(0, 1), (1, 0)]
    place = ring_position(seq_rank, n)
    steps = jnp.arange(n, dtype=jnp.int32)
    block_of = ring_member((place - steps) % n, n)
    slot_of = (place - ring_position(steps, n)) % n
    first_group = group_rank == 0

    def thirds(values):
        width = values.shape[1] // 3
        return [values[:, i * width:(i + 1) * width] for i in range(3)]

    def carried(values):
        left, middle, right = thirds(values)
        return jnp.stack([jnp.where(first_group, left, right), middle])

    front_ring = [carried(front)]
    back_ring = [carried(back)]
    for step in range(1, n):
        front_ring.append(lax.ppermute(front_ring[-1], "seq", forward_pairs))
        back_ring.append(lax.ppermute(back_ring[-1], "seq", backward_pairs))
    front_pieces = [front]
    back_pieces = [back]
    for step in range(1, n):
        handed = lax.ppermute(
            jnp.stack([front_ring[step][0], back_ring[step][0]]), "groups", group_pairs
        )
        for ring, pieces, other in ((front_ring, front_pieces, handed[0]), (back_ring, back_pieces, handed[1])):
            own, middle = ring[step][0], ring[step][1]
            pieces.append(
                jnp.concatenate(
                    [jnp.where(first_group, own, other), middle, jnp.where(first_group, other, own)],
                    axis=1,
                )
            )
    if n <= PIECEWISE_RING:
        for step in range(n - 1):
            front_pieces[step], back_pieces[step], _, _ = lax.optimization_barrier(
                (front_pieces[step], back_pieces[step], front_ring[step + 1], back_ring[step + 1])
            )
    back_pieces = [back_pieces[(n - k) % n] for k in range(n)]
    return front_pieces, back_pieces, block_of, slot_of


def permute_blocks(values, block_order, n):
    lead = values.shape[:-1]
    width = values.shape[-1] // n
    blocks = values.reshape(lead + (n, width))
    return jnp.take(blocks, block_order, axis=-2).reshape(values.shape)


def shards(
    n_seq,
    generator_rows,
    pre_gain,
    query_weight,
    key_weight,
    value_weight,
    out_weight,
    post_gain,
    final_gain,
    label_table,
    lengths,
    label_index,
):
    seq_rank = lax.axis_index("seq")
    core_rank = lax.axis_index("wg")
    guard_half = lax.all_to_all(generator_rows, "seq", split_axis=0, concat_axis=0, tiled=True)
    guard_rows = lax.all_gather(guard_half, "wg", axis=1, tiled=True)
    q_cols = query_weight.shape[1]
    k_cols = key_weight.shape[1]
    front = jnp.concatenate([query_weight, key_weight], axis=1)
    back = jnp.concatenate([value_weight, out_weight.T], axis=1)
    front_pieces, back_pieces, block_of, slot_of = ring_gather(
        front, back, seq_rank, lax.axis_index("groups"), n_seq
    )
    guard_rows = permute_blocks(guard_rows, block_of, n_seq)
    pre_gain, post_gain, final_gain = permute_blocks(
        jnp.stack([pre_gain, post_gain, final_gain]), block_of, n_seq
    )
    label_table = permute_blocks(label_table, block_of, n_seq)
    piecewise = n_seq <= PIECEWISE_RING
    if piecewise:
        w_query_t = jnp.concatenate([piece[:, :q_cols].T for piece in front_pieces], axis=1)
        w_key_t = jnp.concatenate([piece[:, q_cols:].T for piece in front_pieces], axis=1)
        w_value_t = jnp.concatenate([piece[:, :k_cols].T for piece in back_pieces], axis=1)
        w_out = jnp.concatenate([piece[:, k_cols:].T for piece in back_pieces], axis=1)
    else:
        front_all = jnp.concatenate(front_pieces, axis=0)
        back_all = jnp.concatenate(back_pieces, axis=0)
        w_query_t = front_all[:, :q_cols].T
        w_key_t = front_all[:, q_cols:].T
        w_value_t = back_all[:, :k_cols].T
        w_out = back_all[:, k_cols:].T
    tok_rows = guard_rows.shape[0]
    half_width = generator_rows.shape[1]
    local_heads = q_cols // HD
    local_kv = k_cols // HD
    group_size = local_heads // local_kv
    length = lax.dynamic_index_in_dim(lengths, seq_rank, 0, keepdims=False)
    target = lax.dynamic_index_in_dim(label_index, seq_rank, 0, keepdims=False)
    offsets = jnp.arange(tok_rows, dtype=jnp.int32)
    cos_table, sin_table = rope_tables(offsets, HD)
    inputs = guard_rows.astype(jnp.float32)
    scale_in = lax.rsqrt(jnp.mean(inputs * inputs, axis=-1, keepdims=True) + EPSILON)
    normed = (inputs * scale_in * pre_gain).astype(jnp.bfloat16)
    if piecewise:
        block_rows = front_pieces[0].shape[0]
        front_proj = None
        back_proj = None
        for index, (front_piece, back_piece) in enumerate(zip(front_pieces, back_pieces)):
            normed_block = normed[:, index * block_rows:(index + 1) * block_rows]
            front_term = jnp.dot(normed_block, front_piece, preferred_element_type=jnp.float32)
            back_term = jnp.dot(normed_block, back_piece[:, :k_cols], preferred_element_type=jnp.float32)
            front_proj = front_term if front_proj is None else front_proj + front_term
            back_proj = back_term if back_proj is None else back_proj + back_term
    else:
        front_proj = jnp.dot(normed, front_all, preferred_element_type=jnp.float32)
        back_proj = jnp.dot(normed, back_all[:, :k_cols], preferred_element_type=jnp.float32)
    query_proj = front_proj[:, :q_cols].reshape(tok_rows, local_heads, HD).transpose(1, 0, 2)
    queries = (rotate(query_proj, cos_table, sin_table) * QUERY_SCALE).astype(jnp.bfloat16)
    key_proj = front_proj[:, q_cols:].reshape(tok_rows, local_kv, HD).transpose(1, 0, 2)
    keys_own = rotate(key_proj, cos_table, sin_table).astype(jnp.bfloat16)
    values_own = (
        back_proj
        .astype(jnp.bfloat16)
        .reshape(tok_rows, local_kv, HD)
        .transpose(1, 0, 2)
    )
    allowed = (offsets[None, :] <= offsets[:, None]) & (offsets[None, :] < length)
    query_four = queries.reshape(local_kv, group_size, tok_rows, HD)
    raw_scores = jnp.einsum(
        "kgid,kjd->kgij", query_four, keys_own, preferred_element_type=jnp.float32
    )
    capped = jnp.tanh(raw_scores / ATTEND_CAP)
    weight_exp = jnp.where(allowed[None, None], jnp.exp(ATTEND_CAP * capped), 0.0)
    soft_weights = weight_exp / jnp.sum(weight_exp, axis=-1, keepdims=True)
    attend = soft_weights.astype(jnp.bfloat16)
    context = jnp.einsum(
        "kgij,kjd->kgid", attend, values_own, preferred_element_type=jnp.float32
    ).astype(jnp.bfloat16)
    context_rows = (
        context.reshape(local_heads, tok_rows, HD)
        .transpose(1, 0, 2)
        .reshape(tok_rows, local_heads * HD)
    )
    out_part = jnp.dot(context_rows, w_out, preferred_element_type=jnp.float32)
    attention = pair_sum(out_part.astype(jnp.bfloat16))
    scale_attn = lax.rsqrt(jnp.mean(attention * attention, axis=-1, keepdims=True) + EPSILON)
    mixed_rows = inputs + attention * scale_attn * post_gain
    scale_out = lax.rsqrt(jnp.mean(mixed_rows * mixed_rows, axis=-1, keepdims=True) + EPSILON)
    final_rows = (mixed_rows * scale_out * final_gain).astype(jnp.bfloat16)
    logits = times_transposed(final_rows, label_table)
    label_cap = jnp.tanh(logits / LABEL_CAP)
    label_exp = jnp.exp(LABEL_CAP * label_cap)
    chance = label_exp / jnp.sum(label_exp, axis=-1, keepdims=True)
    live_rows = (offsets < length)[:, None]
    onehot = (jnp.arange(LABELS, dtype=jnp.int32) == target).astype(jnp.float32)[None, :]
    grad_logit = (
        jnp.where(live_rows, chance - onehot, 0.0) * (1.0 - label_cap * label_cap)
    ).astype(jnp.bfloat16)
    grad_final = jnp.dot(grad_logit, label_table, preferred_element_type=jnp.float32)
    scaled_final = grad_final * final_gain
    cube_out = scale_out * scale_out * scale_out
    grad_mixed = scale_out * scaled_final - mixed_rows * cube_out * jnp.mean(
        scaled_final * mixed_rows, axis=-1, keepdims=True
    )
    scaled_post = grad_mixed * post_gain
    cube_attn = scale_attn * scale_attn * scale_attn
    grad_attention = scale_attn * scaled_post - attention * cube_attn * jnp.mean(
        scaled_post * attention, axis=-1, keepdims=True
    )
    grad_context = times_transposed(grad_attention.astype(jnp.bfloat16), w_out).astype(jnp.bfloat16)
    grad_four = grad_context.reshape(tok_rows, local_kv, group_size, HD).transpose(1, 2, 0, 3)
    grad_prob = jnp.einsum(
        "kgid,kjd->kgij", grad_four, values_own, preferred_element_type=jnp.float32
    )
    grad_score = (
        soft_weights
        * (grad_prob - jnp.sum(soft_weights * grad_prob, axis=-1, keepdims=True))
        * (1.0 - capped * capped)
    )
    score_round = grad_score.astype(jnp.bfloat16)
    grad_query = jnp.einsum(
        "kgij,kjd->kgid", score_round, keys_own, preferred_element_type=jnp.float32
    ).reshape(local_heads, tok_rows, HD)
    grad_queries = rotate_back(grad_query * QUERY_SCALE, cos_table, sin_table).astype(jnp.bfloat16)
    grad_key = jnp.einsum(
        "kgij,kgid->kjd", score_round, query_four, preferred_element_type=jnp.float32
    )
    grad_value = jnp.einsum("kgij,kgid->kjd", attend, grad_four, preferred_element_type=jnp.float32)
    grad_keys = rotate_back(grad_key, cos_table, sin_table).astype(jnp.bfloat16)
    grad_values = grad_value.astype(jnp.bfloat16)
    query_rows = grad_queries.transpose(1, 0, 2).reshape(tok_rows, local_heads * HD)
    key_rows = grad_keys.transpose(1, 0, 2).reshape(tok_rows, local_kv * HD)
    value_rows = grad_values.transpose(1, 0, 2).reshape(tok_rows, local_kv * HD)
    grad_part = (
        jnp.dot(query_rows, w_query_t, preferred_element_type=jnp.float32)
        + jnp.dot(key_rows, w_key_t, preferred_element_type=jnp.float32)
        + jnp.dot(value_rows, w_value_t, preferred_element_type=jnp.float32)
    )
    cube_in = scale_in * scale_in * scale_in
    grad_normed = pair_sum(grad_part.astype(jnp.bfloat16))
    scaled_in = grad_normed * pre_gain
    row_stat = jnp.mean(scaled_in * inputs, axis=-1, keepdims=True)
    grad_full = scale_in * scaled_in - inputs * cube_in * row_stat + grad_mixed
    grad_full = permute_blocks(grad_full, slot_of, n_seq)
    grad_rows = lax.dynamic_slice_in_dim(grad_full, core_rank * half_width, half_width, 1)
    return lax.all_to_all(
        grad_rows.astype(jnp.bfloat16), "seq", split_axis=0, concat_axis=0, tiled=True
    )


def solution(mesh):
    return jax.shard_map(
        functools.partial(shards, mesh.shape["seq"]),
        mesh=mesh,
        in_specs=(
            P(("groups", "seq"), "wg"),
            P(),
            P("seq", "wg"),
            P("seq", "wg"),
            P("seq", "wg"),
            P("wg", "seq"),
            P(),
            P(),
            P(),
            P("groups"),
            P("groups"),
        ),
        out_specs=P(("groups", "seq"), "wg"),
        check_vma=False,
    )
```

```python
import functools

import jax
import jax.numpy as jnp
from jax import lax
from jax.sharding import PartitionSpec as P

HD = 128
LABELS = 64


PIECEWISE_RING = 16
EPSILON = 1e-06
ATTEND_CAP = 50.0
LABEL_CAP = 30.0
QUERY_SCALE = 1.0 / 12.0


def rope_tables(positions, head_width):
    frequency = 10000.0 ** (-2.0 * jnp.arange(head_width // 2, dtype=jnp.float32) / head_width)
    angles = positions.astype(jnp.float32)[:, None] * frequency[None, :]
    return (jnp.cos(angles), jnp.sin(angles))


def rotate(values, cos_table, sin_table):
    half_width = values.shape[-1] // 2
    lower_part = values[..., :half_width]
    upper_part = values[..., half_width:]
    return jnp.concatenate(
        [
            lower_part * cos_table - upper_part * sin_table,
            upper_part * cos_table + lower_part * sin_table,
        ],
        axis=-1,
    )


def rotate_back(values, cos_table, sin_table):
    half_width = values.shape[-1] // 2
    lower_part = values[..., :half_width]
    upper_part = values[..., half_width:]
    return jnp.concatenate(
        [
            lower_part * cos_table + upper_part * sin_table,
            upper_part * cos_table - lower_part * sin_table,
        ],
        axis=-1,
    )


def times_transposed(left_side, right_side):
    return lax.dot_general(
        left_side, right_side, (((1,), (1,)), ((), ())), preferred_element_type=jnp.float32
    )


def pair_sum(rounded_part):
    other = lax.ppermute(rounded_part, "wg", perm=[(0, 1), (1, 0)])
    return rounded_part.astype(jnp.float32) + other.astype(jnp.float32)


def ring_order(n):
    if n % 2:
        return list(range(n))
    return list(range(0, n, 2)) + list(range(n - 1, 0, -2))


def ring_member(place, n):
    if n % 2:
        return place
    return jnp.where(place < n // 2, 2 * place, 2 * (n - 1 - place) + 1)


def ring_position(member, n):
    if n % 2:
        return member
    return jnp.where(member % 2 == 0, member // 2, n - 1 - member // 2)


def ring_gather(front, back, seq_rank, group_rank, n):
    order = ring_order(n)
    position = [0] * n
    for place, member in enumerate(order):
        position[member] = place
    forward_pairs = [(order[p], order[(p + 1) % n]) for p in range(n)]
    backward_pairs = [(order[p], order[(p - 1) % n]) for p in range(n)]
    group_pairs = [(0, 1), (1, 0)]
    place = ring_position(seq_rank, n)
    steps = jnp.arange(n, dtype=jnp.int32)
    block_of = ring_member((place - steps) % n, n)
    slot_of = (place - ring_position(steps, n)) % n
    first_group = group_rank == 0

    def thirds(values):
        width = values.shape[1] // 3
        return [values[:, i * width:(i + 1) * width] for i in range(3)]

    def carried(values):
        left, middle, right = thirds(values)
        return jnp.stack([jnp.where(first_group, left, right), middle])

    front_ring = [carried(front)]
    back_ring = [carried(back)]
    for step in range(1, n):
        front_ring.append(lax.ppermute(front_ring[-1], "seq", forward_pairs))
        back_ring.append(lax.ppermute(back_ring[-1], "seq", backward_pairs))
    front_pieces = [front]
    back_pieces = [back]
    for step in range(1, n):
        handed = lax.ppermute(
            jnp.stack([front_ring[step][0], back_ring[step][0]]), "groups", group_pairs
        )
        for ring, pieces, other in ((front_ring, front_pieces, handed[0]), (back_ring, back_pieces, handed[1])):
            own, middle = ring[step][0], ring[step][1]
            pieces.append(
                jnp.concatenate(
                    [jnp.where(first_group, own, other), middle, jnp.where(first_group, other, own)],
                    axis=1,
                )
            )
    if n <= PIECEWISE_RING:
        for step in range(n - 1):
            front_pieces[step], back_pieces[step], _, _ = lax.optimization_barrier(
                (front_pieces[step], back_pieces[step], front_ring[step + 1], back_ring[step + 1])
            )
    back_pieces = [back_pieces[(n - k) % n] for k in range(n)]
    return front_pieces, back_pieces, block_of, slot_of


def permute_blocks(values, block_order, n):
    lead = values.shape[:-1]
    width = values.shape[-1] // n
    blocks = values.reshape(lead + (n, width))
    return jnp.take(blocks, block_order, axis=-2).reshape(values.shape)


def shards(
    n_seq,
    generator_rows,
    pre_gain,
    query_weight,
    key_weight,
    value_weight,
    out_weight,
    post_gain,
    final_gain,
    label_table,
    lengths,
    label_index,
):
    seq_rank = lax.axis_index("seq")
    core_rank = lax.axis_index("wg")
    guard_half = lax.all_to_all(generator_rows, "seq", split_axis=0, concat_axis=0, tiled=True)
    guard_rows = lax.all_gather(guard_half, "wg", axis=1, tiled=True)
    q_cols = query_weight.shape[1]
    k_cols = key_weight.shape[1]
    front = jnp.concatenate([query_weight, key_weight], axis=1)
    back = jnp.concatenate([value_weight, out_weight.T], axis=1)
    front_pieces, back_pieces, block_of, slot_of = ring_gather(
        front, back, seq_rank, lax.axis_index("groups"), n_seq
    )
    guard_rows = permute_blocks(guard_rows, block_of, n_seq)
    pre_gain, post_gain, final_gain = permute_blocks(
        jnp.stack([pre_gain, post_gain, final_gain]), block_of, n_seq
    )
    label_table = permute_blocks(label_table, block_of, n_seq)
    piecewise = n_seq <= PIECEWISE_RING
    if piecewise:
        w_query_t = jnp.concatenate([piece[:, :q_cols].T for piece in front_pieces], axis=1)
        w_key_t = jnp.concatenate([piece[:, q_cols:].T for piece in front_pieces], axis=1)
        w_value_t = jnp.concatenate([piece[:, :k_cols].T for piece in back_pieces], axis=1)
        w_out = jnp.concatenate([piece[:, k_cols:].T for piece in back_pieces], axis=1)
    else:
        front_all = jnp.concatenate(front_pieces, axis=0)
        back_all = jnp.concatenate(back_pieces, axis=0)
        w_query_t = front_all[:, :q_cols].T
        w_key_t = front_all[:, q_cols:].T
        w_value_t = back_all[:, :k_cols].T
        w_out = back_all[:, k_cols:].T
    tok_rows = guard_rows.shape[0]
    half_width = generator_rows.shape[1]
    local_heads = q_cols // HD
    local_kv = k_cols // HD
    group_size = local_heads // local_kv
    length = lax.dynamic_index_in_dim(lengths, seq_rank, 0, keepdims=False)
    target = lax.dynamic_index_in_dim(label_index, seq_rank, 0, keepdims=False)
    offsets = jnp.arange(tok_rows, dtype=jnp.int32)
    cos_table, sin_table = rope_tables(offsets, HD)
    inputs = guard_rows.astype(jnp.float32)
    scale_in = lax.rsqrt(jnp.mean(inputs * inputs, axis=-1, keepdims=True) + EPSILON)
    normed = (inputs * scale_in * pre_gain).astype(jnp.bfloat16)
    if piecewise:
        block_rows = front_pieces[0].shape[0]
        front_proj = None
        back_proj = None
        for index, (front_piece, back_piece) in enumerate(zip(front_pieces, back_pieces)):
            normed_block = normed[:, index * block_rows:(index + 1) * block_rows]
            front_term = jnp.dot(normed_block, front_piece, preferred_element_type=jnp.float32)
            back_term = jnp.dot(normed_block, back_piece[:, :k_cols], preferred_element_type=jnp.float32)
            front_proj = front_term if front_proj is None else front_proj + front_term
            back_proj = back_term if back_proj is None else back_proj + back_term
    else:
        front_proj = jnp.dot(normed, front_all, preferred_element_type=jnp.float32)
        back_proj = jnp.dot(normed, back_all[:, :k_cols], preferred_element_type=jnp.float32)
    query_proj = front_proj[:, :q_cols].reshape(tok_rows, local_heads, HD).transpose(1, 0, 2)
    queries = (rotate(query_proj, cos_table, sin_table) * QUERY_SCALE).astype(jnp.bfloat16)
    key_proj = front_proj[:, q_cols:].reshape(tok_rows, local_kv, HD).transpose(1, 0, 2)
    keys_own = rotate(key_proj, cos_table, sin_table).astype(jnp.bfloat16)
    values_own = (
        back_proj
        .astype(jnp.bfloat16)
        .reshape(tok_rows, local_kv, HD)
        .transpose(1, 0, 2)
    )
    allowed = (offsets[None, :] <= offsets[:, None]) & (offsets[None, :] < length)
    query_four = queries.reshape(local_kv, group_size, tok_rows, HD)
    raw_scores = jnp.einsum(
        "kgid,kjd->kgij", query_four, keys_own, preferred_element_type=jnp.float32
    )
    capped = jnp.tanh(raw_scores / ATTEND_CAP)
    weight_exp = jnp.where(allowed[None, None], jnp.exp(ATTEND_CAP * capped), 0.0)
    soft_weights = weight_exp / jnp.sum(weight_exp, axis=-1, keepdims=True)
    attend = soft_weights.astype(jnp.bfloat16)
    context = jnp.einsum(
        "kgij,kjd->kgid", attend, values_own, preferred_element_type=jnp.float32
    ).astype(jnp.bfloat16)
    context_rows = (
        context.reshape(local_heads, tok_rows, HD)
        .transpose(1, 0, 2)
        .reshape(tok_rows, local_heads * HD)
    )
    out_part = jnp.dot(context_rows, w_out, preferred_element_type=jnp.float32)
    attention = pair_sum(out_part.astype(jnp.bfloat16))
    scale_attn = lax.rsqrt(jnp.mean(attention * attention, axis=-1, keepdims=True) + EPSILON)
    mixed_rows = inputs + attention * scale_attn * post_gain
    scale_out = lax.rsqrt(jnp.mean(mixed_rows * mixed_rows, axis=-1, keepdims=True) + EPSILON)
    final_rows = (mixed_rows * scale_out * final_gain).astype(jnp.bfloat16)
    logits = times_transposed(final_rows, label_table)
    label_cap = jnp.tanh(logits / LABEL_CAP)
    label_exp = jnp.exp(LABEL_CAP * label_cap)
    chance = label_exp / jnp.sum(label_exp, axis=-1, keepdims=True)
    live_rows = (offsets < length)[:, None]
    onehot = (jnp.arange(LABELS, dtype=jnp.int32) == target).astype(jnp.float32)[None, :]
    grad_logit = (
        jnp.where(live_rows, chance - onehot, 0.0) * (1.0 - label_cap * label_cap)
    ).astype(jnp.bfloat16)
    grad_final = jnp.dot(grad_logit, label_table, preferred_element_type=jnp.float32)
    scaled_final = grad_final * final_gain
    cube_out = scale_out * scale_out * scale_out
    grad_mixed = scale_out * scaled_final - mixed_rows * cube_out * jnp.mean(
        scaled_final * mixed_rows, axis=-1, keepdims=True
    )
    scaled_post = grad_mixed * post_gain
    cube_attn = scale_attn * scale_attn * scale_attn
    grad_attention = scale_attn * scaled_post - attention * cube_attn * jnp.mean(
        scaled_post * attention, axis=-1, keepdims=True
    )
    grad_context = times_transposed(grad_attention.astype(jnp.bfloat16), w_out).astype(jnp.bfloat16)
    grad_four = grad_context.reshape(tok_rows, local_kv, group_size, HD).transpose(1, 2, 0, 3)
    grad_prob = jnp.einsum(
        "kgid,kjd->kgij", grad_four, values_own, preferred_element_type=jnp.float32
    )
    grad_score = (
        soft_weights
        * (grad_prob - jnp.sum(soft_weights * grad_prob, axis=-1, keepdims=True))
        * (1.0 - capped * capped)
    )
    score_round = grad_score.astype(jnp.bfloat16)
    grad_query = jnp.einsum(
        "kgij,kjd->kgid", score_round, keys_own, preferred_element_type=jnp.float32
    ).reshape(local_heads, tok_rows, HD)
    grad_queries = rotate_back(grad_query * QUERY_SCALE, cos_table, sin_table).astype(jnp.bfloat16)
    grad_key = jnp.einsum(
        "kgij,kgid->kjd", score_round, query_four, preferred_element_type=jnp.float32
    )
    grad_value = jnp.einsum("kgij,kgid->kjd", attend, grad_four, preferred_element_type=jnp.float32)
    grad_keys = rotate_back(grad_key, cos_table, sin_table).astype(jnp.bfloat16)
    grad_values = grad_value.astype(jnp.bfloat16)
    query_rows = grad_queries.transpose(1, 0, 2).reshape(tok_rows, local_heads * HD)
    key_rows = grad_keys.transpose(1, 0, 2).reshape(tok_rows, local_kv * HD)
    value_rows = grad_values.transpose(1, 0, 2).reshape(tok_rows, local_kv * HD)
    grad_part = (
        jnp.dot(query_rows, w_query_t, preferred_element_type=jnp.float32)
        + jnp.dot(key_rows, w_key_t, preferred_element_type=jnp.float32)
        + jnp.dot(value_rows, w_value_t, preferred_element_type=jnp.float32)
    )
    cube_in = scale_in * scale_in * scale_in
    grad_normed = pair_sum(grad_part.astype(jnp.bfloat16))
    scaled_in = grad_normed * pre_gain
    row_stat = jnp.mean(scaled_in * inputs, axis=-1, keepdims=True)
    grad_full = scale_in * scaled_in - inputs * cube_in * row_stat + grad_mixed
    block_width = grad_full.shape[1] // n_seq
    half_blocks = half_width // block_width
    own_blocks = core_rank * half_blocks + jnp.arange(half_blocks, dtype=jnp.int32)
    grad_blocks = grad_full.astype(jnp.bfloat16).reshape(tok_rows, n_seq, block_width)
    grad_rows = jnp.take(grad_blocks, slot_of[own_blocks], axis=1).reshape(tok_rows, half_width)
    return lax.all_to_all(grad_rows, "seq", split_axis=0, concat_axis=0, tiled=True)


def solution(mesh):
    return jax.shard_map(
        functools.partial(shards, mesh.shape["seq"]),
        mesh=mesh,
        in_specs=(
            P(("groups", "seq"), "wg"),
            P(),
            P("seq", "wg"),
            P("seq", "wg"),
            P("seq", "wg"),
            P("wg", "seq"),
            P(),
            P(),
            P(),
            P("groups"),
            P("groups"),
        ),
        out_specs=P(("groups", "seq"), "wg"),
        check_vma=False,
    )
```

```python
import functools

import jax
import jax.numpy as jnp
from jax import lax
from jax.sharding import PartitionSpec as P

HD = 128
LABELS = 64


PIECEWISE_RING = 16
EPSILON = 1e-06
ATTEND_CAP = 50.0
LABEL_CAP = 30.0
QUERY_SCALE = 1.0 / 12.0


def rope_tables(positions, head_width):
    frequency = 10000.0 ** (-2.0 * jnp.arange(head_width // 2, dtype=jnp.float32) / head_width)
    angles = positions.astype(jnp.float32)[:, None] * frequency[None, :]
    return (jnp.cos(angles), jnp.sin(angles))


def rotate(values, cos_table, sin_table):
    half_width = values.shape[-1] // 2
    lower_part = values[..., :half_width]
    upper_part = values[..., half_width:]
    return jnp.concatenate(
        [
            lower_part * cos_table - upper_part * sin_table,
            upper_part * cos_table + lower_part * sin_table,
        ],
        axis=-1,
    )


def rotate_back(values, cos_table, sin_table):
    half_width = values.shape[-1] // 2
    lower_part = values[..., :half_width]
    upper_part = values[..., half_width:]
    return jnp.concatenate(
        [
            lower_part * cos_table + upper_part * sin_table,
            upper_part * cos_table - lower_part * sin_table,
        ],
        axis=-1,
    )


def times_transposed(left_side, right_side):
    return lax.dot_general(
        left_side, right_side, (((1,), (1,)), ((), ())), preferred_element_type=jnp.float32
    )


def pair_sum(rounded_part):
    other = lax.ppermute(rounded_part, "wg", perm=[(0, 1), (1, 0)])
    return rounded_part.astype(jnp.float32) + other.astype(jnp.float32)


def ring_order(n):
    if n % 2:
        return list(range(n))
    return list(range(0, n, 2)) + list(range(n - 1, 0, -2))


def ring_member(place, n):
    if n % 2:
        return place
    return jnp.where(place < n // 2, 2 * place, 2 * (n - 1 - place) + 1)


def ring_position(member, n):
    if n % 2:
        return member
    return jnp.where(member % 2 == 0, member // 2, n - 1 - member // 2)


def ring_gather(front, back, seq_rank, group_rank, n):
    order = ring_order(n)
    position = [0] * n
    for place, member in enumerate(order):
        position[member] = place
    forward_pairs = [(order[p], order[(p + 1) % n]) for p in range(n)]
    backward_pairs = [(order[p], order[(p - 1) % n]) for p in range(n)]
    group_pairs = [(0, 1), (1, 0)]
    place = ring_position(seq_rank, n)
    steps = jnp.arange(n, dtype=jnp.int32)
    block_of = ring_member((place - steps) % n, n)
    slot_of = (place - ring_position(steps, n)) % n
    first_group = group_rank == 0

    def thirds(values):
        width = values.shape[1] // 3
        return [values[:, i * width:(i + 1) * width] for i in range(3)]

    def carried(values):
        left, middle, right = thirds(values)
        return jnp.stack([jnp.where(first_group, left, right), middle])

    front_ring = [carried(front)]
    back_ring = [carried(back)]
    for step in range(1, n):
        front_ring.append(lax.ppermute(front_ring[-1], "seq", forward_pairs))
        back_ring.append(lax.ppermute(back_ring[-1], "seq", backward_pairs))
    front_pieces = [front]
    back_pieces = [back]
    for step in range(1, n):
        handed = lax.ppermute(
            jnp.stack([front_ring[step][0], back_ring[step][0]]), "groups", group_pairs
        )
        for ring, pieces, other in ((front_ring, front_pieces, handed[0]), (back_ring, back_pieces, handed[1])):
            own, middle = ring[step][0], ring[step][1]
            pieces.append(
                jnp.concatenate(
                    [jnp.where(first_group, own, other), middle, jnp.where(first_group, other, own)],
                    axis=1,
                )
            )
    if n <= PIECEWISE_RING:
        for step in range(n - 1):
            front_pieces[step], back_pieces[step], _, _ = lax.optimization_barrier(
                (front_pieces[step], back_pieces[step], front_ring[step + 1], back_ring[step + 1])
            )
    back_pieces = [back_pieces[(n - k) % n] for k in range(n)]
    return front_pieces, back_pieces, block_of, slot_of


def shift_exchange(rows, seq_rank, n):
    blocks = rows.reshape((n, rows.shape[0] // n) + rows.shape[1:])
    received = [blocks[seq_rank]]
    for shift in range(1, n):
        pairs = [(i, (i + shift) % n) for i in range(n)]
        received.append(lax.ppermute(blocks[(seq_rank + shift) % n], "seq", pairs))
    sources = (seq_rank - jnp.arange(n, dtype=jnp.int32)) % n
    return jnp.take(jnp.stack(received), sources, axis=0).reshape(rows.shape)


def permute_blocks(values, block_order, n):
    lead = values.shape[:-1]
    width = values.shape[-1] // n
    blocks = values.reshape(lead + (n, width))
    return jnp.take(blocks, block_order, axis=-2).reshape(values.shape)


def shards(
    n_seq,
    generator_rows,
    pre_gain,
    query_weight,
    key_weight,
    value_weight,
    out_weight,
    post_gain,
    final_gain,
    label_table,
    lengths,
    label_index,
):
    seq_rank = lax.axis_index("seq")
    core_rank = lax.axis_index("wg")
    guard_half = lax.all_to_all(generator_rows, "seq", split_axis=0, concat_axis=0, tiled=True)
    guard_rows = lax.all_gather(guard_half, "wg", axis=1, tiled=True)
    q_cols = query_weight.shape[1]
    k_cols = key_weight.shape[1]
    front = jnp.concatenate([query_weight, key_weight], axis=1)
    back = jnp.concatenate([value_weight, out_weight.T], axis=1)
    front_pieces, back_pieces, block_of, slot_of = ring_gather(
        front, back, seq_rank, lax.axis_index("groups"), n_seq
    )
    guard_rows = permute_blocks(guard_rows, block_of, n_seq)
    pre_gain, post_gain, final_gain = permute_blocks(
        jnp.stack([pre_gain, post_gain, final_gain]), block_of, n_seq
    )
    label_table = permute_blocks(label_table, block_of, n_seq)
    piecewise = n_seq <= PIECEWISE_RING
    if piecewise:
        w_query_t = jnp.concatenate([piece[:, :q_cols].T for piece in front_pieces], axis=1)
        w_key_t = jnp.concatenate([piece[:, q_cols:].T for piece in front_pieces], axis=1)
        w_value_t = jnp.concatenate([piece[:, :k_cols].T for piece in back_pieces], axis=1)
        w_out = jnp.concatenate([piece[:, k_cols:].T for piece in back_pieces], axis=1)
    else:
        front_all = jnp.concatenate(front_pieces, axis=0)
        back_all = jnp.concatenate(back_pieces, axis=0)
        w_query_t = front_all[:, :q_cols].T
        w_key_t = front_all[:, q_cols:].T
        w_value_t = back_all[:, :k_cols].T
        w_out = back_all[:, k_cols:].T
    tok_rows = guard_rows.shape[0]
    half_width = generator_rows.shape[1]
    local_heads = q_cols // HD
    local_kv = k_cols // HD
    group_size = local_heads // local_kv
    length = lax.dynamic_index_in_dim(lengths, seq_rank, 0, keepdims=False)
    target = lax.dynamic_index_in_dim(label_index, seq_rank, 0, keepdims=False)
    offsets = jnp.arange(tok_rows, dtype=jnp.int32)
    cos_table, sin_table = rope_tables(offsets, HD)
    inputs = guard_rows.astype(jnp.float32)
    scale_in = lax.rsqrt(jnp.mean(inputs * inputs, axis=-1, keepdims=True) + EPSILON)
    normed = (inputs * scale_in * pre_gain).astype(jnp.bfloat16)
    if piecewise:
        block_rows = front_pieces[0].shape[0]
        front_proj = None
        back_proj = None
        for index, (front_piece, back_piece) in enumerate(zip(front_pieces, back_pieces)):
            normed_block = normed[:, index * block_rows:(index + 1) * block_rows]
            front_term = jnp.dot(normed_block, front_piece, preferred_element_type=jnp.float32)
            back_term = jnp.dot(normed_block, back_piece[:, :k_cols], preferred_element_type=jnp.float32)
            front_proj = front_term if front_proj is None else front_proj + front_term
            back_proj = back_term if back_proj is None else back_proj + back_term
    else:
        front_proj = jnp.dot(normed, front_all, preferred_element_type=jnp.float32)
        back_proj = jnp.dot(normed, back_all[:, :k_cols], preferred_element_type=jnp.float32)
    query_proj = front_proj[:, :q_cols].reshape(tok_rows, local_heads, HD).transpose(1, 0, 2)
    queries = (rotate(query_proj, cos_table, sin_table) * QUERY_SCALE).astype(jnp.bfloat16)
    key_proj = front_proj[:, q_cols:].reshape(tok_rows, local_kv, HD).transpose(1, 0, 2)
    keys_own = rotate(key_proj, cos_table, sin_table).astype(jnp.bfloat16)
    values_own = (
        back_proj
        .astype(jnp.bfloat16)
        .reshape(tok_rows, local_kv, HD)
        .transpose(1, 0, 2)
    )
    allowed = (offsets[None, :] <= offsets[:, None]) & (offsets[None, :] < length)
    query_four = queries.reshape(local_kv, group_size, tok_rows, HD)
    raw_scores = jnp.einsum(
        "kgid,kjd->kgij", query_four, keys_own, preferred_element_type=jnp.float32
    )
    capped = jnp.tanh(raw_scores / ATTEND_CAP)
    weight_exp = jnp.where(allowed[None, None], jnp.exp(ATTEND_CAP * capped), 0.0)
    soft_weights = weight_exp / jnp.sum(weight_exp, axis=-1, keepdims=True)
    attend = soft_weights.astype(jnp.bfloat16)
    context = jnp.einsum(
        "kgij,kjd->kgid", attend, values_own, preferred_element_type=jnp.float32
    ).astype(jnp.bfloat16)
    context_rows = (
        context.reshape(local_heads, tok_rows, HD)
        .transpose(1, 0, 2)
        .reshape(tok_rows, local_heads * HD)
    )
    out_part = jnp.dot(context_rows, w_out, preferred_element_type=jnp.float32)
    attention = pair_sum(out_part.astype(jnp.bfloat16))
    scale_attn = lax.rsqrt(jnp.mean(attention * attention, axis=-1, keepdims=True) + EPSILON)
    mixed_rows = inputs + attention * scale_attn * post_gain
    scale_out = lax.rsqrt(jnp.mean(mixed_rows * mixed_rows, axis=-1, keepdims=True) + EPSILON)
    final_rows = (mixed_rows * scale_out * final_gain).astype(jnp.bfloat16)
    logits = times_transposed(final_rows, label_table)
    label_cap = jnp.tanh(logits / LABEL_CAP)
    label_exp = jnp.exp(LABEL_CAP * label_cap)
    chance = label_exp / jnp.sum(label_exp, axis=-1, keepdims=True)
    live_rows = (offsets < length)[:, None]
    onehot = (jnp.arange(LABELS, dtype=jnp.int32) == target).astype(jnp.float32)[None, :]
    grad_logit = (
        jnp.where(live_rows, chance - onehot, 0.0) * (1.0 - label_cap * label_cap)
    ).astype(jnp.bfloat16)
    grad_final = jnp.dot(grad_logit, label_table, preferred_element_type=jnp.float32)
    scaled_final = grad_final * final_gain
    cube_out = scale_out * scale_out * scale_out
    grad_mixed = scale_out * scaled_final - mixed_rows * cube_out * jnp.mean(
        scaled_final * mixed_rows, axis=-1, keepdims=True
    )
    scaled_post = grad_mixed * post_gain
    cube_attn = scale_attn * scale_attn * scale_attn
    grad_attention = scale_attn * scaled_post - attention * cube_attn * jnp.mean(
        scaled_post * attention, axis=-1, keepdims=True
    )
    grad_context = times_transposed(grad_attention.astype(jnp.bfloat16), w_out).astype(jnp.bfloat16)
    grad_four = grad_context.reshape(tok_rows, local_kv, group_size, HD).transpose(1, 2, 0, 3)
    grad_prob = jnp.einsum(
        "kgid,kjd->kgij", grad_four, values_own, preferred_element_type=jnp.float32
    )
    grad_score = (
        soft_weights
        * (grad_prob - jnp.sum(soft_weights * grad_prob, axis=-1, keepdims=True))
        * (1.0 - capped * capped)
    )
    score_round = grad_score.astype(jnp.bfloat16)
    grad_query = jnp.einsum(
        "kgij,kjd->kgid", score_round, keys_own, preferred_element_type=jnp.float32
    ).reshape(local_heads, tok_rows, HD)
    grad_queries = rotate_back(grad_query * QUERY_SCALE, cos_table, sin_table).astype(jnp.bfloat16)
    grad_key = jnp.einsum(
        "kgij,kgid->kjd", score_round, query_four, preferred_element_type=jnp.float32
    )
    grad_value = jnp.einsum("kgij,kgid->kjd", attend, grad_four, preferred_element_type=jnp.float32)
    grad_keys = rotate_back(grad_key, cos_table, sin_table).astype(jnp.bfloat16)
    grad_values = grad_value.astype(jnp.bfloat16)
    query_rows = grad_queries.transpose(1, 0, 2).reshape(tok_rows, local_heads * HD)
    key_rows = grad_keys.transpose(1, 0, 2).reshape(tok_rows, local_kv * HD)
    value_rows = grad_values.transpose(1, 0, 2).reshape(tok_rows, local_kv * HD)
    grad_part = (
        jnp.dot(query_rows, w_query_t, preferred_element_type=jnp.float32)
        + jnp.dot(key_rows, w_key_t, preferred_element_type=jnp.float32)
        + jnp.dot(value_rows, w_value_t, preferred_element_type=jnp.float32)
    )
    cube_in = scale_in * scale_in * scale_in
    grad_normed = pair_sum(grad_part.astype(jnp.bfloat16))
    scaled_in = grad_normed * pre_gain
    row_stat = jnp.mean(scaled_in * inputs, axis=-1, keepdims=True)
    grad_full = scale_in * scaled_in - inputs * cube_in * row_stat + grad_mixed
    block_width = grad_full.shape[1] // n_seq
    half_blocks = half_width // block_width
    own_blocks = core_rank * half_blocks + jnp.arange(half_blocks, dtype=jnp.int32)
    grad_blocks = grad_full.astype(jnp.bfloat16).reshape(tok_rows, n_seq, block_width)
    grad_rows = jnp.take(grad_blocks, slot_of[own_blocks], axis=1).reshape(tok_rows, half_width)
    if n_seq > PIECEWISE_RING:
        return lax.all_to_all(grad_rows, "seq", split_axis=0, concat_axis=0, tiled=True)
    return shift_exchange(grad_rows, seq_rank, n_seq)


def solution(mesh):
    return jax.shard_map(
        functools.partial(shards, mesh.shape["seq"]),
        mesh=mesh,
        in_specs=(
            P(("groups", "seq"), "wg"),
            P(),
            P("seq", "wg"),
            P("seq", "wg"),
            P("seq", "wg"),
            P("wg", "seq"),
            P(),
            P(),
            P(),
            P("groups"),
            P("groups"),
        ),
        out_specs=P(("groups", "seq"), "wg"),
        check_vma=False,
    )
```

```python
import functools

import jax
import jax.numpy as jnp
from jax import lax
from jax.sharding import PartitionSpec as P

HD = 128
LABELS = 64


PIECEWISE_RING = 16
EPSILON = 1e-06
ATTEND_CAP = 50.0
LABEL_CAP = 30.0
QUERY_SCALE = 1.0 / 12.0


def rope_tables(positions, head_width):
    frequency = 10000.0 ** (-2.0 * jnp.arange(head_width // 2, dtype=jnp.float32) / head_width)
    angles = positions.astype(jnp.float32)[:, None] * frequency[None, :]
    return (jnp.cos(angles), jnp.sin(angles))


def rotate(values, cos_table, sin_table):
    half_width = values.shape[-1] // 2
    lower_part = values[..., :half_width]
    upper_part = values[..., half_width:]
    return jnp.concatenate(
        [
            lower_part * cos_table - upper_part * sin_table,
            upper_part * cos_table + lower_part * sin_table,
        ],
        axis=-1,
    )


def rotate_back(values, cos_table, sin_table):
    half_width = values.shape[-1] // 2
    lower_part = values[..., :half_width]
    upper_part = values[..., half_width:]
    return jnp.concatenate(
        [
            lower_part * cos_table + upper_part * sin_table,
            upper_part * cos_table - lower_part * sin_table,
        ],
        axis=-1,
    )


def times_transposed(left_side, right_side):
    return lax.dot_general(
        left_side, right_side, (((1,), (1,)), ((), ())), preferred_element_type=jnp.float32
    )


def pair_sum(rounded_part):
    other = lax.ppermute(rounded_part, "wg", perm=[(0, 1), (1, 0)])
    return rounded_part.astype(jnp.float32) + other.astype(jnp.float32)


def ring_order(n):
    if n % 2:
        return list(range(n))
    return list(range(0, n, 2)) + list(range(n - 1, 0, -2))


def ring_member(place, n):
    if n % 2:
        return place
    return jnp.where(place < n // 2, 2 * place, 2 * (n - 1 - place) + 1)


def ring_position(member, n):
    if n % 2:
        return member
    return jnp.where(member % 2 == 0, member // 2, n - 1 - member // 2)


def ring_gather(front, back, seq_rank, group_rank, n):
    order = ring_order(n)
    position = [0] * n
    for place, member in enumerate(order):
        position[member] = place
    forward_pairs = [(order[p], order[(p + 1) % n]) for p in range(n)]
    backward_pairs = [(order[p], order[(p - 1) % n]) for p in range(n)]
    group_pairs = [(0, 1), (1, 0)]
    place = ring_position(seq_rank, n)
    steps = jnp.arange(n, dtype=jnp.int32)
    block_of = ring_member((place - steps) % n, n)
    slot_of = (place - ring_position(steps, n)) % n
    first_group = group_rank == 0

    def thirds(values):
        width = values.shape[1] // 3
        return [values[:, i * width:(i + 1) * width] for i in range(3)]

    def carried(values):
        left, middle, right = thirds(values)
        return jnp.stack([jnp.where(first_group, left, right), middle])

    front_ring = [carried(front)]
    back_ring = [carried(back)]
    for step in range(1, n):
        front_ring.append(lax.ppermute(front_ring[-1], "seq", forward_pairs))
        back_ring.append(lax.ppermute(back_ring[-1], "seq", backward_pairs))
    front_pieces = [front]
    back_pieces = [back]
    for step in range(1, n):
        handed = lax.ppermute(
            jnp.stack([front_ring[step][0], back_ring[step][0]]), "groups", group_pairs
        )
        for ring, pieces, other in ((front_ring, front_pieces, handed[0]), (back_ring, back_pieces, handed[1])):
            own, middle = ring[step][0], ring[step][1]
            pieces.append(
                jnp.concatenate(
                    [jnp.where(first_group, own, other), middle, jnp.where(first_group, other, own)],
                    axis=1,
                )
            )
    if n <= PIECEWISE_RING:
        for step in range(n - 1):
            front_pieces[step], back_pieces[step], _, _ = lax.optimization_barrier(
                (front_pieces[step], back_pieces[step], front_ring[step + 1], back_ring[step + 1])
            )
    back_pieces = [back_pieces[(n - k) % n] for k in range(n)]
    return front_pieces, back_pieces, block_of, slot_of


def permute_blocks(values, block_order, n):
    lead = values.shape[:-1]
    width = values.shape[-1] // n
    blocks = values.reshape(lead + (n, width))
    return jnp.take(blocks, block_order, axis=-2).reshape(values.shape)


def shards(
    n_seq,
    generator_rows,
    pre_gain,
    query_weight,
    key_weight,
    value_weight,
    out_weight,
    post_gain,
    final_gain,
    label_table,
    lengths,
    label_index,
):
    seq_rank = lax.axis_index("seq")
    core_rank = lax.axis_index("wg")
    guard_half = lax.all_to_all(generator_rows, "seq", split_axis=0, concat_axis=0, tiled=True)
    guard_rows = lax.all_gather(guard_half, "wg", axis=1, tiled=True)
    q_cols = query_weight.shape[1]
    k_cols = key_weight.shape[1]
    front = jnp.concatenate([query_weight, key_weight], axis=1)
    back = jnp.concatenate([value_weight, out_weight.T], axis=1)
    front_pieces, back_pieces, block_of, slot_of = ring_gather(
        front, back, seq_rank, lax.axis_index("groups"), n_seq
    )
    guard_rows = permute_blocks(guard_rows, block_of, n_seq)
    pre_gain, post_gain, final_gain = permute_blocks(
        jnp.stack([pre_gain, post_gain, final_gain]), block_of, n_seq
    )
    label_table = permute_blocks(label_table, block_of, n_seq)
    piecewise = n_seq <= PIECEWISE_RING
    if piecewise:
        front_t = jnp.concatenate([piece.T for piece in front_pieces], axis=1)
        back_t = jnp.concatenate([piece.T for piece in back_pieces], axis=1)
        w_query_t = front_t[:q_cols]
        w_key_t = front_t[q_cols:]
        w_value_t = back_t[:k_cols]
        w_out = back_t[k_cols:]
    else:
        front_all = jnp.concatenate(front_pieces, axis=0)
        back_all = jnp.concatenate(back_pieces, axis=0)
        w_query_t = front_all[:, :q_cols].T
        w_key_t = front_all[:, q_cols:].T
        w_value_t = back_all[:, :k_cols].T
        w_out = back_all[:, k_cols:].T
    tok_rows = guard_rows.shape[0]
    half_width = generator_rows.shape[1]
    local_heads = q_cols // HD
    local_kv = k_cols // HD
    group_size = local_heads // local_kv
    length = lax.dynamic_index_in_dim(lengths, seq_rank, 0, keepdims=False)
    target = lax.dynamic_index_in_dim(label_index, seq_rank, 0, keepdims=False)
    offsets = jnp.arange(tok_rows, dtype=jnp.int32)
    cos_table, sin_table = rope_tables(offsets, HD)
    inputs = guard_rows.astype(jnp.float32)
    scale_in = lax.rsqrt(jnp.mean(inputs * inputs, axis=-1, keepdims=True) + EPSILON)
    normed = (inputs * scale_in * pre_gain).astype(jnp.bfloat16)
    if piecewise:
        block_rows = front_pieces[0].shape[0]
        front_proj = None
        back_proj = None
        for index, (front_piece, back_piece) in enumerate(zip(front_pieces, back_pieces)):
            normed_block = normed[:, index * block_rows:(index + 1) * block_rows]
            front_term = jnp.dot(normed_block, front_piece, preferred_element_type=jnp.float32)
            back_term = jnp.dot(normed_block, back_piece[:, :k_cols], preferred_element_type=jnp.float32)
            front_proj = front_term if front_proj is None else front_proj + front_term
            back_proj = back_term if back_proj is None else back_proj + back_term
    else:
        front_proj = jnp.dot(normed, front_all, preferred_element_type=jnp.float32)
        back_proj = jnp.dot(normed, back_all[:, :k_cols], preferred_element_type=jnp.float32)
    query_proj = front_proj[:, :q_cols].reshape(tok_rows, local_heads, HD).transpose(1, 0, 2)
    queries = (rotate(query_proj, cos_table, sin_table) * QUERY_SCALE).astype(jnp.bfloat16)
    key_proj = front_proj[:, q_cols:].reshape(tok_rows, local_kv, HD).transpose(1, 0, 2)
    keys_own = rotate(key_proj, cos_table, sin_table).astype(jnp.bfloat16)
    values_own = (
        back_proj
        .astype(jnp.bfloat16)
        .reshape(tok_rows, local_kv, HD)
        .transpose(1, 0, 2)
    )
    allowed = (offsets[None, :] <= offsets[:, None]) & (offsets[None, :] < length)
    query_four = queries.reshape(local_kv, group_size, tok_rows, HD)
    raw_scores = jnp.einsum(
        "kgid,kjd->kgij", query_four, keys_own, preferred_element_type=jnp.float32
    )
    capped = jnp.tanh(raw_scores / ATTEND_CAP)
    weight_exp = jnp.where(allowed[None, None], jnp.exp(ATTEND_CAP * capped), 0.0)
    soft_weights = weight_exp / jnp.sum(weight_exp, axis=-1, keepdims=True)
    attend = soft_weights.astype(jnp.bfloat16)
    context = jnp.einsum(
        "kgij,kjd->kgid", attend, values_own, preferred_element_type=jnp.float32
    ).astype(jnp.bfloat16)
    context_rows = (
        context.reshape(local_heads, tok_rows, HD)
        .transpose(1, 0, 2)
        .reshape(tok_rows, local_heads * HD)
    )
    out_part = jnp.dot(context_rows, w_out, preferred_element_type=jnp.float32)
    attention = pair_sum(out_part.astype(jnp.bfloat16))
    scale_attn = lax.rsqrt(jnp.mean(attention * attention, axis=-1, keepdims=True) + EPSILON)
    mixed_rows = inputs + attention * scale_attn * post_gain
    scale_out = lax.rsqrt(jnp.mean(mixed_rows * mixed_rows, axis=-1, keepdims=True) + EPSILON)
    final_rows = (mixed_rows * scale_out * final_gain).astype(jnp.bfloat16)
    logits = times_transposed(final_rows, label_table)
    label_cap = jnp.tanh(logits / LABEL_CAP)
    label_exp = jnp.exp(LABEL_CAP * label_cap)
    chance = label_exp / jnp.sum(label_exp, axis=-1, keepdims=True)
    live_rows = (offsets < length)[:, None]
    onehot = (jnp.arange(LABELS, dtype=jnp.int32) == target).astype(jnp.float32)[None, :]
    grad_logit = (
        jnp.where(live_rows, chance - onehot, 0.0) * (1.0 - label_cap * label_cap)
    ).astype(jnp.bfloat16)
    grad_final = jnp.dot(grad_logit, label_table, preferred_element_type=jnp.float32)
    scaled_final = grad_final * final_gain
    cube_out = scale_out * scale_out * scale_out
    grad_mixed = scale_out * scaled_final - mixed_rows * cube_out * jnp.mean(
        scaled_final * mixed_rows, axis=-1, keepdims=True
    )
    scaled_post = grad_mixed * post_gain
    cube_attn = scale_attn * scale_attn * scale_attn
    grad_attention = scale_attn * scaled_post - attention * cube_attn * jnp.mean(
        scaled_post * attention, axis=-1, keepdims=True
    )
    grad_context = times_transposed(grad_attention.astype(jnp.bfloat16), w_out).astype(jnp.bfloat16)
    grad_four = grad_context.reshape(tok_rows, local_kv, group_size, HD).transpose(1, 2, 0, 3)
    grad_prob = jnp.einsum(
        "kgid,kjd->kgij", grad_four, values_own, preferred_element_type=jnp.float32
    )
    grad_score = (
        soft_weights
        * (grad_prob - jnp.sum(soft_weights * grad_prob, axis=-1, keepdims=True))
        * (1.0 - capped * capped)
    )
    score_round = grad_score.astype(jnp.bfloat16)
    grad_query = jnp.einsum(
        "kgij,kjd->kgid", score_round, keys_own, preferred_element_type=jnp.float32
    ).reshape(local_heads, tok_rows, HD)
    grad_queries = rotate_back(grad_query * QUERY_SCALE, cos_table, sin_table).astype(jnp.bfloat16)
    grad_key = jnp.einsum(
        "kgij,kgid->kjd", score_round, query_four, preferred_element_type=jnp.float32
    )
    grad_value = jnp.einsum("kgij,kgid->kjd", attend, grad_four, preferred_element_type=jnp.float32)
    grad_keys = rotate_back(grad_key, cos_table, sin_table).astype(jnp.bfloat16)
    grad_values = grad_value.astype(jnp.bfloat16)
    query_rows = grad_queries.transpose(1, 0, 2).reshape(tok_rows, local_heads * HD)
    key_rows = grad_keys.transpose(1, 0, 2).reshape(tok_rows, local_kv * HD)
    value_rows = grad_values.transpose(1, 0, 2).reshape(tok_rows, local_kv * HD)
    grad_part = (
        jnp.dot(query_rows, w_query_t, preferred_element_type=jnp.float32)
        + jnp.dot(key_rows, w_key_t, preferred_element_type=jnp.float32)
        + jnp.dot(value_rows, w_value_t, preferred_element_type=jnp.float32)
    )
    cube_in = scale_in * scale_in * scale_in
    grad_normed = pair_sum(grad_part.astype(jnp.bfloat16))
    scaled_in = grad_normed * pre_gain
    row_stat = jnp.mean(scaled_in * inputs, axis=-1, keepdims=True)
    grad_full = scale_in * scaled_in - inputs * cube_in * row_stat + grad_mixed
    block_width = grad_full.shape[1] // n_seq
    half_blocks = half_width // block_width
    own_blocks = core_rank * half_blocks + jnp.arange(half_blocks, dtype=jnp.int32)
    grad_blocks = grad_full.astype(jnp.bfloat16).reshape(tok_rows, n_seq, block_width)
    grad_rows = jnp.take(grad_blocks, slot_of[own_blocks], axis=1).reshape(tok_rows, half_width)
    return lax.all_to_all(grad_rows, "seq", split_axis=0, concat_axis=0, tiled=True)


def solution(mesh):
    return jax.shard_map(
        functools.partial(shards, mesh.shape["seq"]),
        mesh=mesh,
        in_specs=(
            P(("groups", "seq"), "wg"),
            P(),
            P("seq", "wg"),
            P("seq", "wg"),
            P("seq", "wg"),
            P("wg", "seq"),
            P(),
            P(),
            P(),
            P("groups"),
            P("groups"),
        ),
        out_specs=P(("groups", "seq"), "wg"),
        check_vma=False,
    )
```

```python
import functools

import jax
import jax.numpy as jnp
from jax import lax
from jax.sharding import PartitionSpec as P

HD = 128
LABELS = 64


PIECEWISE_RING = 16
EPSILON = 1e-06
ATTEND_CAP = 50.0
LABEL_CAP = 30.0
QUERY_SCALE = 1.0 / 12.0


def rope_tables(positions, head_width):
    frequency = 10000.0 ** (-2.0 * jnp.arange(head_width // 2, dtype=jnp.float32) / head_width)
    angles = positions.astype(jnp.float32)[:, None] * frequency[None, :]
    return (jnp.cos(angles), jnp.sin(angles))


def rotate(values, cos_table, sin_table):
    half_width = values.shape[-1] // 2
    lower_part = values[..., :half_width]
    upper_part = values[..., half_width:]
    return jnp.concatenate(
        [
            lower_part * cos_table - upper_part * sin_table,
            upper_part * cos_table + lower_part * sin_table,
        ],
        axis=-1,
    )


def rotate_back(values, cos_table, sin_table):
    half_width = values.shape[-1] // 2
    lower_part = values[..., :half_width]
    upper_part = values[..., half_width:]
    return jnp.concatenate(
        [
            lower_part * cos_table + upper_part * sin_table,
            upper_part * cos_table - lower_part * sin_table,
        ],
        axis=-1,
    )


def times_transposed(left_side, right_side):
    return lax.dot_general(
        left_side, right_side, (((1,), (1,)), ((), ())), preferred_element_type=jnp.float32
    )


def pair_sum(rounded_part):
    other = lax.ppermute(rounded_part, "wg", perm=[(0, 1), (1, 0)])
    return rounded_part.astype(jnp.float32) + other.astype(jnp.float32)


def ring_order(n):
    if n % 2:
        return list(range(n))
    return list(range(0, n, 2)) + list(range(n - 1, 0, -2))


def ring_member(place, n):
    if n % 2:
        return place
    return jnp.where(place < n // 2, 2 * place, 2 * (n - 1 - place) + 1)


def ring_position(member, n):
    if n % 2:
        return member
    return jnp.where(member % 2 == 0, member // 2, n - 1 - member // 2)


def ring_gather(front, back, seq_rank, group_rank, n):
    order = ring_order(n)
    position = [0] * n
    for place, member in enumerate(order):
        position[member] = place
    forward_pairs = [(order[p], order[(p + 1) % n]) for p in range(n)]
    backward_pairs = [(order[p], order[(p - 1) % n]) for p in range(n)]
    group_pairs = [(0, 1), (1, 0)]
    place = ring_position(seq_rank, n)
    steps = jnp.arange(n, dtype=jnp.int32)
    block_of = ring_member((place - steps) % n, n)
    slot_of = (place - ring_position(steps, n)) % n
    first_group = group_rank == 0

    def thirds(values):
        width = values.shape[1] // 3
        return [values[:, i * width:(i + 1) * width] for i in range(3)]

    def carried(values):
        left, middle, right = thirds(values)
        return jnp.stack([jnp.where(first_group, left, right), middle])

    front_ring = [carried(front)]
    back_ring = [carried(back)]
    for step in range(1, n):
        front_ring.append(lax.ppermute(front_ring[-1], "seq", forward_pairs))
        back_ring.append(lax.ppermute(back_ring[-1], "seq", backward_pairs))
    front_pieces = [front]
    back_pieces = [back]
    for step in range(1, n):
        handed = lax.ppermute(
            jnp.stack([front_ring[step][0], back_ring[step][0]]), "groups", group_pairs
        )
        for ring, pieces, other in ((front_ring, front_pieces, handed[0]), (back_ring, back_pieces, handed[1])):
            own, middle = ring[step][0], ring[step][1]
            pieces.append(
                jnp.concatenate(
                    [jnp.where(first_group, own, other), middle, jnp.where(first_group, other, own)],
                    axis=1,
                )
            )
    if n <= PIECEWISE_RING:
        for step in range(n - 1):
            front_pieces[step], back_pieces[step], _, _ = lax.optimization_barrier(
                (front_pieces[step], back_pieces[step], front_ring[step + 1], back_ring[step + 1])
            )
    back_pieces = [back_pieces[(n - k) % n] for k in range(n)]
    return front_pieces, back_pieces, block_of, slot_of, (front_ring[1], back_ring[1])


def permute_blocks(values, block_order, n):
    lead = values.shape[:-1]
    width = values.shape[-1] // n
    blocks = values.reshape(lead + (n, width))
    return jnp.take(blocks, block_order, axis=-2).reshape(values.shape)


def shards(
    n_seq,
    generator_rows,
    pre_gain,
    query_weight,
    key_weight,
    value_weight,
    out_weight,
    post_gain,
    final_gain,
    label_table,
    lengths,
    label_index,
):
    seq_rank = lax.axis_index("seq")
    core_rank = lax.axis_index("wg")
    guard_half = lax.all_to_all(generator_rows, "seq", split_axis=0, concat_axis=0, tiled=True)
    q_cols = query_weight.shape[1]
    k_cols = key_weight.shape[1]
    front = jnp.concatenate([query_weight, key_weight], axis=1)
    back = jnp.concatenate([value_weight, out_weight.T], axis=1)
    front_pieces, back_pieces, block_of, slot_of, first_arrival = ring_gather(
        front, back, seq_rank, lax.axis_index("groups"), n_seq
    )
    guard_half, _ = lax.optimization_barrier((guard_half, first_arrival))
    guard_rows = lax.all_gather(guard_half, "wg", axis=1, tiled=True)
    guard_rows = permute_blocks(guard_rows, block_of, n_seq)
    pre_gain, post_gain, final_gain = permute_blocks(
        jnp.stack([pre_gain, post_gain, final_gain]), block_of, n_seq
    )
    label_table = permute_blocks(label_table, block_of, n_seq)
    piecewise = n_seq <= PIECEWISE_RING
    if piecewise:
        w_query_t = jnp.concatenate([piece[:, :q_cols].T for piece in front_pieces], axis=1)
        w_key_t = jnp.concatenate([piece[:, q_cols:].T for piece in front_pieces], axis=1)
        w_value_t = jnp.concatenate([piece[:, :k_cols].T for piece in back_pieces], axis=1)
        w_out = jnp.concatenate([piece[:, k_cols:].T for piece in back_pieces], axis=1)
    else:
        front_all = jnp.concatenate(front_pieces, axis=0)
        back_all = jnp.concatenate(back_pieces, axis=0)
        w_query_t = front_all[:, :q_cols].T
        w_key_t = front_all[:, q_cols:].T
        w_value_t = back_all[:, :k_cols].T
        w_out = back_all[:, k_cols:].T
    tok_rows = guard_rows.shape[0]
    half_width = generator_rows.shape[1]
    local_heads = q_cols // HD
    local_kv = k_cols // HD
    group_size = local_heads // local_kv
    length = lax.dynamic_index_in_dim(lengths, seq_rank, 0, keepdims=False)
    target = lax.dynamic_index_in_dim(label_index, seq_rank, 0, keepdims=False)
    offsets = jnp.arange(tok_rows, dtype=jnp.int32)
    cos_table, sin_table = rope_tables(offsets, HD)
    inputs = guard_rows.astype(jnp.float32)
    scale_in = lax.rsqrt(jnp.mean(inputs * inputs, axis=-1, keepdims=True) + EPSILON)
    normed = (inputs * scale_in * pre_gain).astype(jnp.bfloat16)
    if piecewise:
        block_rows = front_pieces[0].shape[0]
        front_proj = None
        back_proj = None
        for index, (front_piece, back_piece) in enumerate(zip(front_pieces, back_pieces)):
            normed_block = normed[:, index * block_rows:(index + 1) * block_rows]
            front_term = jnp.dot(normed_block, front_piece, preferred_element_type=jnp.float32)
            back_term = jnp.dot(normed_block, back_piece[:, :k_cols], preferred_element_type=jnp.float32)
            front_proj = front_term if front_proj is None else front_proj + front_term
            back_proj = back_term if back_proj is None else back_proj + back_term
    else:
        front_proj = jnp.dot(normed, front_all, preferred_element_type=jnp.float32)
        back_proj = jnp.dot(normed, back_all[:, :k_cols], preferred_element_type=jnp.float32)
    query_proj = front_proj[:, :q_cols].reshape(tok_rows, local_heads, HD).transpose(1, 0, 2)
    queries = (rotate(query_proj, cos_table, sin_table) * QUERY_SCALE).astype(jnp.bfloat16)
    key_proj = front_proj[:, q_cols:].reshape(tok_rows, local_kv, HD).transpose(1, 0, 2)
    keys_own = rotate(key_proj, cos_table, sin_table).astype(jnp.bfloat16)
    values_own = (
        back_proj
        .astype(jnp.bfloat16)
        .reshape(tok_rows, local_kv, HD)
        .transpose(1, 0, 2)
    )
    allowed = (offsets[None, :] <= offsets[:, None]) & (offsets[None, :] < length)
    query_four = queries.reshape(local_kv, group_size, tok_rows, HD)
    raw_scores = jnp.einsum(
        "kgid,kjd->kgij", query_four, keys_own, preferred_element_type=jnp.float32
    )
    capped = jnp.tanh(raw_scores / ATTEND_CAP)
    weight_exp = jnp.where(allowed[None, None], jnp.exp(ATTEND_CAP * capped), 0.0)
    soft_weights = weight_exp / jnp.sum(weight_exp, axis=-1, keepdims=True)
    attend = soft_weights.astype(jnp.bfloat16)
    context = jnp.einsum(
        "kgij,kjd->kgid", attend, values_own, preferred_element_type=jnp.float32
    ).astype(jnp.bfloat16)
    context_rows = (
        context.reshape(local_heads, tok_rows, HD)
        .transpose(1, 0, 2)
        .reshape(tok_rows, local_heads * HD)
    )
    out_part = jnp.dot(context_rows, w_out, preferred_element_type=jnp.float32)
    attention = pair_sum(out_part.astype(jnp.bfloat16))
    scale_attn = lax.rsqrt(jnp.mean(attention * attention, axis=-1, keepdims=True) + EPSILON)
    mixed_rows = inputs + attention * scale_attn * post_gain
    scale_out = lax.rsqrt(jnp.mean(mixed_rows * mixed_rows, axis=-1, keepdims=True) + EPSILON)
    final_rows = (mixed_rows * scale_out * final_gain).astype(jnp.bfloat16)
    logits = times_transposed(final_rows, label_table)
    label_cap = jnp.tanh(logits / LABEL_CAP)
    label_exp = jnp.exp(LABEL_CAP * label_cap)
    chance = label_exp / jnp.sum(label_exp, axis=-1, keepdims=True)
    live_rows = (offsets < length)[:, None]
    onehot = (jnp.arange(LABELS, dtype=jnp.int32) == target).astype(jnp.float32)[None, :]
    grad_logit = (
        jnp.where(live_rows, chance - onehot, 0.0) * (1.0 - label_cap * label_cap)
    ).astype(jnp.bfloat16)
    grad_final = jnp.dot(grad_logit, label_table, preferred_element_type=jnp.float32)
    scaled_final = grad_final * final_gain
    cube_out = scale_out * scale_out * scale_out
    grad_mixed = scale_out * scaled_final - mixed_rows * cube_out * jnp.mean(
        scaled_final * mixed_rows, axis=-1, keepdims=True
    )
    scaled_post = grad_mixed * post_gain
    cube_attn = scale_attn * scale_attn * scale_attn
    grad_attention = scale_attn * scaled_post - attention * cube_attn * jnp.mean(
        scaled_post * attention, axis=-1, keepdims=True
    )
    grad_context = times_transposed(grad_attention.astype(jnp.bfloat16), w_out).astype(jnp.bfloat16)
    grad_four = grad_context.reshape(tok_rows, local_kv, group_size, HD).transpose(1, 2, 0, 3)
    grad_prob = jnp.einsum(
        "kgid,kjd->kgij", grad_four, values_own, preferred_element_type=jnp.float32
    )
    grad_score = (
        soft_weights
        * (grad_prob - jnp.sum(soft_weights * grad_prob, axis=-1, keepdims=True))
        * (1.0 - capped * capped)
    )
    score_round = grad_score.astype(jnp.bfloat16)
    grad_query = jnp.einsum(
        "kgij,kjd->kgid", score_round, keys_own, preferred_element_type=jnp.float32
    ).reshape(local_heads, tok_rows, HD)
    grad_queries = rotate_back(grad_query * QUERY_SCALE, cos_table, sin_table).astype(jnp.bfloat16)
    grad_key = jnp.einsum(
        "kgij,kgid->kjd", score_round, query_four, preferred_element_type=jnp.float32
    )
    grad_value = jnp.einsum("kgij,kgid->kjd", attend, grad_four, preferred_element_type=jnp.float32)
    grad_keys = rotate_back(grad_key, cos_table, sin_table).astype(jnp.bfloat16)
    grad_values = grad_value.astype(jnp.bfloat16)
    query_rows = grad_queries.transpose(1, 0, 2).reshape(tok_rows, local_heads * HD)
    key_rows = grad_keys.transpose(1, 0, 2).reshape(tok_rows, local_kv * HD)
    value_rows = grad_values.transpose(1, 0, 2).reshape(tok_rows, local_kv * HD)
    grad_part = (
        jnp.dot(query_rows, w_query_t, preferred_element_type=jnp.float32)
        + jnp.dot(key_rows, w_key_t, preferred_element_type=jnp.float32)
        + jnp.dot(value_rows, w_value_t, preferred_element_type=jnp.float32)
    )
    cube_in = scale_in * scale_in * scale_in
    grad_normed = pair_sum(grad_part.astype(jnp.bfloat16))
    scaled_in = grad_normed * pre_gain
    row_stat = jnp.mean(scaled_in * inputs, axis=-1, keepdims=True)
    grad_full = scale_in * scaled_in - inputs * cube_in * row_stat + grad_mixed
    block_width = grad_full.shape[1] // n_seq
    half_blocks = half_width // block_width
    own_blocks = core_rank * half_blocks + jnp.arange(half_blocks, dtype=jnp.int32)
    grad_blocks = grad_full.astype(jnp.bfloat16).reshape(tok_rows, n_seq, block_width)
    grad_rows = jnp.take(grad_blocks, slot_of[own_blocks], axis=1).reshape(tok_rows, half_width)
    return lax.all_to_all(grad_rows, "seq", split_axis=0, concat_axis=0, tiled=True)


def solution(mesh):
    return jax.shard_map(
        functools.partial(shards, mesh.shape["seq"]),
        mesh=mesh,
        in_specs=(
            P(("groups", "seq"), "wg"),
            P(),
            P("seq", "wg"),
            P("seq", "wg"),
            P("seq", "wg"),
            P("wg", "seq"),
            P(),
            P(),
            P(),
            P("groups"),
            P("groups"),
        ),
        out_specs=P(("groups", "seq"), "wg"),
        check_vma=False,
    )
```

```python
import functools

import jax
import jax.numpy as jnp
from jax import lax
from jax.sharding import PartitionSpec as P

HD = 128
LABELS = 64


PIECEWISE_RING = 16
EPSILON = 1e-06
ATTEND_CAP = 50.0
LABEL_CAP = 30.0
QUERY_SCALE = 1.0 / 12.0


def rope_tables(positions, head_width):
    frequency = 10000.0 ** (-2.0 * jnp.arange(head_width // 2, dtype=jnp.float32) / head_width)
    angles = positions.astype(jnp.float32)[:, None] * frequency[None, :]
    return (jnp.cos(angles), jnp.sin(angles))


def rotate(values, cos_table, sin_table):
    half_width = values.shape[-1] // 2
    lower_part = values[..., :half_width]
    upper_part = values[..., half_width:]
    return jnp.concatenate(
        [
            lower_part * cos_table - upper_part * sin_table,
            upper_part * cos_table + lower_part * sin_table,
        ],
        axis=-1,
    )


def rotate_back(values, cos_table, sin_table):
    half_width = values.shape[-1] // 2
    lower_part = values[..., :half_width]
    upper_part = values[..., half_width:]
    return jnp.concatenate(
        [
            lower_part * cos_table + upper_part * sin_table,
            upper_part * cos_table - lower_part * sin_table,
        ],
        axis=-1,
    )


def times_transposed(left_side, right_side):
    return lax.dot_general(
        left_side, right_side, (((1,), (1,)), ((), ())), preferred_element_type=jnp.float32
    )


def pair_sum(rounded_part):
    other = lax.ppermute(rounded_part, "wg", perm=[(0, 1), (1, 0)])
    return rounded_part.astype(jnp.float32) + other.astype(jnp.float32)


def ring_order(n):
    if n % 2:
        return list(range(n))
    return list(range(0, n, 2)) + list(range(n - 1, 0, -2))


def ring_member(place, n):
    if n % 2:
        return place
    return jnp.where(place < n // 2, 2 * place, 2 * (n - 1 - place) + 1)


def ring_position(member, n):
    if n % 2:
        return member
    return jnp.where(member % 2 == 0, member // 2, n - 1 - member // 2)


def ring_gather(front, back, seq_rank, group_rank, n):
    order = ring_order(n)
    position = [0] * n
    for place, member in enumerate(order):
        position[member] = place
    forward_pairs = [(order[p], order[(p + 1) % n]) for p in range(n)]
    backward_pairs = [(order[p], order[(p - 1) % n]) for p in range(n)]
    group_pairs = [(0, 1), (1, 0)]
    place = ring_position(seq_rank, n)
    steps = jnp.arange(n, dtype=jnp.int32)
    block_of = ring_member((place - steps) % n, n)
    slot_of = (place - ring_position(steps, n)) % n
    first_group = group_rank == 0

    def thirds(values):
        width = values.shape[1] // 3
        return [values[:, i * width:(i + 1) * width] for i in range(3)]

    def carried(values):
        left, middle, right = thirds(values)
        return jnp.stack([jnp.where(first_group, left, right), middle])

    front_ring = [carried(front)]
    back_ring = [carried(back)]
    for step in range(1, n):
        front_ring.append(lax.ppermute(front_ring[-1], "seq", forward_pairs))
        back_ring.append(lax.ppermute(back_ring[-1], "seq", backward_pairs))
    front_pieces = [front]
    back_pieces = [back]
    for step in range(1, n):
        handed = lax.ppermute(
            jnp.stack([front_ring[step][0], back_ring[step][0]]), "groups", group_pairs
        )
        for ring, pieces, other in ((front_ring, front_pieces, handed[0]), (back_ring, back_pieces, handed[1])):
            own, middle = ring[step][0], ring[step][1]
            pieces.append(
                jnp.concatenate(
                    [jnp.where(first_group, own, other), middle, jnp.where(first_group, other, own)],
                    axis=1,
                )
            )
    if n <= PIECEWISE_RING:
        for step in range(n - 1):
            front_pieces[step], back_pieces[step], _, _ = lax.optimization_barrier(
                (front_pieces[step], back_pieces[step], front_ring[step + 1], back_ring[step + 1])
            )
    back_pieces = [back_pieces[(n - k) % n] for k in range(n)]
    return front_pieces, back_pieces, block_of, slot_of, (front_ring[2], back_ring[2])


def permute_blocks(values, block_order, n):
    lead = values.shape[:-1]
    width = values.shape[-1] // n
    blocks = values.reshape(lead + (n, width))
    return jnp.take(blocks, block_order, axis=-2).reshape(values.shape)


def shards(
    n_seq,
    generator_rows,
    pre_gain,
    query_weight,
    key_weight,
    value_weight,
    out_weight,
    post_gain,
    final_gain,
    label_table,
    lengths,
    label_index,
):
    seq_rank = lax.axis_index("seq")
    core_rank = lax.axis_index("wg")
    guard_half = lax.all_to_all(generator_rows, "seq", split_axis=0, concat_axis=0, tiled=True)
    q_cols = query_weight.shape[1]
    k_cols = key_weight.shape[1]
    front = jnp.concatenate([query_weight, key_weight], axis=1)
    back = jnp.concatenate([value_weight, out_weight.T], axis=1)
    front_pieces, back_pieces, block_of, slot_of, first_arrival = ring_gather(
        front, back, seq_rank, lax.axis_index("groups"), n_seq
    )
    guard_half, _ = lax.optimization_barrier((guard_half, first_arrival))
    guard_rows = lax.all_gather(guard_half, "wg", axis=1, tiled=True)
    guard_rows = permute_blocks(guard_rows, block_of, n_seq)
    pre_gain, post_gain, final_gain = permute_blocks(
        jnp.stack([pre_gain, post_gain, final_gain]), block_of, n_seq
    )
    label_table = permute_blocks(label_table, block_of, n_seq)
    piecewise = n_seq <= PIECEWISE_RING
    if piecewise:
        w_query_t = jnp.concatenate([piece[:, :q_cols].T for piece in front_pieces], axis=1)
        w_key_t = jnp.concatenate([piece[:, q_cols:].T for piece in front_pieces], axis=1)
        w_value_t = jnp.concatenate([piece[:, :k_cols].T for piece in back_pieces], axis=1)
        w_out = jnp.concatenate([piece[:, k_cols:].T for piece in back_pieces], axis=1)
    else:
        front_all = jnp.concatenate(front_pieces, axis=0)
        back_all = jnp.concatenate(back_pieces, axis=0)
        w_query_t = front_all[:, :q_cols].T
        w_key_t = front_all[:, q_cols:].T
        w_value_t = back_all[:, :k_cols].T
        w_out = back_all[:, k_cols:].T
    tok_rows = guard_rows.shape[0]
    half_width = generator_rows.shape[1]
    local_heads = q_cols // HD
    local_kv = k_cols // HD
    group_size = local_heads // local_kv
    length = lax.dynamic_index_in_dim(lengths, seq_rank, 0, keepdims=False)
    target = lax.dynamic_index_in_dim(label_index, seq_rank, 0, keepdims=False)
    offsets = jnp.arange(tok_rows, dtype=jnp.int32)
    cos_table, sin_table = rope_tables(offsets, HD)
    inputs = guard_rows.astype(jnp.float32)
    scale_in = lax.rsqrt(jnp.mean(inputs * inputs, axis=-1, keepdims=True) + EPSILON)
    normed = (inputs * scale_in * pre_gain).astype(jnp.bfloat16)
    if piecewise:
        block_rows = front_pieces[0].shape[0]
        front_proj = None
        back_proj = None
        for index, (front_piece, back_piece) in enumerate(zip(front_pieces, back_pieces)):
            normed_block = normed[:, index * block_rows:(index + 1) * block_rows]
            front_term = jnp.dot(normed_block, front_piece, preferred_element_type=jnp.float32)
            back_term = jnp.dot(normed_block, back_piece[:, :k_cols], preferred_element_type=jnp.float32)
            front_proj = front_term if front_proj is None else front_proj + front_term
            back_proj = back_term if back_proj is None else back_proj + back_term
    else:
        front_proj = jnp.dot(normed, front_all, preferred_element_type=jnp.float32)
        back_proj = jnp.dot(normed, back_all[:, :k_cols], preferred_element_type=jnp.float32)
    query_proj = front_proj[:, :q_cols].reshape(tok_rows, local_heads, HD).transpose(1, 0, 2)
    queries = (rotate(query_proj, cos_table, sin_table) * QUERY_SCALE).astype(jnp.bfloat16)
    key_proj = front_proj[:, q_cols:].reshape(tok_rows, local_kv, HD).transpose(1, 0, 2)
    keys_own = rotate(key_proj, cos_table, sin_table).astype(jnp.bfloat16)
    values_own = (
        back_proj
        .astype(jnp.bfloat16)
        .reshape(tok_rows, local_kv, HD)
        .transpose(1, 0, 2)
    )
    allowed = (offsets[None, :] <= offsets[:, None]) & (offsets[None, :] < length)
    query_four = queries.reshape(local_kv, group_size, tok_rows, HD)
    raw_scores = jnp.einsum(
        "kgid,kjd->kgij", query_four, keys_own, preferred_element_type=jnp.float32
    )
    capped = jnp.tanh(raw_scores / ATTEND_CAP)
    weight_exp = jnp.where(allowed[None, None], jnp.exp(ATTEND_CAP * capped), 0.0)
    soft_weights = weight_exp / jnp.sum(weight_exp, axis=-1, keepdims=True)
    attend = soft_weights.astype(jnp.bfloat16)
    context = jnp.einsum(
        "kgij,kjd->kgid", attend, values_own, preferred_element_type=jnp.float32
    ).astype(jnp.bfloat16)
    context_rows = (
        context.reshape(local_heads, tok_rows, HD)
        .transpose(1, 0, 2)
        .reshape(tok_rows, local_heads * HD)
    )
    out_part = jnp.dot(context_rows, w_out, preferred_element_type=jnp.float32)
    attention = pair_sum(out_part.astype(jnp.bfloat16))
    scale_attn = lax.rsqrt(jnp.mean(attention * attention, axis=-1, keepdims=True) + EPSILON)
    mixed_rows = inputs + attention * scale_attn * post_gain
    scale_out = lax.rsqrt(jnp.mean(mixed_rows * mixed_rows, axis=-1, keepdims=True) + EPSILON)
    final_rows = (mixed_rows * scale_out * final_gain).astype(jnp.bfloat16)
    logits = times_transposed(final_rows, label_table)
    label_cap = jnp.tanh(logits / LABEL_CAP)
    label_exp = jnp.exp(LABEL_CAP * label_cap)
    chance = label_exp / jnp.sum(label_exp, axis=-1, keepdims=True)
    live_rows = (offsets < length)[:, None]
    onehot = (jnp.arange(LABELS, dtype=jnp.int32) == target).astype(jnp.float32)[None, :]
    grad_logit = (
        jnp.where(live_rows, chance - onehot, 0.0) * (1.0 - label_cap * label_cap)
    ).astype(jnp.bfloat16)
    grad_final = jnp.dot(grad_logit, label_table, preferred_element_type=jnp.float32)
    scaled_final = grad_final * final_gain
    cube_out = scale_out * scale_out * scale_out
    grad_mixed = scale_out * scaled_final - mixed_rows * cube_out * jnp.mean(
        scaled_final * mixed_rows, axis=-1, keepdims=True
    )
    scaled_post = grad_mixed * post_gain
    cube_attn = scale_attn * scale_attn * scale_attn
    grad_attention = scale_attn * scaled_post - attention * cube_attn * jnp.mean(
        scaled_post * attention, axis=-1, keepdims=True
    )
    grad_context = times_transposed(grad_attention.astype(jnp.bfloat16), w_out).astype(jnp.bfloat16)
    grad_four = grad_context.reshape(tok_rows, local_kv, group_size, HD).transpose(1, 2, 0, 3)
    grad_prob = jnp.einsum(
        "kgid,kjd->kgij", grad_four, values_own, preferred_element_type=jnp.float32
    )
    grad_score = (
        soft_weights
        * (grad_prob - jnp.sum(soft_weights * grad_prob, axis=-1, keepdims=True))
        * (1.0 - capped * capped)
    )
    score_round = grad_score.astype(jnp.bfloat16)
    grad_query = jnp.einsum(
        "kgij,kjd->kgid", score_round, keys_own, preferred_element_type=jnp.float32
    ).reshape(local_heads, tok_rows, HD)
    grad_queries = rotate_back(grad_query * QUERY_SCALE, cos_table, sin_table).astype(jnp.bfloat16)
    grad_key = jnp.einsum(
        "kgij,kgid->kjd", score_round, query_four, preferred_element_type=jnp.float32
    )
    grad_value = jnp.einsum("kgij,kgid->kjd", attend, grad_four, preferred_element_type=jnp.float32)
    grad_keys = rotate_back(grad_key, cos_table, sin_table).astype(jnp.bfloat16)
    grad_values = grad_value.astype(jnp.bfloat16)
    query_rows = grad_queries.transpose(1, 0, 2).reshape(tok_rows, local_heads * HD)
    key_rows = grad_keys.transpose(1, 0, 2).reshape(tok_rows, local_kv * HD)
    value_rows = grad_values.transpose(1, 0, 2).reshape(tok_rows, local_kv * HD)
    grad_part = (
        jnp.dot(query_rows, w_query_t, preferred_element_type=jnp.float32)
        + jnp.dot(key_rows, w_key_t, preferred_element_type=jnp.float32)
        + jnp.dot(value_rows, w_value_t, preferred_element_type=jnp.float32)
    )
    cube_in = scale_in * scale_in * scale_in
    grad_normed = pair_sum(grad_part.astype(jnp.bfloat16))
    scaled_in = grad_normed * pre_gain
    row_stat = jnp.mean(scaled_in * inputs, axis=-1, keepdims=True)
    grad_full = scale_in * scaled_in - inputs * cube_in * row_stat + grad_mixed
    block_width = grad_full.shape[1] // n_seq
    half_blocks = half_width // block_width
    own_blocks = core_rank * half_blocks + jnp.arange(half_blocks, dtype=jnp.int32)
    grad_blocks = grad_full.astype(jnp.bfloat16).reshape(tok_rows, n_seq, block_width)
    grad_rows = jnp.take(grad_blocks, slot_of[own_blocks], axis=1).reshape(tok_rows, half_width)
    return lax.all_to_all(grad_rows, "seq", split_axis=0, concat_axis=0, tiled=True)


def solution(mesh):
    return jax.shard_map(
        functools.partial(shards, mesh.shape["seq"]),
        mesh=mesh,
        in_specs=(
            P(("groups", "seq"), "wg"),
            P(),
            P("seq", "wg"),
            P("seq", "wg"),
            P("seq", "wg"),
            P("wg", "seq"),
            P(),
            P(),
            P(),
            P("groups"),
            P("groups"),
        ),
        out_specs=P(("groups", "seq"), "wg"),
        check_vma=False,
    )
```

```python
import functools

import jax
import jax.numpy as jnp
from jax import lax
from jax.sharding import PartitionSpec as P

HD = 128
LABELS = 64


PIECEWISE_RING = 16
EPSILON = 1e-06
ATTEND_CAP = 50.0
LABEL_CAP = 30.0
QUERY_SCALE = 1.0 / 12.0


def rope_tables(positions, head_width):
    frequency = 10000.0 ** (-2.0 * jnp.arange(head_width // 2, dtype=jnp.float32) / head_width)
    angles = positions.astype(jnp.float32)[:, None] * frequency[None, :]
    return (jnp.cos(angles), jnp.sin(angles))


def rotate(values, cos_table, sin_table):
    half_width = values.shape[-1] // 2
    lower_part = values[..., :half_width]
    upper_part = values[..., half_width:]
    return jnp.concatenate(
        [
            lower_part * cos_table - upper_part * sin_table,
            upper_part * cos_table + lower_part * sin_table,
        ],
        axis=-1,
    )


def rotate_back(values, cos_table, sin_table):
    half_width = values.shape[-1] // 2
    lower_part = values[..., :half_width]
    upper_part = values[..., half_width:]
    return jnp.concatenate(
        [
            lower_part * cos_table + upper_part * sin_table,
            upper_part * cos_table - lower_part * sin_table,
        ],
        axis=-1,
    )


def times_transposed(left_side, right_side):
    return lax.dot_general(
        left_side, right_side, (((1,), (1,)), ((), ())), preferred_element_type=jnp.float32
    )


def pair_sum(rounded_part):
    other = lax.ppermute(rounded_part, "wg", perm=[(0, 1), (1, 0)])
    return rounded_part.astype(jnp.float32) + other.astype(jnp.float32)


def ring_order(n):
    if n % 2:
        return list(range(n))
    return list(range(0, n, 2)) + list(range(n - 1, 0, -2))


def ring_member(place, n):
    if n % 2:
        return place
    return jnp.where(place < n // 2, 2 * place, 2 * (n - 1 - place) + 1)


def ring_position(member, n):
    if n % 2:
        return member
    return jnp.where(member % 2 == 0, member // 2, n - 1 - member // 2)


def ring_gather(front, back, seq_rank, group_rank, n):
    order = ring_order(n)
    position = [0] * n
    for place, member in enumerate(order):
        position[member] = place
    forward_pairs = [(order[p], order[(p + 1) % n]) for p in range(n)]
    backward_pairs = [(order[p], order[(p - 1) % n]) for p in range(n)]
    group_pairs = [(0, 1), (1, 0)]
    place = ring_position(seq_rank, n)
    steps = jnp.arange(n, dtype=jnp.int32)
    block_of = ring_member((place - steps) % n, n)
    slot_of = (place - ring_position(steps, n)) % n
    first_group = group_rank == 0

    def thirds(values):
        width = values.shape[1] // 3
        return [values[:, i * width:(i + 1) * width] for i in range(3)]

    def carried(values):
        left, middle, right = thirds(values)
        return jnp.stack([jnp.where(first_group, left, right), middle])

    front_ring = [carried(front)]
    back_ring = [carried(back)]
    for step in range(1, n):
        front_ring.append(lax.ppermute(front_ring[-1], "seq", forward_pairs))
        back_ring.append(lax.ppermute(back_ring[-1], "seq", backward_pairs))
    front_pieces = [front]
    back_pieces = [back]
    for step in range(1, n):
        handed = lax.ppermute(
            jnp.stack([front_ring[step][0], back_ring[step][0]]), "groups", group_pairs
        )
        for ring, pieces, other in ((front_ring, front_pieces, handed[0]), (back_ring, back_pieces, handed[1])):
            own, middle = ring[step][0], ring[step][1]
            pieces.append(
                jnp.concatenate(
                    [jnp.where(first_group, own, other), middle, jnp.where(first_group, other, own)],
                    axis=1,
                )
            )
    if n <= PIECEWISE_RING:
        for step in range(n - 1):
            front_pieces[step], back_pieces[step], _, _ = lax.optimization_barrier(
                (front_pieces[step], back_pieces[step], front_ring[step + 1], back_ring[step + 1])
            )
    back_pieces = [back_pieces[(n - k) % n] for k in range(n)]
    return front_pieces, back_pieces, block_of, slot_of, (front_ring[1], back_ring[1])


def permute_blocks(values, block_order, n):
    lead = values.shape[:-1]
    width = values.shape[-1] // n
    blocks = values.reshape(lead + (n, width))
    return jnp.take(blocks, block_order, axis=-2).reshape(values.shape)


def shards(
    n_seq,
    generator_rows,
    pre_gain,
    query_weight,
    key_weight,
    value_weight,
    out_weight,
    post_gain,
    final_gain,
    label_table,
    lengths,
    label_index,
):
    seq_rank = lax.axis_index("seq")
    core_rank = lax.axis_index("wg")
    guard_half = lax.all_to_all(generator_rows, "seq", split_axis=0, concat_axis=0, tiled=True)
    q_cols = query_weight.shape[1]
    k_cols = key_weight.shape[1]
    front = jnp.concatenate([query_weight, key_weight], axis=1)
    back = jnp.concatenate([value_weight, out_weight.T], axis=1)
    front_pieces, back_pieces, block_of, slot_of, first_arrival = ring_gather(
        front, back, seq_rank, lax.axis_index("groups"), n_seq
    )
    guard_half, _ = lax.optimization_barrier((guard_half, first_arrival))
    partner_half = lax.ppermute(guard_half, "wg", perm=[(0, 1), (1, 0)])
    guard_rows = jnp.where(
        core_rank == 0,
        jnp.concatenate([guard_half, partner_half], axis=1),
        jnp.concatenate([partner_half, guard_half], axis=1),
    )
    guard_rows = permute_blocks(guard_rows, block_of, n_seq)
    pre_gain, post_gain, final_gain = permute_blocks(
        jnp.stack([pre_gain, post_gain, final_gain]), block_of, n_seq
    )
    label_table = permute_blocks(label_table, block_of, n_seq)
    piecewise = n_seq <= PIECEWISE_RING
    if piecewise:
        w_query_t = jnp.concatenate([piece[:, :q_cols].T for piece in front_pieces], axis=1)
        w_key_t = jnp.concatenate([piece[:, q_cols:].T for piece in front_pieces], axis=1)
        w_value_t = jnp.concatenate([piece[:, :k_cols].T for piece in back_pieces], axis=1)
        w_out = jnp.concatenate([piece[:, k_cols:].T for piece in back_pieces], axis=1)
    else:
        front_all = jnp.concatenate(front_pieces, axis=0)
        back_all = jnp.concatenate(back_pieces, axis=0)
        w_query_t = front_all[:, :q_cols].T
        w_key_t = front_all[:, q_cols:].T
        w_value_t = back_all[:, :k_cols].T
        w_out = back_all[:, k_cols:].T
    tok_rows = guard_rows.shape[0]
    half_width = generator_rows.shape[1]
    local_heads = q_cols // HD
    local_kv = k_cols // HD
    group_size = local_heads // local_kv
    length = lax.dynamic_index_in_dim(lengths, seq_rank, 0, keepdims=False)
    target = lax.dynamic_index_in_dim(label_index, seq_rank, 0, keepdims=False)
    offsets = jnp.arange(tok_rows, dtype=jnp.int32)
    cos_table, sin_table = rope_tables(offsets, HD)
    inputs = guard_rows.astype(jnp.float32)
    scale_in = lax.rsqrt(jnp.mean(inputs * inputs, axis=-1, keepdims=True) + EPSILON)
    normed = (inputs * scale_in * pre_gain).astype(jnp.bfloat16)
    if piecewise:
        block_rows = front_pieces[0].shape[0]
        front_proj = None
        back_proj = None
        for index, (front_piece, back_piece) in enumerate(zip(front_pieces, back_pieces)):
            normed_block = normed[:, index * block_rows:(index + 1) * block_rows]
            front_term = jnp.dot(normed_block, front_piece, preferred_element_type=jnp.float32)
            back_term = jnp.dot(normed_block, back_piece[:, :k_cols], preferred_element_type=jnp.float32)
            front_proj = front_term if front_proj is None else front_proj + front_term
            back_proj = back_term if back_proj is None else back_proj + back_term
    else:
        front_proj = jnp.dot(normed, front_all, preferred_element_type=jnp.float32)
        back_proj = jnp.dot(normed, back_all[:, :k_cols], preferred_element_type=jnp.float32)
    query_proj = front_proj[:, :q_cols].reshape(tok_rows, local_heads, HD).transpose(1, 0, 2)
    queries = (rotate(query_proj, cos_table, sin_table) * QUERY_SCALE).astype(jnp.bfloat16)
    key_proj = front_proj[:, q_cols:].reshape(tok_rows, local_kv, HD).transpose(1, 0, 2)
    keys_own = rotate(key_proj, cos_table, sin_table).astype(jnp.bfloat16)
    values_own = (
        back_proj
        .astype(jnp.bfloat16)
        .reshape(tok_rows, local_kv, HD)
        .transpose(1, 0, 2)
    )
    allowed = (offsets[None, :] <= offsets[:, None]) & (offsets[None, :] < length)
    query_four = queries.reshape(local_kv, group_size, tok_rows, HD)
    raw_scores = jnp.einsum(
        "kgid,kjd->kgij", query_four, keys_own, preferred_element_type=jnp.float32
    )
    capped = jnp.tanh(raw_scores / ATTEND_CAP)
    weight_exp = jnp.where(allowed[None, None], jnp.exp(ATTEND_CAP * capped), 0.0)
    soft_weights = weight_exp / jnp.sum(weight_exp, axis=-1, keepdims=True)
    attend = soft_weights.astype(jnp.bfloat16)
    context = jnp.einsum(
        "kgij,kjd->kgid", attend, values_own, preferred_element_type=jnp.float32
    ).astype(jnp.bfloat16)
    context_rows = (
        context.reshape(local_heads, tok_rows, HD)
        .transpose(1, 0, 2)
        .reshape(tok_rows, local_heads * HD)
    )
    out_part = jnp.dot(context_rows, w_out, preferred_element_type=jnp.float32)
    attention = pair_sum(out_part.astype(jnp.bfloat16))
    scale_attn = lax.rsqrt(jnp.mean(attention * attention, axis=-1, keepdims=True) + EPSILON)
    mixed_rows = inputs + attention * scale_attn * post_gain
    scale_out = lax.rsqrt(jnp.mean(mixed_rows * mixed_rows, axis=-1, keepdims=True) + EPSILON)
    final_rows = (mixed_rows * scale_out * final_gain).astype(jnp.bfloat16)
    logits = times_transposed(final_rows, label_table)
    label_cap = jnp.tanh(logits / LABEL_CAP)
    label_exp = jnp.exp(LABEL_CAP * label_cap)
    chance = label_exp / jnp.sum(label_exp, axis=-1, keepdims=True)
    live_rows = (offsets < length)[:, None]
    onehot = (jnp.arange(LABELS, dtype=jnp.int32) == target).astype(jnp.float32)[None, :]
    grad_logit = (
        jnp.where(live_rows, chance - onehot, 0.0) * (1.0 - label_cap * label_cap)
    ).astype(jnp.bfloat16)
    grad_final = jnp.dot(grad_logit, label_table, preferred_element_type=jnp.float32)
    scaled_final = grad_final * final_gain
    cube_out = scale_out * scale_out * scale_out
    grad_mixed = scale_out * scaled_final - mixed_rows * cube_out * jnp.mean(
        scaled_final * mixed_rows, axis=-1, keepdims=True
    )
    scaled_post = grad_mixed * post_gain
    cube_attn = scale_attn * scale_attn * scale_attn
    grad_attention = scale_attn * scaled_post - attention * cube_attn * jnp.mean(
        scaled_post * attention, axis=-1, keepdims=True
    )
    grad_context = times_transposed(grad_attention.astype(jnp.bfloat16), w_out).astype(jnp.bfloat16)
    grad_four = grad_context.reshape(tok_rows, local_kv, group_size, HD).transpose(1, 2, 0, 3)
    grad_prob = jnp.einsum(
        "kgid,kjd->kgij", grad_four, values_own, preferred_element_type=jnp.float32
    )
    grad_score = (
        soft_weights
        * (grad_prob - jnp.sum(soft_weights * grad_prob, axis=-1, keepdims=True))
        * (1.0 - capped * capped)
    )
    score_round = grad_score.astype(jnp.bfloat16)
    grad_query = jnp.einsum(
        "kgij,kjd->kgid", score_round, keys_own, preferred_element_type=jnp.float32
    ).reshape(local_heads, tok_rows, HD)
    grad_queries = rotate_back(grad_query * QUERY_SCALE, cos_table, sin_table).astype(jnp.bfloat16)
    grad_key = jnp.einsum(
        "kgij,kgid->kjd", score_round, query_four, preferred_element_type=jnp.float32
    )
    grad_value = jnp.einsum("kgij,kgid->kjd", attend, grad_four, preferred_element_type=jnp.float32)
    grad_keys = rotate_back(grad_key, cos_table, sin_table).astype(jnp.bfloat16)
    grad_values = grad_value.astype(jnp.bfloat16)
    query_rows = grad_queries.transpose(1, 0, 2).reshape(tok_rows, local_heads * HD)
    key_rows = grad_keys.transpose(1, 0, 2).reshape(tok_rows, local_kv * HD)
    value_rows = grad_values.transpose(1, 0, 2).reshape(tok_rows, local_kv * HD)
    grad_part = (
        jnp.dot(query_rows, w_query_t, preferred_element_type=jnp.float32)
        + jnp.dot(key_rows, w_key_t, preferred_element_type=jnp.float32)
        + jnp.dot(value_rows, w_value_t, preferred_element_type=jnp.float32)
    )
    cube_in = scale_in * scale_in * scale_in
    grad_normed = pair_sum(grad_part.astype(jnp.bfloat16))
    scaled_in = grad_normed * pre_gain
    row_stat = jnp.mean(scaled_in * inputs, axis=-1, keepdims=True)
    grad_full = scale_in * scaled_in - inputs * cube_in * row_stat + grad_mixed
    block_width = grad_full.shape[1] // n_seq
    half_blocks = half_width // block_width
    own_blocks = core_rank * half_blocks + jnp.arange(half_blocks, dtype=jnp.int32)
    grad_blocks = grad_full.astype(jnp.bfloat16).reshape(tok_rows, n_seq, block_width)
    grad_rows = jnp.take(grad_blocks, slot_of[own_blocks], axis=1).reshape(tok_rows, half_width)
    return lax.all_to_all(grad_rows, "seq", split_axis=0, concat_axis=0, tiled=True)


def solution(mesh):
    return jax.shard_map(
        functools.partial(shards, mesh.shape["seq"]),
        mesh=mesh,
        in_specs=(
            P(("groups", "seq"), "wg"),
            P(),
            P("seq", "wg"),
            P("seq", "wg"),
            P("seq", "wg"),
            P("wg", "seq"),
            P(),
            P(),
            P(),
            P("groups"),
            P("groups"),
        ),
        out_specs=P(("groups", "seq"), "wg"),
        check_vma=False,
    )
```

```python
import functools

import jax
import jax.numpy as jnp
from jax import lax
from jax.sharding import PartitionSpec as P

HD = 128
LABELS = 64


PIECEWISE_RING = 16
EPSILON = 1e-06
ATTEND_CAP = 50.0
LABEL_CAP = 30.0
QUERY_SCALE = 1.0 / 12.0


def rope_tables(positions, head_width):
    frequency = 10000.0 ** (-2.0 * jnp.arange(head_width // 2, dtype=jnp.float32) / head_width)
    angles = positions.astype(jnp.float32)[:, None] * frequency[None, :]
    return (jnp.cos(angles), jnp.sin(angles))


def rotate(values, cos_table, sin_table):
    half_width = values.shape[-1] // 2
    lower_part = values[..., :half_width]
    upper_part = values[..., half_width:]
    return jnp.concatenate(
        [
            lower_part * cos_table - upper_part * sin_table,
            upper_part * cos_table + lower_part * sin_table,
        ],
        axis=-1,
    )


def rotate_back(values, cos_table, sin_table):
    half_width = values.shape[-1] // 2
    lower_part = values[..., :half_width]
    upper_part = values[..., half_width:]
    return jnp.concatenate(
        [
            lower_part * cos_table + upper_part * sin_table,
            upper_part * cos_table - lower_part * sin_table,
        ],
        axis=-1,
    )


def times_transposed(left_side, right_side):
    return lax.dot_general(
        left_side, right_side, (((1,), (1,)), ((), ())), preferred_element_type=jnp.float32
    )


def pair_sum(rounded_part):
    other = lax.ppermute(rounded_part, "wg", perm=[(0, 1), (1, 0)])
    return rounded_part.astype(jnp.float32) + other.astype(jnp.float32)


def ring_order(n):
    if n % 2:
        return list(range(n))
    return list(range(0, n, 2)) + list(range(n - 1, 0, -2))


def ring_member(place, n):
    if n % 2:
        return place
    return jnp.where(place < n // 2, 2 * place, 2 * (n - 1 - place) + 1)


def ring_position(member, n):
    if n % 2:
        return member
    return jnp.where(member % 2 == 0, member // 2, n - 1 - member // 2)


def ring_gather(front, back, seq_rank, group_rank, n):
    order = ring_order(n)
    position = [0] * n
    for place, member in enumerate(order):
        position[member] = place
    forward_pairs = [(order[p], order[(p + 1) % n]) for p in range(n)]
    backward_pairs = [(order[p], order[(p - 1) % n]) for p in range(n)]
    group_pairs = [(0, 1), (1, 0)]
    place = ring_position(seq_rank, n)
    steps = jnp.arange(n, dtype=jnp.int32)
    block_of = ring_member((place - steps) % n, n)
    slot_of = (place - ring_position(steps, n)) % n
    first_group = group_rank == 0

    def thirds(values):
        width = values.shape[1] // 3
        return [values[:, i * width:(i + 1) * width] for i in range(3)]

    def carried(values):
        left, middle, right = thirds(values)
        return jnp.stack([jnp.where(first_group, left, right), middle])

    front_ring = [carried(front)]
    back_ring = [carried(back)]
    for step in range(1, n):
        front_ring.append(lax.ppermute(front_ring[-1], "seq", forward_pairs))
        back_ring.append(lax.ppermute(back_ring[-1], "seq", backward_pairs))
    front_pieces = [front]
    back_pieces = [back]
    for step in range(1, n):
        handed = lax.ppermute(
            jnp.stack([front_ring[step][0], back_ring[step][0]]), "groups", group_pairs
        )
        for ring, pieces, other in ((front_ring, front_pieces, handed[0]), (back_ring, back_pieces, handed[1])):
            own, middle = ring[step][0], ring[step][1]
            pieces.append(
                jnp.concatenate(
                    [jnp.where(first_group, own, other), middle, jnp.where(first_group, other, own)],
                    axis=1,
                )
            )
    if n <= PIECEWISE_RING:
        for step in range(n - 2):
            front_pieces[step], back_pieces[step], _, _ = lax.optimization_barrier(
                (front_pieces[step], back_pieces[step], front_ring[step + 1], back_ring[step + 1])
            )
    back_pieces = [back_pieces[(n - k) % n] for k in range(n)]
    return front_pieces, back_pieces, block_of, slot_of, (front_ring[1], back_ring[1])


def permute_blocks(values, block_order, n):
    lead = values.shape[:-1]
    width = values.shape[-1] // n
    blocks = values.reshape(lead + (n, width))
    return jnp.take(blocks, block_order, axis=-2).reshape(values.shape)


def shards(
    n_seq,
    generator_rows,
    pre_gain,
    query_weight,
    key_weight,
    value_weight,
    out_weight,
    post_gain,
    final_gain,
    label_table,
    lengths,
    label_index,
):
    seq_rank = lax.axis_index("seq")
    core_rank = lax.axis_index("wg")
    guard_half = lax.all_to_all(generator_rows, "seq", split_axis=0, concat_axis=0, tiled=True)
    q_cols = query_weight.shape[1]
    k_cols = key_weight.shape[1]
    front = jnp.concatenate([query_weight, key_weight], axis=1)
    back = jnp.concatenate([value_weight, out_weight.T], axis=1)
    front_pieces, back_pieces, block_of, slot_of, first_arrival = ring_gather(
        front, back, seq_rank, lax.axis_index("groups"), n_seq
    )
    guard_half, _ = lax.optimization_barrier((guard_half, first_arrival))
    guard_rows = lax.all_gather(guard_half, "wg", axis=1, tiled=True)
    guard_rows = permute_blocks(guard_rows, block_of, n_seq)
    pre_gain, post_gain, final_gain = permute_blocks(
        jnp.stack([pre_gain, post_gain, final_gain]), block_of, n_seq
    )
    label_table = permute_blocks(label_table, block_of, n_seq)
    piecewise = n_seq <= PIECEWISE_RING
    if piecewise:
        w_query_t = jnp.concatenate([piece[:, :q_cols].T for piece in front_pieces], axis=1)
        w_key_t = jnp.concatenate([piece[:, q_cols:].T for piece in front_pieces], axis=1)
        w_value_t = jnp.concatenate([piece[:, :k_cols].T for piece in back_pieces], axis=1)
        w_out = jnp.concatenate([piece[:, k_cols:].T for piece in back_pieces], axis=1)
    else:
        front_all = jnp.concatenate(front_pieces, axis=0)
        back_all = jnp.concatenate(back_pieces, axis=0)
        w_query_t = front_all[:, :q_cols].T
        w_key_t = front_all[:, q_cols:].T
        w_value_t = back_all[:, :k_cols].T
        w_out = back_all[:, k_cols:].T
    tok_rows = guard_rows.shape[0]
    half_width = generator_rows.shape[1]
    local_heads = q_cols // HD
    local_kv = k_cols // HD
    group_size = local_heads // local_kv
    length = lax.dynamic_index_in_dim(lengths, seq_rank, 0, keepdims=False)
    target = lax.dynamic_index_in_dim(label_index, seq_rank, 0, keepdims=False)
    offsets = jnp.arange(tok_rows, dtype=jnp.int32)
    cos_table, sin_table = rope_tables(offsets, HD)
    inputs = guard_rows.astype(jnp.float32)
    scale_in = lax.rsqrt(jnp.mean(inputs * inputs, axis=-1, keepdims=True) + EPSILON)
    normed = (inputs * scale_in * pre_gain).astype(jnp.bfloat16)
    if piecewise:
        block_rows = front_pieces[0].shape[0]
        front_proj = None
        back_proj = None
        for index, (front_piece, back_piece) in enumerate(zip(front_pieces, back_pieces)):
            normed_block = normed[:, index * block_rows:(index + 1) * block_rows]
            front_term = jnp.dot(normed_block, front_piece, preferred_element_type=jnp.float32)
            back_term = jnp.dot(normed_block, back_piece[:, :k_cols], preferred_element_type=jnp.float32)
            front_proj = front_term if front_proj is None else front_proj + front_term
            back_proj = back_term if back_proj is None else back_proj + back_term
    else:
        front_proj = jnp.dot(normed, front_all, preferred_element_type=jnp.float32)
        back_proj = jnp.dot(normed, back_all[:, :k_cols], preferred_element_type=jnp.float32)
    query_proj = front_proj[:, :q_cols].reshape(tok_rows, local_heads, HD).transpose(1, 0, 2)
    queries = (rotate(query_proj, cos_table, sin_table) * QUERY_SCALE).astype(jnp.bfloat16)
    key_proj = front_proj[:, q_cols:].reshape(tok_rows, local_kv, HD).transpose(1, 0, 2)
    keys_own = rotate(key_proj, cos_table, sin_table).astype(jnp.bfloat16)
    values_own = (
        back_proj
        .astype(jnp.bfloat16)
        .reshape(tok_rows, local_kv, HD)
        .transpose(1, 0, 2)
    )
    allowed = (offsets[None, :] <= offsets[:, None]) & (offsets[None, :] < length)
    query_four = queries.reshape(local_kv, group_size, tok_rows, HD)
    raw_scores = jnp.einsum(
        "kgid,kjd->kgij", query_four, keys_own, preferred_element_type=jnp.float32
    )
    capped = jnp.tanh(raw_scores / ATTEND_CAP)
    weight_exp = jnp.where(allowed[None, None], jnp.exp(ATTEND_CAP * capped), 0.0)
    soft_weights = weight_exp / jnp.sum(weight_exp, axis=-1, keepdims=True)
    attend = soft_weights.astype(jnp.bfloat16)
    context = jnp.einsum(
        "kgij,kjd->kgid", attend, values_own, preferred_element_type=jnp.float32
    ).astype(jnp.bfloat16)
    context_rows = (
        context.reshape(local_heads, tok_rows, HD)
        .transpose(1, 0, 2)
        .reshape(tok_rows, local_heads * HD)
    )
    out_part = jnp.dot(context_rows, w_out, preferred_element_type=jnp.float32)
    attention = pair_sum(out_part.astype(jnp.bfloat16))
    scale_attn = lax.rsqrt(jnp.mean(attention * attention, axis=-1, keepdims=True) + EPSILON)
    mixed_rows = inputs + attention * scale_attn * post_gain
    scale_out = lax.rsqrt(jnp.mean(mixed_rows * mixed_rows, axis=-1, keepdims=True) + EPSILON)
    final_rows = (mixed_rows * scale_out * final_gain).astype(jnp.bfloat16)
    logits = times_transposed(final_rows, label_table)
    label_cap = jnp.tanh(logits / LABEL_CAP)
    label_exp = jnp.exp(LABEL_CAP * label_cap)
    chance = label_exp / jnp.sum(label_exp, axis=-1, keepdims=True)
    live_rows = (offsets < length)[:, None]
    onehot = (jnp.arange(LABELS, dtype=jnp.int32) == target).astype(jnp.float32)[None, :]
    grad_logit = (
        jnp.where(live_rows, chance - onehot, 0.0) * (1.0 - label_cap * label_cap)
    ).astype(jnp.bfloat16)
    grad_final = jnp.dot(grad_logit, label_table, preferred_element_type=jnp.float32)
    scaled_final = grad_final * final_gain
    cube_out = scale_out * scale_out * scale_out
    grad_mixed = scale_out * scaled_final - mixed_rows * cube_out * jnp.mean(
        scaled_final * mixed_rows, axis=-1, keepdims=True
    )
    scaled_post = grad_mixed * post_gain
    cube_attn = scale_attn * scale_attn * scale_attn
    grad_attention = scale_attn * scaled_post - attention * cube_attn * jnp.mean(
        scaled_post * attention, axis=-1, keepdims=True
    )
    grad_context = times_transposed(grad_attention.astype(jnp.bfloat16), w_out).astype(jnp.bfloat16)
    grad_four = grad_context.reshape(tok_rows, local_kv, group_size, HD).transpose(1, 2, 0, 3)
    grad_prob = jnp.einsum(
        "kgid,kjd->kgij", grad_four, values_own, preferred_element_type=jnp.float32
    )
    grad_score = (
        soft_weights
        * (grad_prob - jnp.sum(soft_weights * grad_prob, axis=-1, keepdims=True))
        * (1.0 - capped * capped)
    )
    score_round = grad_score.astype(jnp.bfloat16)
    grad_query = jnp.einsum(
        "kgij,kjd->kgid", score_round, keys_own, preferred_element_type=jnp.float32
    ).reshape(local_heads, tok_rows, HD)
    grad_queries = rotate_back(grad_query * QUERY_SCALE, cos_table, sin_table).astype(jnp.bfloat16)
    grad_key = jnp.einsum(
        "kgij,kgid->kjd", score_round, query_four, preferred_element_type=jnp.float32
    )
    grad_value = jnp.einsum("kgij,kgid->kjd", attend, grad_four, preferred_element_type=jnp.float32)
    grad_keys = rotate_back(grad_key, cos_table, sin_table).astype(jnp.bfloat16)
    grad_values = grad_value.astype(jnp.bfloat16)
    query_rows = grad_queries.transpose(1, 0, 2).reshape(tok_rows, local_heads * HD)
    key_rows = grad_keys.transpose(1, 0, 2).reshape(tok_rows, local_kv * HD)
    value_rows = grad_values.transpose(1, 0, 2).reshape(tok_rows, local_kv * HD)
    grad_part = (
        jnp.dot(query_rows, w_query_t, preferred_element_type=jnp.float32)
        + jnp.dot(key_rows, w_key_t, preferred_element_type=jnp.float32)
        + jnp.dot(value_rows, w_value_t, preferred_element_type=jnp.float32)
    )
    cube_in = scale_in * scale_in * scale_in
    grad_normed = pair_sum(grad_part.astype(jnp.bfloat16))
    scaled_in = grad_normed * pre_gain
    row_stat = jnp.mean(scaled_in * inputs, axis=-1, keepdims=True)
    grad_full = scale_in * scaled_in - inputs * cube_in * row_stat + grad_mixed
    block_width = grad_full.shape[1] // n_seq
    half_blocks = half_width // block_width
    own_blocks = core_rank * half_blocks + jnp.arange(half_blocks, dtype=jnp.int32)
    grad_blocks = grad_full.astype(jnp.bfloat16).reshape(tok_rows, n_seq, block_width)
    grad_rows = jnp.take(grad_blocks, slot_of[own_blocks], axis=1).reshape(tok_rows, half_width)
    return lax.all_to_all(grad_rows, "seq", split_axis=0, concat_axis=0, tiled=True)


def solution(mesh):
    return jax.shard_map(
        functools.partial(shards, mesh.shape["seq"]),
        mesh=mesh,
        in_specs=(
            P(("groups", "seq"), "wg"),
            P(),
            P("seq", "wg"),
            P("seq", "wg"),
            P("seq", "wg"),
            P("wg", "seq"),
            P(),
            P(),
            P(),
            P("groups"),
            P("groups"),
        ),
        out_specs=P(("groups", "seq"), "wg"),
        check_vma=False,
    )
```

```python
import functools

import jax
import jax.numpy as jnp
from jax import lax
from jax.sharding import PartitionSpec as P

HD = 128
LABELS = 64


PIECEWISE_RING = 16
EPSILON = 1e-06
ATTEND_CAP = 50.0
LABEL_CAP = 30.0
QUERY_SCALE = 1.0 / 12.0


def rope_tables(positions, head_width):
    frequency = 10000.0 ** (-2.0 * jnp.arange(head_width // 2, dtype=jnp.float32) / head_width)
    angles = positions.astype(jnp.float32)[:, None] * frequency[None, :]
    return (jnp.cos(angles), jnp.sin(angles))


def rotate(values, cos_table, sin_table):
    half_width = values.shape[-1] // 2
    lower_part = values[..., :half_width]
    upper_part = values[..., half_width:]
    return jnp.concatenate(
        [
            lower_part * cos_table - upper_part * sin_table,
            upper_part * cos_table + lower_part * sin_table,
        ],
        axis=-1,
    )


def rotate_back(values, cos_table, sin_table):
    half_width = values.shape[-1] // 2
    lower_part = values[..., :half_width]
    upper_part = values[..., half_width:]
    return jnp.concatenate(
        [
            lower_part * cos_table + upper_part * sin_table,
            upper_part * cos_table - lower_part * sin_table,
        ],
        axis=-1,
    )


def times_transposed(left_side, right_side):
    return lax.dot_general(
        left_side, right_side, (((1,), (1,)), ((), ())), preferred_element_type=jnp.float32
    )


def pair_sum(rounded_part):
    other = lax.ppermute(rounded_part, "wg", perm=[(0, 1), (1, 0)])
    return rounded_part.astype(jnp.float32) + other.astype(jnp.float32)


def ring_order(n):
    if n % 2:
        return list(range(n))
    return list(range(0, n, 2)) + list(range(n - 1, 0, -2))


def ring_member(place, n):
    if n % 2:
        return place
    return jnp.where(place < n // 2, 2 * place, 2 * (n - 1 - place) + 1)


def ring_position(member, n):
    if n % 2:
        return member
    return jnp.where(member % 2 == 0, member // 2, n - 1 - member // 2)


def ring_gather(front, back, seq_rank, group_rank, n):
    order = ring_order(n)
    position = [0] * n
    for place, member in enumerate(order):
        position[member] = place
    forward_pairs = [(order[p], order[(p + 1) % n]) for p in range(n)]
    backward_pairs = [(order[p], order[(p - 1) % n]) for p in range(n)]
    group_pairs = [(0, 1), (1, 0)]
    place = ring_position(seq_rank, n)
    steps = jnp.arange(n, dtype=jnp.int32)
    block_of = ring_member((place - steps) % n, n)
    slot_of = (place - ring_position(steps, n)) % n
    first_group = group_rank == 0

    def thirds(values):
        width = values.shape[1] // 3
        return [values[:, i * width:(i + 1) * width] for i in range(3)]

    def carried(values):
        left, middle, right = thirds(values)
        return jnp.stack([jnp.where(first_group, left, right), middle])

    front_ring = [carried(front)]
    back_ring = [carried(back)]
    for step in range(1, n):
        front_ring.append(lax.ppermute(front_ring[-1], "seq", forward_pairs))
        back_ring.append(lax.ppermute(back_ring[-1], "seq", backward_pairs))
    front_pieces = [front]
    back_pieces = [back]
    for step in range(1, n):
        handed = lax.ppermute(
            jnp.stack([front_ring[step][0], back_ring[step][0]]), "groups", group_pairs
        )
        for ring, pieces, other in ((front_ring, front_pieces, handed[0]), (back_ring, back_pieces, handed[1])):
            own, middle = ring[step][0], ring[step][1]
            pieces.append(
                jnp.concatenate(
                    [jnp.where(first_group, own, other), middle, jnp.where(first_group, other, own)],
                    axis=1,
                )
            )
    if n <= PIECEWISE_RING:
        for step in range(n - 1):
            front_pieces[step], _ = lax.optimization_barrier((front_pieces[step], front_ring[step + 1]))
            back_pieces[step], _ = lax.optimization_barrier((back_pieces[step], back_ring[step + 1]))
    back_pieces = [back_pieces[(n - k) % n] for k in range(n)]
    return front_pieces, back_pieces, block_of, slot_of, (front_ring[1], back_ring[1])


def permute_blocks(values, block_order, n):
    lead = values.shape[:-1]
    width = values.shape[-1] // n
    blocks = values.reshape(lead + (n, width))
    return jnp.take(blocks, block_order, axis=-2).reshape(values.shape)


def shards(
    n_seq,
    generator_rows,
    pre_gain,
    query_weight,
    key_weight,
    value_weight,
    out_weight,
    post_gain,
    final_gain,
    label_table,
    lengths,
    label_index,
):
    seq_rank = lax.axis_index("seq")
    core_rank = lax.axis_index("wg")
    guard_half = lax.all_to_all(generator_rows, "seq", split_axis=0, concat_axis=0, tiled=True)
    q_cols = query_weight.shape[1]
    k_cols = key_weight.shape[1]
    front = jnp.concatenate([query_weight, key_weight], axis=1)
    back = jnp.concatenate([value_weight, out_weight.T], axis=1)
    front_pieces, back_pieces, block_of, slot_of, first_arrival = ring_gather(
        front, back, seq_rank, lax.axis_index("groups"), n_seq
    )
    guard_half, _ = lax.optimization_barrier((guard_half, first_arrival))
    guard_rows = lax.all_gather(guard_half, "wg", axis=1, tiled=True)
    guard_rows = permute_blocks(guard_rows, block_of, n_seq)
    pre_gain, post_gain, final_gain = permute_blocks(
        jnp.stack([pre_gain, post_gain, final_gain]), block_of, n_seq
    )
    label_table = permute_blocks(label_table, block_of, n_seq)
    piecewise = n_seq <= PIECEWISE_RING
    if piecewise:
        w_query_t = jnp.concatenate([piece[:, :q_cols].T for piece in front_pieces], axis=1)
        w_key_t = jnp.concatenate([piece[:, q_cols:].T for piece in front_pieces], axis=1)
        w_value_t = jnp.concatenate([piece[:, :k_cols].T for piece in back_pieces], axis=1)
        w_out = jnp.concatenate([piece[:, k_cols:].T for piece in back_pieces], axis=1)
    else:
        front_all = jnp.concatenate(front_pieces, axis=0)
        back_all = jnp.concatenate(back_pieces, axis=0)
        w_query_t = front_all[:, :q_cols].T
        w_key_t = front_all[:, q_cols:].T
        w_value_t = back_all[:, :k_cols].T
        w_out = back_all[:, k_cols:].T
    tok_rows = guard_rows.shape[0]
    half_width = generator_rows.shape[1]
    local_heads = q_cols // HD
    local_kv = k_cols // HD
    group_size = local_heads // local_kv
    length = lax.dynamic_index_in_dim(lengths, seq_rank, 0, keepdims=False)
    target = lax.dynamic_index_in_dim(label_index, seq_rank, 0, keepdims=False)
    offsets = jnp.arange(tok_rows, dtype=jnp.int32)
    cos_table, sin_table = rope_tables(offsets, HD)
    inputs = guard_rows.astype(jnp.float32)
    scale_in = lax.rsqrt(jnp.mean(inputs * inputs, axis=-1, keepdims=True) + EPSILON)
    normed = (inputs * scale_in * pre_gain).astype(jnp.bfloat16)
    if piecewise:
        block_rows = front_pieces[0].shape[0]
        front_proj = None
        back_proj = None
        for index, (front_piece, back_piece) in enumerate(zip(front_pieces, back_pieces)):
            normed_block = normed[:, index * block_rows:(index + 1) * block_rows]
            front_term = jnp.dot(normed_block, front_piece, preferred_element_type=jnp.float32)
            back_term = jnp.dot(normed_block, back_piece[:, :k_cols], preferred_element_type=jnp.float32)
            front_proj = front_term if front_proj is None else front_proj + front_term
            back_proj = back_term if back_proj is None else back_proj + back_term
    else:
        front_proj = jnp.dot(normed, front_all, preferred_element_type=jnp.float32)
        back_proj = jnp.dot(normed, back_all[:, :k_cols], preferred_element_type=jnp.float32)
    query_proj = front_proj[:, :q_cols].reshape(tok_rows, local_heads, HD).transpose(1, 0, 2)
    queries = (rotate(query_proj, cos_table, sin_table) * QUERY_SCALE).astype(jnp.bfloat16)
    key_proj = front_proj[:, q_cols:].reshape(tok_rows, local_kv, HD).transpose(1, 0, 2)
    keys_own = rotate(key_proj, cos_table, sin_table).astype(jnp.bfloat16)
    values_own = (
        back_proj
        .astype(jnp.bfloat16)
        .reshape(tok_rows, local_kv, HD)
        .transpose(1, 0, 2)
    )
    allowed = (offsets[None, :] <= offsets[:, None]) & (offsets[None, :] < length)
    query_four = queries.reshape(local_kv, group_size, tok_rows, HD)
    raw_scores = jnp.einsum(
        "kgid,kjd->kgij", query_four, keys_own, preferred_element_type=jnp.float32
    )
    capped = jnp.tanh(raw_scores / ATTEND_CAP)
    weight_exp = jnp.where(allowed[None, None], jnp.exp(ATTEND_CAP * capped), 0.0)
    soft_weights = weight_exp / jnp.sum(weight_exp, axis=-1, keepdims=True)
    attend = soft_weights.astype(jnp.bfloat16)
    context = jnp.einsum(
        "kgij,kjd->kgid", attend, values_own, preferred_element_type=jnp.float32
    ).astype(jnp.bfloat16)
    context_rows = (
        context.reshape(local_heads, tok_rows, HD)
        .transpose(1, 0, 2)
        .reshape(tok_rows, local_heads * HD)
    )
    out_part = jnp.dot(context_rows, w_out, preferred_element_type=jnp.float32)
    attention = pair_sum(out_part.astype(jnp.bfloat16))
    scale_attn = lax.rsqrt(jnp.mean(attention * attention, axis=-1, keepdims=True) + EPSILON)
    mixed_rows = inputs + attention * scale_attn * post_gain
    scale_out = lax.rsqrt(jnp.mean(mixed_rows * mixed_rows, axis=-1, keepdims=True) + EPSILON)
    final_rows = (mixed_rows * scale_out * final_gain).astype(jnp.bfloat16)
    logits = times_transposed(final_rows, label_table)
    label_cap = jnp.tanh(logits / LABEL_CAP)
    label_exp = jnp.exp(LABEL_CAP * label_cap)
    chance = label_exp / jnp.sum(label_exp, axis=-1, keepdims=True)
    live_rows = (offsets < length)[:, None]
    onehot = (jnp.arange(LABELS, dtype=jnp.int32) == target).astype(jnp.float32)[None, :]
    grad_logit = (
        jnp.where(live_rows, chance - onehot, 0.0) * (1.0 - label_cap * label_cap)
    ).astype(jnp.bfloat16)
    grad_final = jnp.dot(grad_logit, label_table, preferred_element_type=jnp.float32)
    scaled_final = grad_final * final_gain
    cube_out = scale_out * scale_out * scale_out
    grad_mixed = scale_out * scaled_final - mixed_rows * cube_out * jnp.mean(
        scaled_final * mixed_rows, axis=-1, keepdims=True
    )
    scaled_post = grad_mixed * post_gain
    cube_attn = scale_attn * scale_attn * scale_attn
    grad_attention = scale_attn * scaled_post - attention * cube_attn * jnp.mean(
        scaled_post * attention, axis=-1, keepdims=True
    )
    grad_context = times_transposed(grad_attention.astype(jnp.bfloat16), w_out).astype(jnp.bfloat16)
    grad_four = grad_context.reshape(tok_rows, local_kv, group_size, HD).transpose(1, 2, 0, 3)
    grad_prob = jnp.einsum(
        "kgid,kjd->kgij", grad_four, values_own, preferred_element_type=jnp.float32
    )
    grad_score = (
        soft_weights
        * (grad_prob - jnp.sum(soft_weights * grad_prob, axis=-1, keepdims=True))
        * (1.0 - capped * capped)
    )
    score_round = grad_score.astype(jnp.bfloat16)
    grad_query = jnp.einsum(
        "kgij,kjd->kgid", score_round, keys_own, preferred_element_type=jnp.float32
    ).reshape(local_heads, tok_rows, HD)
    grad_queries = rotate_back(grad_query * QUERY_SCALE, cos_table, sin_table).astype(jnp.bfloat16)
    grad_key = jnp.einsum(
        "kgij,kgid->kjd", score_round, query_four, preferred_element_type=jnp.float32
    )
    grad_value = jnp.einsum("kgij,kgid->kjd", attend, grad_four, preferred_element_type=jnp.float32)
    grad_keys = rotate_back(grad_key, cos_table, sin_table).astype(jnp.bfloat16)
    grad_values = grad_value.astype(jnp.bfloat16)
    query_rows = grad_queries.transpose(1, 0, 2).reshape(tok_rows, local_heads * HD)
    key_rows = grad_keys.transpose(1, 0, 2).reshape(tok_rows, local_kv * HD)
    value_rows = grad_values.transpose(1, 0, 2).reshape(tok_rows, local_kv * HD)
    grad_part = (
        jnp.dot(query_rows, w_query_t, preferred_element_type=jnp.float32)
        + jnp.dot(key_rows, w_key_t, preferred_element_type=jnp.float32)
        + jnp.dot(value_rows, w_value_t, preferred_element_type=jnp.float32)
    )
    cube_in = scale_in * scale_in * scale_in
    grad_normed = pair_sum(grad_part.astype(jnp.bfloat16))
    scaled_in = grad_normed * pre_gain
    row_stat = jnp.mean(scaled_in * inputs, axis=-1, keepdims=True)
    grad_full = scale_in * scaled_in - inputs * cube_in * row_stat + grad_mixed
    block_width = grad_full.shape[1] // n_seq
    half_blocks = half_width // block_width
    own_blocks = core_rank * half_blocks + jnp.arange(half_blocks, dtype=jnp.int32)
    grad_blocks = grad_full.astype(jnp.bfloat16).reshape(tok_rows, n_seq, block_width)
    grad_rows = jnp.take(grad_blocks, slot_of[own_blocks], axis=1).reshape(tok_rows, half_width)
    return lax.all_to_all(grad_rows, "seq", split_axis=0, concat_axis=0, tiled=True)


def solution(mesh):
    return jax.shard_map(
        functools.partial(shards, mesh.shape["seq"]),
        mesh=mesh,
        in_specs=(
            P(("groups", "seq"), "wg"),
            P(),
            P("seq", "wg"),
            P("seq", "wg"),
            P("seq", "wg"),
            P("wg", "seq"),
            P(),
            P(),
            P(),
            P("groups"),
            P("groups"),
        ),
        out_specs=P(("groups", "seq"), "wg"),
        check_vma=False,
    )
```

```python
import functools

import jax
import jax.numpy as jnp
from jax import lax
from jax.sharding import PartitionSpec as P

HD = 128
LABELS = 64


PIECEWISE_RING = 16
EPSILON = 1e-06
ATTEND_CAP = 50.0
LABEL_CAP = 30.0
QUERY_SCALE = 1.0 / 12.0


def rope_tables(positions, head_width):
    frequency = 10000.0 ** (-2.0 * jnp.arange(head_width // 2, dtype=jnp.float32) / head_width)
    angles = positions.astype(jnp.float32)[:, None] * frequency[None, :]
    return (jnp.cos(angles), jnp.sin(angles))


def rotate(values, cos_table, sin_table):
    half_width = values.shape[-1] // 2
    lower_part = values[..., :half_width]
    upper_part = values[..., half_width:]
    return jnp.concatenate(
        [
            lower_part * cos_table - upper_part * sin_table,
            upper_part * cos_table + lower_part * sin_table,
        ],
        axis=-1,
    )


def rotate_back(values, cos_table, sin_table):
    half_width = values.shape[-1] // 2
    lower_part = values[..., :half_width]
    upper_part = values[..., half_width:]
    return jnp.concatenate(
        [
            lower_part * cos_table + upper_part * sin_table,
            upper_part * cos_table - lower_part * sin_table,
        ],
        axis=-1,
    )


def times_transposed(left_side, right_side):
    return lax.dot_general(
        left_side, right_side, (((1,), (1,)), ((), ())), preferred_element_type=jnp.float32
    )


def pair_sum(rounded_part):
    other = lax.ppermute(rounded_part, "wg", perm=[(0, 1), (1, 0)])
    return rounded_part.astype(jnp.float32) + other.astype(jnp.float32)


def ring_order(n):
    if n % 2:
        return list(range(n))
    return list(range(0, n, 2)) + list(range(n - 1, 0, -2))


def ring_member(place, n):
    if n % 2:
        return place
    return jnp.where(place < n // 2, 2 * place, 2 * (n - 1 - place) + 1)


def ring_position(member, n):
    if n % 2:
        return member
    return jnp.where(member % 2 == 0, member // 2, n - 1 - member // 2)


def ring_gather(front, back, seq_rank, group_rank, n):
    order = ring_order(n)
    position = [0] * n
    for place, member in enumerate(order):
        position[member] = place
    forward_pairs = [(order[p], order[(p + 1) % n]) for p in range(n)]
    backward_pairs = [(order[p], order[(p - 1) % n]) for p in range(n)]
    group_pairs = [(0, 1), (1, 0)]
    place = ring_position(seq_rank, n)
    steps = jnp.arange(n, dtype=jnp.int32)
    block_of = ring_member((place - steps) % n, n)
    slot_of = (place - ring_position(steps, n)) % n
    first_group = group_rank == 0

    def thirds(values):
        width = values.shape[1] // 3
        return [values[:, i * width:(i + 1) * width] for i in range(3)]

    def carried(values):
        left, middle, right = thirds(values)
        return jnp.stack([jnp.where(first_group, left, right), middle])

    front_ring = [carried(front)]
    back_ring = [carried(back)]
    for step in range(1, n):
        front_ring.append(lax.ppermute(front_ring[-1], "seq", forward_pairs))
        back_ring.append(lax.ppermute(back_ring[-1], "seq", backward_pairs))
    front_pieces = [front]
    back_pieces = [back]
    for step in range(1, n):
        handed = lax.ppermute(
            jnp.stack([front_ring[step][0], back_ring[step][0]]), "groups", group_pairs
        )
        for ring, pieces, other in ((front_ring, front_pieces, handed[0]), (back_ring, back_pieces, handed[1])):
            own, middle = ring[step][0], ring[step][1]
            pieces.append(
                jnp.concatenate(
                    [jnp.where(first_group, own, other), middle, jnp.where(first_group, other, own)],
                    axis=1,
                )
            )
    if n <= PIECEWISE_RING:
        for step in range(n - 1):
            front_pieces[step], back_pieces[step], _, _ = lax.optimization_barrier(
                (front_pieces[step], back_pieces[step], front_ring[min(step + 2, n - 1) if step == 0 else step + 1],
                 back_ring[min(step + 2, n - 1) if step == 0 else step + 1])
            )
    back_pieces = [back_pieces[(n - k) % n] for k in range(n)]
    return front_pieces, back_pieces, block_of, slot_of, (front_ring[1], back_ring[1])


def permute_blocks(values, block_order, n):
    lead = values.shape[:-1]
    width = values.shape[-1] // n
    blocks = values.reshape(lead + (n, width))
    return jnp.take(blocks, block_order, axis=-2).reshape(values.shape)


def shards(
    n_seq,
    generator_rows,
    pre_gain,
    query_weight,
    key_weight,
    value_weight,
    out_weight,
    post_gain,
    final_gain,
    label_table,
    lengths,
    label_index,
):
    seq_rank = lax.axis_index("seq")
    core_rank = lax.axis_index("wg")
    guard_half = lax.all_to_all(generator_rows, "seq", split_axis=0, concat_axis=0, tiled=True)
    q_cols = query_weight.shape[1]
    k_cols = key_weight.shape[1]
    front = jnp.concatenate([query_weight, key_weight], axis=1)
    back = jnp.concatenate([value_weight, out_weight.T], axis=1)
    front_pieces, back_pieces, block_of, slot_of, first_arrival = ring_gather(
        front, back, seq_rank, lax.axis_index("groups"), n_seq
    )
    guard_half, _ = lax.optimization_barrier((guard_half, first_arrival))
    guard_rows = lax.all_gather(guard_half, "wg", axis=1, tiled=True)
    guard_rows = permute_blocks(guard_rows, block_of, n_seq)
    pre_gain, post_gain, final_gain = permute_blocks(
        jnp.stack([pre_gain, post_gain, final_gain]), block_of, n_seq
    )
    label_table = permute_blocks(label_table, block_of, n_seq)
    piecewise = n_seq <= PIECEWISE_RING
    if piecewise:
        w_query_t = jnp.concatenate([piece[:, :q_cols].T for piece in front_pieces], axis=1)
        w_key_t = jnp.concatenate([piece[:, q_cols:].T for piece in front_pieces], axis=1)
        w_value_t = jnp.concatenate([piece[:, :k_cols].T for piece in back_pieces], axis=1)
        w_out = jnp.concatenate([piece[:, k_cols:].T for piece in back_pieces], axis=1)
    else:
        front_all = jnp.concatenate(front_pieces, axis=0)
        back_all = jnp.concatenate(back_pieces, axis=0)
        w_query_t = front_all[:, :q_cols].T
        w_key_t = front_all[:, q_cols:].T
        w_value_t = back_all[:, :k_cols].T
        w_out = back_all[:, k_cols:].T
    tok_rows = guard_rows.shape[0]
    half_width = generator_rows.shape[1]
    local_heads = q_cols // HD
    local_kv = k_cols // HD
    group_size = local_heads // local_kv
    length = lax.dynamic_index_in_dim(lengths, seq_rank, 0, keepdims=False)
    target = lax.dynamic_index_in_dim(label_index, seq_rank, 0, keepdims=False)
    offsets = jnp.arange(tok_rows, dtype=jnp.int32)
    cos_table, sin_table = rope_tables(offsets, HD)
    inputs = guard_rows.astype(jnp.float32)
    scale_in = lax.rsqrt(jnp.mean(inputs * inputs, axis=-1, keepdims=True) + EPSILON)
    normed = (inputs * scale_in * pre_gain).astype(jnp.bfloat16)
    if piecewise:
        block_rows = front_pieces[0].shape[0]
        front_proj = None
        back_proj = None
        for index, (front_piece, back_piece) in enumerate(zip(front_pieces, back_pieces)):
            normed_block = normed[:, index * block_rows:(index + 1) * block_rows]
            front_term = jnp.dot(normed_block, front_piece, preferred_element_type=jnp.float32)
            back_term = jnp.dot(normed_block, back_piece[:, :k_cols], preferred_element_type=jnp.float32)
            front_proj = front_term if front_proj is None else front_proj + front_term
            back_proj = back_term if back_proj is None else back_proj + back_term
    else:
        front_proj = jnp.dot(normed, front_all, preferred_element_type=jnp.float32)
        back_proj = jnp.dot(normed, back_all[:, :k_cols], preferred_element_type=jnp.float32)
    query_proj = front_proj[:, :q_cols].reshape(tok_rows, local_heads, HD).transpose(1, 0, 2)
    queries = (rotate(query_proj, cos_table, sin_table) * QUERY_SCALE).astype(jnp.bfloat16)
    key_proj = front_proj[:, q_cols:].reshape(tok_rows, local_kv, HD).transpose(1, 0, 2)
    keys_own = rotate(key_proj, cos_table, sin_table).astype(jnp.bfloat16)
    values_own = (
        back_proj
        .astype(jnp.bfloat16)
        .reshape(tok_rows, local_kv, HD)
        .transpose(1, 0, 2)
    )
    allowed = (offsets[None, :] <= offsets[:, None]) & (offsets[None, :] < length)
    query_four = queries.reshape(local_kv, group_size, tok_rows, HD)
    raw_scores = jnp.einsum(
        "kgid,kjd->kgij", query_four, keys_own, preferred_element_type=jnp.float32
    )
    capped = jnp.tanh(raw_scores / ATTEND_CAP)
    weight_exp = jnp.where(allowed[None, None], jnp.exp(ATTEND_CAP * capped), 0.0)
    soft_weights = weight_exp / jnp.sum(weight_exp, axis=-1, keepdims=True)
    attend = soft_weights.astype(jnp.bfloat16)
    context = jnp.einsum(
        "kgij,kjd->kgid", attend, values_own, preferred_element_type=jnp.float32
    ).astype(jnp.bfloat16)
    context_rows = (
        context.reshape(local_heads, tok_rows, HD)
        .transpose(1, 0, 2)
        .reshape(tok_rows, local_heads * HD)
    )
    out_part = jnp.dot(context_rows, w_out, preferred_element_type=jnp.float32)
    attention = pair_sum(out_part.astype(jnp.bfloat16))
    scale_attn = lax.rsqrt(jnp.mean(attention * attention, axis=-1, keepdims=True) + EPSILON)
    mixed_rows = inputs + attention * scale_attn * post_gain
    scale_out = lax.rsqrt(jnp.mean(mixed_rows * mixed_rows, axis=-1, keepdims=True) + EPSILON)
    final_rows = (mixed_rows * scale_out * final_gain).astype(jnp.bfloat16)
    logits = times_transposed(final_rows, label_table)
    label_cap = jnp.tanh(logits / LABEL_CAP)
    label_exp = jnp.exp(LABEL_CAP * label_cap)
    chance = label_exp / jnp.sum(label_exp, axis=-1, keepdims=True)
    live_rows = (offsets < length)[:, None]
    onehot = (jnp.arange(LABELS, dtype=jnp.int32) == target).astype(jnp.float32)[None, :]
    grad_logit = (
        jnp.where(live_rows, chance - onehot, 0.0) * (1.0 - label_cap * label_cap)
    ).astype(jnp.bfloat16)
    grad_final = jnp.dot(grad_logit, label_table, preferred_element_type=jnp.float32)
    scaled_final = grad_final * final_gain
    cube_out = scale_out * scale_out * scale_out
    grad_mixed = scale_out * scaled_final - mixed_rows * cube_out * jnp.mean(
        scaled_final * mixed_rows, axis=-1, keepdims=True
    )
    scaled_post = grad_mixed * post_gain
    cube_attn = scale_attn * scale_attn * scale_attn
    grad_attention = scale_attn * scaled_post - attention * cube_attn * jnp.mean(
        scaled_post * attention, axis=-1, keepdims=True
    )
    grad_context = times_transposed(grad_attention.astype(jnp.bfloat16), w_out).astype(jnp.bfloat16)
    grad_four = grad_context.reshape(tok_rows, local_kv, group_size, HD).transpose(1, 2, 0, 3)
    grad_prob = jnp.einsum(
        "kgid,kjd->kgij", grad_four, values_own, preferred_element_type=jnp.float32
    )
    grad_score = (
        soft_weights
        * (grad_prob - jnp.sum(soft_weights * grad_prob, axis=-1, keepdims=True))
        * (1.0 - capped * capped)
    )
    score_round = grad_score.astype(jnp.bfloat16)
    grad_query = jnp.einsum(
        "kgij,kjd->kgid", score_round, keys_own, preferred_element_type=jnp.float32
    ).reshape(local_heads, tok_rows, HD)
    grad_queries = rotate_back(grad_query * QUERY_SCALE, cos_table, sin_table).astype(jnp.bfloat16)
    grad_key = jnp.einsum(
        "kgij,kgid->kjd", score_round, query_four, preferred_element_type=jnp.float32
    )
    grad_value = jnp.einsum("kgij,kgid->kjd", attend, grad_four, preferred_element_type=jnp.float32)
    grad_keys = rotate_back(grad_key, cos_table, sin_table).astype(jnp.bfloat16)
    grad_values = grad_value.astype(jnp.bfloat16)
    query_rows = grad_queries.transpose(1, 0, 2).reshape(tok_rows, local_heads * HD)
    key_rows = grad_keys.transpose(1, 0, 2).reshape(tok_rows, local_kv * HD)
    value_rows = grad_values.transpose(1, 0, 2).reshape(tok_rows, local_kv * HD)
    grad_part = (
        jnp.dot(query_rows, w_query_t, preferred_element_type=jnp.float32)
        + jnp.dot(key_rows, w_key_t, preferred_element_type=jnp.float32)
        + jnp.dot(value_rows, w_value_t, preferred_element_type=jnp.float32)
    )
    cube_in = scale_in * scale_in * scale_in
    grad_normed = pair_sum(grad_part.astype(jnp.bfloat16))
    scaled_in = grad_normed * pre_gain
    row_stat = jnp.mean(scaled_in * inputs, axis=-1, keepdims=True)
    grad_full = scale_in * scaled_in - inputs * cube_in * row_stat + grad_mixed
    block_width = grad_full.shape[1] // n_seq
    half_blocks = half_width // block_width
    own_blocks = core_rank * half_blocks + jnp.arange(half_blocks, dtype=jnp.int32)
    grad_blocks = grad_full.astype(jnp.bfloat16).reshape(tok_rows, n_seq, block_width)
    grad_rows = jnp.take(grad_blocks, slot_of[own_blocks], axis=1).reshape(tok_rows, half_width)
    return lax.all_to_all(grad_rows, "seq", split_axis=0, concat_axis=0, tiled=True)


def solution(mesh):
    return jax.shard_map(
        functools.partial(shards, mesh.shape["seq"]),
        mesh=mesh,
        in_specs=(
            P(("groups", "seq"), "wg"),
            P(),
            P("seq", "wg"),
            P("seq", "wg"),
            P("seq", "wg"),
            P("wg", "seq"),
            P(),
            P(),
            P(),
            P("groups"),
            P("groups"),
        ),
        out_specs=P(("groups", "seq"), "wg"),
        check_vma=False,
    )
```

```python
import functools

import jax
import jax.numpy as jnp
from jax import lax
from jax.sharding import PartitionSpec as P

HD = 128
LABELS = 64


PIECEWISE_RING = 16
EPSILON = 1e-06
ATTEND_CAP = 50.0
LABEL_CAP = 30.0
QUERY_SCALE = 1.0 / 12.0


def rope_tables(positions, head_width):
    frequency = 10000.0 ** (-2.0 * jnp.arange(head_width // 2, dtype=jnp.float32) / head_width)
    angles = positions.astype(jnp.float32)[:, None] * frequency[None, :]
    return (jnp.cos(angles), jnp.sin(angles))


def rotate(values, cos_table, sin_table):
    half_width = values.shape[-1] // 2
    lower_part = values[..., :half_width]
    upper_part = values[..., half_width:]
    return jnp.concatenate(
        [
            lower_part * cos_table - upper_part * sin_table,
            upper_part * cos_table + lower_part * sin_table,
        ],
        axis=-1,
    )


def rotate_back(values, cos_table, sin_table):
    half_width = values.shape[-1] // 2
    lower_part = values[..., :half_width]
    upper_part = values[..., half_width:]
    return jnp.concatenate(
        [
            lower_part * cos_table + upper_part * sin_table,
            upper_part * cos_table - lower_part * sin_table,
        ],
        axis=-1,
    )


def times_transposed(left_side, right_side):
    return lax.dot_general(
        left_side, right_side, (((1,), (1,)), ((), ())), preferred_element_type=jnp.float32
    )


def pair_sum(rounded_part):
    other = lax.ppermute(rounded_part, "wg", perm=[(0, 1), (1, 0)])
    return rounded_part.astype(jnp.float32) + other.astype(jnp.float32)


def ring_order(n):
    if n % 2:
        return list(range(n))
    return list(range(0, n, 2)) + list(range(n - 1, 0, -2))


def ring_member(place, n):
    if n % 2:
        return place
    return jnp.where(place < n // 2, 2 * place, 2 * (n - 1 - place) + 1)


def ring_position(member, n):
    if n % 2:
        return member
    return jnp.where(member % 2 == 0, member // 2, n - 1 - member // 2)


def ring_gather(front, back, seq_rank, group_rank, n):
    order = ring_order(n)
    position = [0] * n
    for place, member in enumerate(order):
        position[member] = place
    forward_pairs = [(order[p], order[(p + 1) % n]) for p in range(n)]
    backward_pairs = [(order[p], order[(p - 1) % n]) for p in range(n)]
    group_pairs = [(0, 1), (1, 0)]
    place = ring_position(seq_rank, n)
    steps = jnp.arange(n, dtype=jnp.int32)
    block_of = ring_member((place - steps) % n, n)
    slot_of = (place - ring_position(steps, n)) % n
    first_group = group_rank == 0

    def thirds(values):
        width = values.shape[1] // 3
        return [values[:, i * width:(i + 1) * width] for i in range(3)]

    def carried(values):
        left, middle, right = thirds(values)
        return jnp.stack([jnp.where(first_group, left, right), middle])

    front_ring = [carried(front)]
    back_ring = [carried(back)]
    for step in range(1, n):
        front_ring.append(lax.ppermute(front_ring[-1], "seq", forward_pairs))
        back_ring.append(lax.ppermute(back_ring[-1], "seq", backward_pairs))
    front_pieces = [front]
    back_pieces = [back]
    for step in range(1, n):
        handed = [lax.ppermute(ring[step][0], "groups", group_pairs) for ring in (front_ring, back_ring)]
        for ring, pieces, other in ((front_ring, front_pieces, handed[0]), (back_ring, back_pieces, handed[1])):
            own, middle = ring[step][0], ring[step][1]
            pieces.append(
                jnp.concatenate(
                    [jnp.where(first_group, own, other), middle, jnp.where(first_group, other, own)],
                    axis=1,
                )
            )
    if n <= PIECEWISE_RING:
        for step in range(n - 1):
            front_pieces[step], back_pieces[step], _, _ = lax.optimization_barrier(
                (front_pieces[step], back_pieces[step], front_ring[step + 1], back_ring[step + 1])
            )
    back_pieces = [back_pieces[(n - k) % n] for k in range(n)]
    return front_pieces, back_pieces, block_of, slot_of, (front_ring[1], back_ring[1])


def permute_blocks(values, block_order, n):
    lead = values.shape[:-1]
    width = values.shape[-1] // n
    blocks = values.reshape(lead + (n, width))
    return jnp.take(blocks, block_order, axis=-2).reshape(values.shape)


def shards(
    n_seq,
    generator_rows,
    pre_gain,
    query_weight,
    key_weight,
    value_weight,
    out_weight,
    post_gain,
    final_gain,
    label_table,
    lengths,
    label_index,
):
    seq_rank = lax.axis_index("seq")
    core_rank = lax.axis_index("wg")
    guard_half = lax.all_to_all(generator_rows, "seq", split_axis=0, concat_axis=0, tiled=True)
    q_cols = query_weight.shape[1]
    k_cols = key_weight.shape[1]
    front = jnp.concatenate([query_weight, key_weight], axis=1)
    back = jnp.concatenate([value_weight, out_weight.T], axis=1)
    front_pieces, back_pieces, block_of, slot_of, first_arrival = ring_gather(
        front, back, seq_rank, lax.axis_index("groups"), n_seq
    )
    guard_half, _ = lax.optimization_barrier((guard_half, first_arrival))
    guard_rows = lax.all_gather(guard_half, "wg", axis=1, tiled=True)
    guard_rows = permute_blocks(guard_rows, block_of, n_seq)
    pre_gain, post_gain, final_gain = permute_blocks(
        jnp.stack([pre_gain, post_gain, final_gain]), block_of, n_seq
    )
    label_table = permute_blocks(label_table, block_of, n_seq)
    piecewise = n_seq <= PIECEWISE_RING
    if piecewise:
        w_query_t = jnp.concatenate([piece[:, :q_cols].T for piece in front_pieces], axis=1)
        w_key_t = jnp.concatenate([piece[:, q_cols:].T for piece in front_pieces], axis=1)
        w_value_t = jnp.concatenate([piece[:, :k_cols].T for piece in back_pieces], axis=1)
        w_out = jnp.concatenate([piece[:, k_cols:].T for piece in back_pieces], axis=1)
    else:
        front_all = jnp.concatenate(front_pieces, axis=0)
        back_all = jnp.concatenate(back_pieces, axis=0)
        w_query_t = front_all[:, :q_cols].T
        w_key_t = front_all[:, q_cols:].T
        w_value_t = back_all[:, :k_cols].T
        w_out = back_all[:, k_cols:].T
    tok_rows = guard_rows.shape[0]
    half_width = generator_rows.shape[1]
    local_heads = q_cols // HD
    local_kv = k_cols // HD
    group_size = local_heads // local_kv
    length = lax.dynamic_index_in_dim(lengths, seq_rank, 0, keepdims=False)
    target = lax.dynamic_index_in_dim(label_index, seq_rank, 0, keepdims=False)
    offsets = jnp.arange(tok_rows, dtype=jnp.int32)
    cos_table, sin_table = rope_tables(offsets, HD)
    inputs = guard_rows.astype(jnp.float32)
    scale_in = lax.rsqrt(jnp.mean(inputs * inputs, axis=-1, keepdims=True) + EPSILON)
    normed = (inputs * scale_in * pre_gain).astype(jnp.bfloat16)
    if piecewise:
        block_rows = front_pieces[0].shape[0]
        front_proj = None
        back_proj = None
        for index, (front_piece, back_piece) in enumerate(zip(front_pieces, back_pieces)):
            normed_block = normed[:, index * block_rows:(index + 1) * block_rows]
            front_term = jnp.dot(normed_block, front_piece, preferred_element_type=jnp.float32)
            back_term = jnp.dot(normed_block, back_piece[:, :k_cols], preferred_element_type=jnp.float32)
            front_proj = front_term if front_proj is None else front_proj + front_term
            back_proj = back_term if back_proj is None else back_proj + back_term
    else:
        front_proj = jnp.dot(normed, front_all, preferred_element_type=jnp.float32)
        back_proj = jnp.dot(normed, back_all[:, :k_cols], preferred_element_type=jnp.float32)
    query_proj = front_proj[:, :q_cols].reshape(tok_rows, local_heads, HD).transpose(1, 0, 2)
    queries = (rotate(query_proj, cos_table, sin_table) * QUERY_SCALE).astype(jnp.bfloat16)
    key_proj = front_proj[:, q_cols:].reshape(tok_rows, local_kv, HD).transpose(1, 0, 2)
    keys_own = rotate(key_proj, cos_table, sin_table).astype(jnp.bfloat16)
    values_own = (
        back_proj
        .astype(jnp.bfloat16)
        .reshape(tok_rows, local_kv, HD)
        .transpose(1, 0, 2)
    )
    allowed = (offsets[None, :] <= offsets[:, None]) & (offsets[None, :] < length)
    query_four = queries.reshape(local_kv, group_size, tok_rows, HD)
    raw_scores = jnp.einsum(
        "kgid,kjd->kgij", query_four, keys_own, preferred_element_type=jnp.float32
    )
    capped = jnp.tanh(raw_scores / ATTEND_CAP)
    weight_exp = jnp.where(allowed[None, None], jnp.exp(ATTEND_CAP * capped), 0.0)
    soft_weights = weight_exp / jnp.sum(weight_exp, axis=-1, keepdims=True)
    attend = soft_weights.astype(jnp.bfloat16)
    context = jnp.einsum(
        "kgij,kjd->kgid", attend, values_own, preferred_element_type=jnp.float32
    ).astype(jnp.bfloat16)
    context_rows = (
        context.reshape(local_heads, tok_rows, HD)
        .transpose(1, 0, 2)
        .reshape(tok_rows, local_heads * HD)
    )
    out_part = jnp.dot(context_rows, w_out, preferred_element_type=jnp.float32)
    attention = pair_sum(out_part.astype(jnp.bfloat16))
    scale_attn = lax.rsqrt(jnp.mean(attention * attention, axis=-1, keepdims=True) + EPSILON)
    mixed_rows = inputs + attention * scale_attn * post_gain
    scale_out = lax.rsqrt(jnp.mean(mixed_rows * mixed_rows, axis=-1, keepdims=True) + EPSILON)
    final_rows = (mixed_rows * scale_out * final_gain).astype(jnp.bfloat16)
    logits = times_transposed(final_rows, label_table)
    label_cap = jnp.tanh(logits / LABEL_CAP)
    label_exp = jnp.exp(LABEL_CAP * label_cap)
    chance = label_exp / jnp.sum(label_exp, axis=-1, keepdims=True)
    live_rows = (offsets < length)[:, None]
    onehot = (jnp.arange(LABELS, dtype=jnp.int32) == target).astype(jnp.float32)[None, :]
    grad_logit = (
        jnp.where(live_rows, chance - onehot, 0.0) * (1.0 - label_cap * label_cap)
    ).astype(jnp.bfloat16)
    grad_final = jnp.dot(grad_logit, label_table, preferred_element_type=jnp.float32)
    scaled_final = grad_final * final_gain
    cube_out = scale_out * scale_out * scale_out
    grad_mixed = scale_out * scaled_final - mixed_rows * cube_out * jnp.mean(
        scaled_final * mixed_rows, axis=-1, keepdims=True
    )
    scaled_post = grad_mixed * post_gain
    cube_attn = scale_attn * scale_attn * scale_attn
    grad_attention = scale_attn * scaled_post - attention * cube_attn * jnp.mean(
        scaled_post * attention, axis=-1, keepdims=True
    )
    grad_context = times_transposed(grad_attention.astype(jnp.bfloat16), w_out).astype(jnp.bfloat16)
    grad_four = grad_context.reshape(tok_rows, local_kv, group_size, HD).transpose(1, 2, 0, 3)
    grad_prob = jnp.einsum(
        "kgid,kjd->kgij", grad_four, values_own, preferred_element_type=jnp.float32
    )
    grad_score = (
        soft_weights
        * (grad_prob - jnp.sum(soft_weights * grad_prob, axis=-1, keepdims=True))
        * (1.0 - capped * capped)
    )
    score_round = grad_score.astype(jnp.bfloat16)
    grad_query = jnp.einsum(
        "kgij,kjd->kgid", score_round, keys_own, preferred_element_type=jnp.float32
    ).reshape(local_heads, tok_rows, HD)
    grad_queries = rotate_back(grad_query * QUERY_SCALE, cos_table, sin_table).astype(jnp.bfloat16)
    grad_key = jnp.einsum(
        "kgij,kgid->kjd", score_round, query_four, preferred_element_type=jnp.float32
    )
    grad_value = jnp.einsum("kgij,kgid->kjd", attend, grad_four, preferred_element_type=jnp.float32)
    grad_keys = rotate_back(grad_key, cos_table, sin_table).astype(jnp.bfloat16)
    grad_values = grad_value.astype(jnp.bfloat16)
    query_rows = grad_queries.transpose(1, 0, 2).reshape(tok_rows, local_heads * HD)
    key_rows = grad_keys.transpose(1, 0, 2).reshape(tok_rows, local_kv * HD)
    value_rows = grad_values.transpose(1, 0, 2).reshape(tok_rows, local_kv * HD)
    grad_part = (
        jnp.dot(query_rows, w_query_t, preferred_element_type=jnp.float32)
        + jnp.dot(key_rows, w_key_t, preferred_element_type=jnp.float32)
        + jnp.dot(value_rows, w_value_t, preferred_element_type=jnp.float32)
    )
    cube_in = scale_in * scale_in * scale_in
    grad_normed = pair_sum(grad_part.astype(jnp.bfloat16))
    scaled_in = grad_normed * pre_gain
    row_stat = jnp.mean(scaled_in * inputs, axis=-1, keepdims=True)
    grad_full = scale_in * scaled_in - inputs * cube_in * row_stat + grad_mixed
    block_width = grad_full.shape[1] // n_seq
    half_blocks = half_width // block_width
    own_blocks = core_rank * half_blocks + jnp.arange(half_blocks, dtype=jnp.int32)
    grad_blocks = grad_full.astype(jnp.bfloat16).reshape(tok_rows, n_seq, block_width)
    grad_rows = jnp.take(grad_blocks, slot_of[own_blocks], axis=1).reshape(tok_rows, half_width)
    return lax.all_to_all(grad_rows, "seq", split_axis=0, concat_axis=0, tiled=True)


def solution(mesh):
    return jax.shard_map(
        functools.partial(shards, mesh.shape["seq"]),
        mesh=mesh,
        in_specs=(
            P(("groups", "seq"), "wg"),
            P(),
            P("seq", "wg"),
            P("seq", "wg"),
            P("seq", "wg"),
            P("wg", "seq"),
            P(),
            P(),
            P(),
            P("groups"),
            P("groups"),
        ),
        out_specs=P(("groups", "seq"), "wg"),
        check_vma=False,
    )
```
